32 devices in a mesh: dp: 8 (over y, x, core), tensor: 4 (over z).
Axes of the slice: x: 2, y: 2, z: 4, core: 2. Of those that a mesh axis runs over, the one named last changes fastest.
Arguments:
- tokens: bfloat16 [2, 8, 1216, 2048], P(None, 'dp', 'tensor'), may hold values from -6 to 6
- cotangent: bfloat16 [2, 8, 1216, 2048], P(None, 'dp', 'tensor'), may hold values from -6 to 6
- cont_lengths: int32 [2, 8, 3], P(None, 'dp'), may hold values from 1 to 128, 192 in all within a row
- query_weight: float32 [2048, 2048], P('dp', 'tensor'), may hold values from -0.5 to 0.5
- keyval_weight: float32 [2048, 8, 128], P('dp', 'tensor'), may hold values from -0.5 to 0.5
- output_weight: float32 [2048, 2048], P('tensor', 'dp'), may hold values from -0.125 to 0.125
- gateup_weight: float32 [2048, 2, 8192], P('dp', None, 'tensor'), may hold values from -0.125 to 0.125
- down_weight: float32 [8192, 2048], P('tensor', 'dp'), may hold values from -0.0625 to 0.0625
- norm_gains: float32 [2, 2048], P(None, 'dp'), may hold values from 0.5 to 1.5
- query_moment: float32 [2048, 2048], P('dp', 'tensor'), may hold values from -128 to 128
- keyval_moment: float32 [2048, 8, 128], P('dp', 'tensor'), may hold values from -128 to 128
- output_moment: float32 [2048, 2048], P('tensor', 'dp'), may hold values from -256 to 256
- gateup_moment: float32 [2048, 2, 8192], P('dp', None, 'tensor'), may hold values from -64 to 64
- down_moment: float32 [8192, 2048], P('tensor', 'dp'), may hold values from -160 to 160
- gains_moment: float32 [2, 2048], P(None, 'dp'), may hold values from -320 to 320
- query_square: float32 [2048, 2048], P('dp', 'tensor'), may hold values from 100 to 1000
- keyval_square: float32 [2048, 8, 128], P('dp', 'tensor'), may hold values from 100 to 1000
- output_square: float32 [2048, 2048], P('tensor', 'dp'), may hold values from 400 to 4000
- gateup_square: float32 [2048, 2, 8192], P('dp', None, 'tensor'), may hold values from 40 to 400
- down_square: float32 [8192, 2048], P('tensor', 'dp'), may hold values from 200 to 2000
- gains_square: float32 [2, 2048], P(None, 'dp'), may hold values from 700 to 7000
Outputs:
- layer_output: bfloat16 [2, 8, 1216, 2048], P(None, 'dp', 'tensor')
- input_grad: float32 [2, 8, 1216, 2048], P(None, 'dp', 'tensor')
- new_query: float32 [2048, 2048], P('dp', 'tensor')
- new_keyval: float32 [2048, 8, 128], P('dp', 'tensor')
- new_output: float32 [2048, 2048], P('tensor', 'dp')
- new_gateup: float32 [2048, 2, 8192], P('dp', None, 'tensor')
- new_down: float32 [8192, 2048], P('tensor', 'dp')
- new_gains: float32 [2, 2048], P(None, 'dp')
- next_query_moment: float32 [2048, 2048], P('dp', 'tensor')
- next_keyval_moment: float32 [2048, 8, 128], P('dp', 'tensor')
- next_output_moment: float32 [2048, 2048], P('tensor', 'dp')
- next_gateup_moment: float32 [2048, 2, 8192], P('dp', None, 'tensor')
- next_down_moment: float32 [8192, 2048], P('tensor', 'dp')
- next_gains_moment: float32 [2, 2048], P(None, 'dp')
- next_query_square: float32 [2048, 2048], P('dp', 'tensor')
- next_keyval_square: float32 [2048, 8, 128], P('dp', 'tensor')
- next_output_square: float32 [2048, 2048], P('tensor', 'dp')
- next_gateup_square: float32 [2048, 2, 8192], P('dp', None, 'tensor')
- next_down_square: float32 [8192, 2048], P('tensor', 'dp')
- next_gains_square: float32 [2, 2048], P(None, 'dp')
- trust_norms: float32 [2, 7], replicated
The draws below stay inside these ranges and needn't reach their ends.
Inputs may be any that keep to these rules, and one draw needn't show every extreme that they name: `cont_lengths`: each group's 3 continuation lengths sum to 192, and the longest is exactly 128.
All inputs are finite; a program needn't handle non-finite values.
Results may differ from the reference program's by a relative error of at most 0.025.
Values may be sent and summed in bfloat16 or wider, within the bound.
No kernel may reach another device: no remote copies, remote signals or barrier semaphores. Data moves between devices by JAX's collectives and lax.ppermute only.
A program may use at most 448 MiB of HBM per device.

```python
import math
import jax
import jax.numpy as jnp
import numpy as np
from jax import lax

MODEL_WIDTH = 2048
QH = 32
KVH = 8
HD = 64
FF = 8192
PROMPT = 1024
CONTS = 3
CONT_TOTAL = 192
CONT_MOST = 128
STEP = 3
MICRO = 2
DP_GROUPS = 8
GROUP = 1216
N_TENSOR = 4


def level_of(stream_key, shape, pieces, low, largest):
    def one(axis_at, parts):
        heights = jax.random.uniform(jax.random.fold_in(jax.random.fold_in(stream_key, 6), axis_at), (parts,), jnp.float32, low / len(pieces), largest / len(pieces))
        return jnp.repeat(jnp.exp(heights), shape[axis_at] // parts).reshape((-1,) + (1,) * (len(shape) - axis_at - 1))

    gain = one(*pieces[0])
    for cut in pieces[1:]:
        gain = gain * one(*cut)
    return gain


def profile(amount, total, reach, lean):
    portions = [(1 << 20) // math.isqrt(standing ** lean) + 1 for standing in range(2, amount + 1)]
    rest, holding = total - reach - (amount - 1), [1] * (amount - 1)
    while rest > 0:
        candidates = [i for i in range(amount - 1) if holding[i] < reach]
        mass, budget = sum([portions[i] for i in candidates]), rest
        for i in candidates:
            more = min(reach - holding[i], max(1, budget * portions[i] // mass), rest)
            holding[i] = holding[i] + more
            rest = rest - more
    return np.array([reach] + holding)


def uneven(key, number_of, total, reach, slope):
    if number_of == 2:
        one = jax.random.randint(key, (), max(1, total - reach), min(reach, total - 1) + 1)
        return jnp.stack([one, total - one])
    tallies = jnp.asarray(profile(number_of, total, reach, slope), jnp.int32)
    twos = (number_of - 1) // 2
    giver, receiver = tallies[1:1 + 2 * twos:2], tallies[2:2 + 2 * twos:2]
    room = jnp.minimum(giver - 1, reach - receiver)
    shifted = jax.random.randint(jax.random.fold_in(key, 1), (twos,), 0, 1 << 20) % (room + 1)
    tallies = tallies.at[1:1 + 2 * twos:2].set(giver - shifted).at[2:2 + 2 * twos:2].set(receiver + shifted)
    return tallies[jax.random.permutation(jax.random.fold_in(key, 2), number_of)]


def gaussian(rng, shape, spread, most, shards=(), kind=jnp.bfloat16):
    factor_of = level_of(rng, shape, shards, -0.22, 0.18) if shards else 1.0
    entries = jax.random.normal(rng, shape, jnp.float32) * spread * factor_of
    return jnp.minimum(jnp.maximum(entries, -most), most).astype(kind)


def setup_inputs(seed: int = 0) -> dict:
    key_list = jax.random.split(jax.random.key(seed), 22)
    tokens = gaussian(key_list[0], (MICRO, DP_GROUPS, GROUP, MODEL_WIDTH), 1.0, 6.0, ((1, 8), (2, 4)))
    cotangent = gaussian(key_list[1], (MICRO, DP_GROUPS, GROUP, MODEL_WIDTH), 1.0, 6.0, ((1, 8), (2, 4)))
    cont_lengths = jax.vmap(lambda own: uneven(own, CONTS, CONT_TOTAL, CONT_MOST, 1))(jax.random.split(key_list[2], MICRO * DP_GROUPS)).reshape((MICRO, DP_GROUPS, CONTS)).astype(jnp.int32)
    query_weight = gaussian(key_list[3], (MODEL_WIDTH, QH * HD), (MODEL_WIDTH // 16) ** -0.5, 0.5, ((0, 8), (1, 4)), jnp.float32)
    keyval_weight = gaussian(key_list[4], (MODEL_WIDTH, KVH, 2 * HD), (MODEL_WIDTH // 16) ** -0.5, 0.5, ((0, 8), (1, 4)), jnp.float32)
    output_weight = gaussian(key_list[5], (QH * HD, MODEL_WIDTH), (QH * HD) ** -0.5, 0.125, ((0, 4), (1, 8)), jnp.float32)
    gateup_weight = gaussian(key_list[6], (MODEL_WIDTH, 2, FF), MODEL_WIDTH ** -0.5, 0.125, ((0, 8), (2, 4)), jnp.float32)
    down_weight = gaussian(key_list[7], (FF, MODEL_WIDTH), FF ** -0.5, 0.0625, ((0, 4), (1, 8)), jnp.float32)
    norm_gains = jnp.clip(1.0 + 0.1 * jax.random.normal(key_list[8], (2, MODEL_WIDTH), jnp.float32), 0.5, 1.5)
    query_moment = gaussian(key_list[9], (MODEL_WIDTH, QH * HD), 20.0, 128.0, ((0, 8), (1, 4)), jnp.float32)
    keyval_moment = gaussian(key_list[10], (MODEL_WIDTH, KVH, 2 * HD), 20.0, 128.0, ((0, 8), (1, 4)), jnp.float32)
    output_moment = gaussian(key_list[11], (QH * HD, MODEL_WIDTH), 40.0, 256.0, ((0, 4), (1, 8)), jnp.float32)
    gateup_moment = gaussian(key_list[12], (MODEL_WIDTH, 2, FF), 12.0, 64.0, ((0, 8), (2, 4)), jnp.float32)
    down_moment = gaussian(key_list[13], (FF, MODEL_WIDTH), 26.0, 160.0, ((0, 4), (1, 8)), jnp.float32)
    gains_moment = gaussian(key_list[14], (2, MODEL_WIDTH), 50.0, 320.0, ((1, 8),), jnp.float32)
    query_square = jnp.clip(jnp.exp(math.log(1000.0) - 2.3025851 * jax.random.uniform(key_list[15], (MODEL_WIDTH, QH * HD), jnp.float32) ** level_of(key_list[15], (MODEL_WIDTH, QH * HD), ((0, 8), (1, 4)), -0.2, 0.2)), 100.0, 1000.0)
    keyval_square = jnp.clip(jnp.exp(math.log(1000.0) - 2.3025851 * jax.random.uniform(key_list[16], (MODEL_WIDTH, KVH, 2 * HD), jnp.float32) ** level_of(key_list[16], (MODEL_WIDTH, KVH, 2 * HD), ((0, 8), (1, 4)), -0.2, 0.2)), 100.0, 1000.0)
    output_square = jnp.clip(jnp.exp(math.log(4000.0) - 2.3025851 * jax.random.uniform(key_list[17], (QH * HD, MODEL_WIDTH), jnp.float32) ** level_of(key_list[17], (QH * HD, MODEL_WIDTH), ((0, 4), (1, 8)), -0.2, 0.2)), 400.0, 4000.0)
    gateup_square = jnp.clip(jnp.exp(math.log(400.0) - 2.3025851 * jax.random.uniform(key_list[18], (MODEL_WIDTH, 2, FF), jnp.float32) ** level_of(key_list[18], (MODEL_WIDTH, 2, FF), ((0, 8), (2, 4)), -0.2, 0.2)), 40.0, 400.0)
    down_square = jnp.clip(jnp.exp(math.log(2000.0) - 2.3025851 * jax.random.uniform(key_list[19], (FF, MODEL_WIDTH), jnp.float32) ** level_of(key_list[19], (FF, MODEL_WIDTH), ((0, 4), (1, 8)), -0.2, 0.2)), 200.0, 2000.0)
    gains_square = jnp.clip(jnp.exp(math.log(7000.0) - 2.3025851 * jax.random.uniform(key_list[20], (2, MODEL_WIDTH), jnp.float32) ** level_of(key_list[20], (2, MODEL_WIDTH), ((1, 8),), -0.2, 0.2)), 700.0, 7000.0)
    return dict(tokens=tokens, cotangent=cotangent, cont_lengths=cont_lengths, query_weight=query_weight, keyval_weight=keyval_weight, output_weight=output_weight, gateup_weight=gateup_weight, down_weight=down_weight, norm_gains=norm_gains, query_moment=query_moment, keyval_moment=keyval_moment, output_moment=output_moment, gateup_moment=gateup_moment, down_moment=down_moment, gains_moment=gains_moment, query_square=query_square, keyval_square=keyval_square, output_square=output_square, gateup_square=gateup_square, down_square=down_square, gains_square=gains_square)


@jax.custom_vjp
def reduced_precision(v):
    return lax.optimization_barrier(v.astype(jnp.bfloat16)).astype(jnp.float32)

@jax.custom_vjp
def low_back(v):
    return v

def low_keep(v):
    return (reduced_precision(v), None)

def low_pass(kept, grad):
    return (grad,)

def back_keep(v):
    return (v, None)

def back_low(kept, grad):
    return (reduced_precision(grad),)
reduced_precision.defvjp(low_keep, low_pass)
low_back.defvjp(back_keep, back_low)
norm_eps = 1e-05
branch_scale = 0.22
score_scale = 0.015625
rope_base = 10000000.0
moment_decay = 0.5
learn_rate = 0.25
ratio_eps = 1e-06
masked_fill = -1e+30
highest_precision = lax.Precision.HIGHEST

def layout(lengths):
    row_index = jnp.arange(GROUP, dtype=jnp.int32)
    ends = jnp.cumsum(lengths).astype(jnp.int32)
    starts = (ends - lengths).astype(jnp.int32)
    within = row_index - PROMPT
    inside = (within[:, None] >= starts[None, :]) & (within[:, None] < ends[None, :])
    labels = jnp.arange(1, CONTS + 1, dtype=jnp.int32)
    segment = lax.optimization_barrier(jnp.sum(jnp.where(inside, labels[None, :], 0), axis=1)).astype(jnp.int32)
    offsets = lax.optimization_barrier(jnp.sum(jnp.where(inside, starts[None, :], 0), axis=1)).astype(jnp.int32)
    position = (row_index - offsets).astype(jnp.int32)
    causal = row_index[None, :] <= row_index[:, None]
    shared = (segment[None, :] == segment[:, None]) | (segment[None, :] == 0)
    return (causal & shared, position)

def rope_tables(position):
    half_size = HD // 2
    inverse = rope_base ** (-2.0 * jnp.arange(half_size, dtype=jnp.float32) / HD)
    angle = position.astype(jnp.float32)[:, None] * inverse[None, :]
    return (jnp.cos(angle)[:, None, :], jnp.sin(angle)[:, None, :])

def rotate(field, cos_table, sin_table):
    half_size = field.shape[-1] // 2
    first_half = field[..., :half_size]
    second_half = field[..., half_size:]
    return jnp.concatenate([first_half * cos_table - second_half * sin_table, second_half * cos_table + first_half * sin_table], axis=-1)

def forward(weights, tokens, visible, position):
    query_low, keyval_low, output_low, gateup_low, down_weight_reduced, gains_low = [reduced_precision(weight) for weight in weights]
    prompt_groups = N_TENSOR
    rows = tokens.shape[0]
    query_local = QH // prompt_groups
    keyval_local = KVH // prompt_groups
    hidden_state_shard_local = FF // prompt_groups
    head_repeat = QH // KVH
    cos_table, sin_table = rope_tables(position)
    scale_one = lax.rsqrt(lax.optimization_barrier(jnp.mean(tokens * tokens, axis=1, keepdims=True)) + norm_eps)
    normed_one = reduced_precision(tokens * scale_one * gains_low[0][None, :])
    copies_one = low_back(jnp.broadcast_to(normed_one[None], (prompt_groups, rows, MODEL_WIDTH)))
    query_raw = low_back(jnp.einsum('trd,dtk->trk', copies_one, query_low.reshape(MODEL_WIDTH, prompt_groups, query_local * HD), precision=highest_precision))
    keyval_raw = low_back(jnp.einsum('trd,dthk->trhk', copies_one, keyval_low.reshape(MODEL_WIDTH, prompt_groups, keyval_local, 2 * HD), precision=highest_precision))
    query_raw = jnp.transpose(query_raw, (1, 0, 2)).reshape(rows, QH, HD)
    keyval_raw = jnp.transpose(keyval_raw, (1, 0, 2, 3)).reshape(rows, KVH, 2 * HD)
    queries = reduced_precision(rotate(query_raw, cos_table, sin_table)).reshape(rows, KVH, head_repeat, HD)
    key_rows = reduced_precision(rotate(keyval_raw[:, :, :HD], cos_table, sin_table))
    values = reduced_precision(keyval_raw[:, :, HD:])
    scores = low_back(jnp.einsum('ikrd,jkd->krij', queries, key_rows, precision=highest_precision) * score_scale)
    scores = jnp.where(visible[None, None], scores, masked_fill)
    attn_prob = reduced_precision(jax.nn.softmax(scores, axis=-1))
    mixed = jnp.einsum('krij,jkd->ikrd', attn_prob, values, precision=highest_precision).reshape(rows, QH * HD)
    mixed = reduced_precision(low_back(mixed))
    partial_attn = reduced_precision(jnp.einsum('rtk,tkd->trd', mixed.reshape(rows, prompt_groups, query_local * HD), output_low.reshape(prompt_groups, query_local * HD, MODEL_WIDTH), precision=highest_precision))
    attn_branch = low_back(lax.optimization_barrier(jnp.sum(partial_attn, axis=0)))
    middle = tokens + branch_scale * attn_branch
    scale_two = lax.rsqrt(lax.optimization_barrier(jnp.mean(middle * middle, axis=1, keepdims=True)) + norm_eps)
    normed_two = reduced_precision(middle * scale_two * gains_low[1][None, :])
    copies_two = low_back(jnp.broadcast_to(normed_two[None], (prompt_groups, rows, MODEL_WIDTH)))
    gate_up = low_back(jnp.einsum('trd,dctf->trcf', copies_two, gateup_low.reshape(MODEL_WIDTH, 2, prompt_groups, hidden_state_shard_local), precision=highest_precision))
    hidden_state = reduced_precision(jax.nn.silu(gate_up[:, :, 0]) * gate_up[:, :, 1])
    partial_feedforward = reduced_precision(jnp.einsum('ies,isg->ieg', hidden_state, down_weight_reduced.reshape(prompt_groups, hidden_state_shard_local, MODEL_WIDTH), precision=highest_precision))
    ffn_branch = low_back(lax.optimization_barrier(jnp.sum(partial_feedforward, axis=0)))
    return middle + branch_scale * ffn_branch

def reference(tokens, cotangent, cont_lengths, query_weight, keyval_weight, output_weight, gateup_weight, down_weight, norm_gains, query_moment, keyval_moment, output_moment, gateup_moment, down_moment, gains_moment, query_square, keyval_square, output_square, gateup_square, down_square, gains_square):
    weights = (query_weight, keyval_weight, output_weight, gateup_weight, down_weight, norm_gains)
    firsts = (query_moment, keyval_moment, output_moment, gateup_moment, down_moment, gains_moment)
    seconds = (query_square, keyval_square, output_square, gateup_square, down_square, gains_square)
    group_count = MICRO * DP_GROUPS
    flat_tokens = tokens.reshape(group_count, GROUP, MODEL_WIDTH).astype(jnp.float32)
    flat_cot = cotangent.reshape(group_count, GROUP, MODEL_WIDTH).astype(jnp.float32)
    flat_lengths = cont_lengths.reshape(group_count, CONTS).astype(jnp.int32)

    def one_group(totals, group_data):
        group_tokens, group_cot, lengths = group_data
        visible, position = layout(lengths)

        def apply_layer(params, inputs):
            return forward(params, inputs, visible, position)
        output, pullback = jax.vjp(apply_layer, weights, group_tokens)
        grads, group_input_grad = pullback(group_cot)
        totals = tuple((old_sum + new_term for old_sum, new_term in zip(totals, grads)))
        return (totals, (output.astype(jnp.bfloat16), group_input_grad))
    zeros = tuple((jnp.zeros(weight.shape, jnp.float32) for weight in weights))
    grads, (outputs, input_grads) = lax.scan(one_group, zeros, (flat_tokens, flat_cot, flat_lengths))
    correction = 1.0 - moment_decay ** STEP
    new_firsts = []
    new_seconds = []
    directions = []
    for grad, first, second in zip(grads, firsts, seconds):
        first_new = moment_decay * first + (1.0 - moment_decay) * grad
        second_new = moment_decay * second + (1.0 - moment_decay) * grad * grad
        direction = first_new / correction / (jnp.sqrt(second_new / correction) + ratio_eps)
        new_firsts.append(first_new)
        new_seconds.append(second_new)
        directions.append(direction)
    weight_norms = jnp.concatenate([jnp.stack([jnp.sqrt(jnp.sum(weights[slot] * weights[slot])) for slot in range(5)]), jnp.sqrt(lax.optimization_barrier(jnp.sum(norm_gains * norm_gains, axis=1)))])
    update_norms = jnp.concatenate([jnp.stack([jnp.sqrt(jnp.sum(directions[slot] * directions[slot])) for slot in range(5)]), jnp.sqrt(lax.optimization_barrier(jnp.sum(directions[5] * directions[5], axis=1)))])
    trust_norms = jnp.stack([weight_norms, update_norms])
    ratio = weight_norms / (update_norms + ratio_eps)
    new_weights = [weights[slot] - learn_rate * ratio[slot] * directions[slot] for slot in range(5)]
    new_gains = norm_gains - learn_rate * ratio[5:7][:, None] * directions[5]
    layer_output = outputs.reshape(MICRO, DP_GROUPS, GROUP, MODEL_WIDTH)
    input_grad = input_grads.reshape(MICRO, DP_GROUPS, GROUP, MODEL_WIDTH)
    return (layer_output, input_grad, new_weights[0], new_weights[1], new_weights[2], new_weights[3], new_weights[4], new_gains, new_firsts[0], new_firsts[1], new_firsts[2], new_firsts[3], new_firsts[4], new_firsts[5], new_seconds[0], new_seconds[1], new_seconds[2], new_seconds[3], new_seconds[4], new_seconds[5], trust_norms)
```

```python
import jax
import jax.numpy as jnp
from jax import lax
from jax.sharding import PartitionSpec as P

HD = 64
PROMPT = 1024
CONTS = 3
STEP = 3


norm_eps = 1e-05
branch_scale = 0.22
score_scale = 0.015625
rope_base = 10000000.0
moment_decay = 0.5
learn_rate = 0.25
ratio_eps = 1e-06
masked_fill = -1e30


def layout(lengths, group_rows):
    row_index = jnp.arange(group_rows, dtype=jnp.int32)
    ends = jnp.cumsum(lengths)
    starts = ends - lengths
    within = row_index - PROMPT
    inside = (within[:, None] >= starts[None, :]) & (within[:, None] < ends[None, :])
    labels = jnp.arange(1, CONTS + 1, dtype=jnp.int32)
    segment = jnp.sum(jnp.where(inside, labels[None, :], 0), axis=1)
    offsets = jnp.sum(jnp.where(inside, starts[None, :], 0), axis=1)
    position = row_index - offsets
    causal = row_index[None, :] <= row_index[:, None]
    shared = (segment[None, :] == segment[:, None]) | (segment[None, :] == 0)
    return (causal & shared, position)


def rope_tables(position):
    half_size = HD // 2
    inverse = rope_base ** (-2.0 * jnp.arange(half_size, dtype=jnp.float32) / HD)
    angle = position.astype(jnp.float32)[:, None] * inverse[None, :]
    return (jnp.cos(angle)[:, None, :], jnp.sin(angle)[:, None, :])


def rotate(field, cos_table, sin_table):
    half_size = field.shape[-1] // 2
    first_half = field[..., :half_size]
    second_half = field[..., half_size:]
    return jnp.concatenate(
        [
            first_half * cos_table - second_half * sin_table,
            second_half * cos_table + first_half * sin_table,
        ],
        axis=-1,
    )


def rotate_back(grad_field, cos_table, sin_table):
    half_size = grad_field.shape[-1] // 2
    first_half = grad_field[..., :half_size]
    second_half = grad_field[..., half_size:]
    return jnp.concatenate(
        [
            first_half * cos_table + second_half * sin_table,
            second_half * cos_table - first_half * sin_table,
        ],
        axis=-1,
    )


def attend(queries, key_rows, values, visible, block_rows):
    outputs = []
    log_totals = []
    for block in range(2):
        begin = block * block_rows
        stop = begin + block_rows
        scores = (
            jnp.einsum(
                "ikrd,jkd->krij",
                queries[begin:stop],
                key_rows[:stop],
                preferred_element_type=jnp.float32,
            )
            * score_scale
        )
        scores = jnp.where(visible[begin:stop, :stop][None, None], scores, masked_fill)
        row_peak = jnp.max(scores, axis=-1, keepdims=True)
        shifted_exp = jnp.exp(scores - row_peak)
        row_total = jnp.sum(shifted_exp, axis=-1, keepdims=True)
        attn_prob = (shifted_exp / row_total).astype(jnp.bfloat16)
        outputs.append(
            jnp.einsum(
                "krij,jkd->ikrd", attn_prob, values[:stop], preferred_element_type=jnp.float32
            )
        )
        log_totals.append(row_peak + jnp.log(row_total))
    return (jnp.concatenate(outputs, axis=0), jnp.concatenate(log_totals, axis=2))


def attend_back(queries, key_rows, values, visible, log_totals, mixed_grad, block_rows):
    query_grads = []
    key_grad = jnp.zeros(key_rows.shape, jnp.float32)
    value_grad = jnp.zeros(values.shape, jnp.float32)
    for block in range(2):
        begin = block * block_rows
        stop = begin + block_rows
        query_block = queries[begin:stop]
        grad_block = mixed_grad[begin:stop]
        scores = (
            jnp.einsum(
                "ikrd,jkd->krij", query_block, key_rows[:stop], preferred_element_type=jnp.float32
            )
            * score_scale
        )
        attn_prob = jnp.where(
            visible[begin:stop, :stop][None, None],
            jnp.exp(scores - log_totals[:, :, begin:stop]),
            0.0,
        )
        prob_grad = jnp.einsum(
            "ikrd,jkd->krij", grad_block, values[:stop], preferred_element_type=jnp.float32
        )
        row_dot = jnp.sum(attn_prob * prob_grad, axis=-1, keepdims=True)
        score_grad = (attn_prob * (prob_grad - row_dot)).astype(jnp.bfloat16)
        query_grads.append(
            jnp.einsum(
                "krij,jkd->ikrd", score_grad, key_rows[:stop], preferred_element_type=jnp.float32
            )
            * score_scale
        )
        key_grad = key_grad.at[:stop].add(
            jnp.einsum(
                "krij,ikrd->jkd", score_grad, query_block, preferred_element_type=jnp.float32
            )
            * score_scale
        )
        value_grad = value_grad.at[:stop].add(
            jnp.einsum(
                "krij,ikrd->jkd",
                attn_prob.astype(jnp.bfloat16),
                grad_block,
                preferred_element_type=jnp.float32,
            )
        )
    return (jnp.concatenate(query_grads, axis=0), key_grad, value_grad)


def norm_back(upstream, normed_hat, scale_rows, gain_row):
    scaled = upstream * gain_row[None, :]
    through = scale_rows * (
        scaled - normed_hat * jnp.mean(scaled * normed_hat, axis=1, keepdims=True)
    )
    return (through, jnp.sum(upstream * normed_hat, axis=0))


def contract_rows(left, right):
    return lax.dot_general(
        left, right, (((0,), (0,)), ((), ())), preferred_element_type=jnp.float32
    )


def contract_cols(left, right):
    return lax.dot_general(
        left, right, (((1,), (1,)), ((), ())), preferred_element_type=jnp.float32
    )


def line_gather(x, count):
    place = lax.axis_index("tensor")
    rows = x.shape[0]
    out = jnp.zeros((count * rows,) + x.shape[1:], x.dtype)
    from_left = x
    from_right = x
    received = []
    for step in range(1, count):
        from_left = lax.ppermute(
            from_left, "tensor", [(i, i + 1) for i in range(step - 1, count - 1)]
        )
        from_right = lax.ppermute(
            from_right, "tensor", [(i, i - 1) for i in range(1, count - step + 1)]
        )
        received.append((from_left, place - step, place - step >= 0))
        received.append((from_right, place + step, place + step <= count - 1))
    for piece, slot, valid in received:
        out = lax.dynamic_update_slice_in_dim(out, piece, jnp.where(valid, slot, place) * rows, 0)
    return lax.dynamic_update_slice_in_dim(out, x, place * rows, 0)


def line_scatter(partial, count):
    place = lax.axis_index("tensor")
    rows = partial.shape[0] // count

    def chunk(index):
        return lax.dynamic_slice_in_dim(partial, jnp.clip(index, 0, count - 1) * rows, rows, 0)

    to_right = None
    to_left = None
    for step in range(1, count):
        send = chunk(place + count - step)
        if to_right is not None:
            send = send + to_right
        to_right = lax.ppermute(
            send.astype(jnp.bfloat16), "tensor", [(i, i + 1) for i in range(step)]
        ).astype(jnp.float32)
        send = chunk(place - count + step)
        if to_left is not None:
            send = send + to_left
        to_left = lax.ppermute(
            send.astype(jnp.bfloat16), "tensor", [(i, i - 1) for i in range(count - step, count)]
        ).astype(jnp.float32)
    total = chunk(place)
    if to_right is not None:
        total = total + to_right + to_left
    return total


def per_device(
    tokens,
    cotangent,
    cont_lengths,
    query_weight,
    keyval_weight,
    output_weight,
    gateup_weight,
    down_weight,
    norm_gains,
    query_moment,
    keyval_moment,
    output_moment,
    gateup_moment,
    down_moment,
    gains_moment,
    query_square,
    keyval_square,
    output_square,
    gateup_square,
    down_square,
    gains_square,
):
    masters = (query_weight, keyval_weight, output_weight, gateup_weight, down_weight, norm_gains)
    firsts = (query_moment, keyval_moment, output_moment, gateup_moment, down_moment, gains_moment)
    seconds = (query_square, keyval_square, output_square, gateup_square, down_square, gains_square)
    rounded = tuple((master.astype(jnp.bfloat16) for master in masters))
    gathered = (
        lax.all_gather(rounded[0], "dp", axis=0, tiled=True),
        lax.all_gather(rounded[1], "dp", axis=0, tiled=True),
        lax.all_gather(rounded[2], "dp", axis=1, tiled=True),
        lax.all_gather(rounded[3], "dp", axis=0, tiled=True),
        lax.all_gather(rounded[4], "dp", axis=1, tiled=True),
        lax.all_gather(rounded[5], "dp", axis=1, tiled=True),
    )
    full_query, full_keyval, full_output, full_gateup, full_down, full_gains = gathered
    gain_values = full_gains.astype(jnp.float32)
    tensor_count = lax.axis_size("tensor")
    group_rows = tokens.shape[2] * tensor_count
    block_rows = group_rows // 2
    keyval_heads = full_keyval.shape[1]
    query_heads = full_query.shape[1] // HD
    head_repeat = query_heads // keyval_heads

    def micro_step(token_rows, cot_rows, lengths):
        visible, position = layout(lengths, group_rows)
        cos_table, sin_table = rope_tables(position)
        start_rows = token_rows.astype(jnp.float32)
        scale_one = lax.rsqrt(jnp.mean(start_rows * start_rows, axis=1, keepdims=True) + norm_eps)
        hat_one = start_rows * scale_one
        normed_one = (hat_one * gain_values[0][None, :]).astype(jnp.bfloat16)
        rows_one = line_gather(normed_one, tensor_count)
        query_raw = jnp.dot(rows_one, full_query, preferred_element_type=jnp.float32).reshape(
            group_rows, query_heads, HD
        )
        keyval_raw = jnp.einsum(
            "rd,dhk->rhk", rows_one, full_keyval, preferred_element_type=jnp.float32
        )
        queries = (
            rotate(query_raw, cos_table, sin_table)
            .astype(jnp.bfloat16)
            .reshape(group_rows, keyval_heads, head_repeat, HD)
        )
        key_rows = rotate(keyval_raw[:, :, :HD], cos_table, sin_table).astype(jnp.bfloat16)
        values = keyval_raw[:, :, HD:].astype(jnp.bfloat16)
        mixed_full, log_totals = attend(queries, key_rows, values, visible, block_rows)
        mixed = mixed_full.astype(jnp.bfloat16).reshape(group_rows, query_heads * HD)
        attn_branch = line_scatter(
            jnp.dot(mixed, full_output, preferred_element_type=jnp.float32), tensor_count
        )
        middle = start_rows + branch_scale * attn_branch
        scale_two = lax.rsqrt(jnp.mean(middle * middle, axis=1, keepdims=True) + norm_eps)
        hat_two = middle * scale_two
        normed_two = (hat_two * gain_values[1][None, :]).astype(jnp.bfloat16)
        rows_two = line_gather(normed_two, tensor_count)
        gate_up = jnp.einsum(
            "rd,dcf->rcf", rows_two, full_gateup, preferred_element_type=jnp.float32
        )
        gate_part = gate_up[:, 0]
        up_part = gate_up[:, 1]
        sigmoid_gate = jax.nn.sigmoid(gate_part)
        silu_gate = gate_part * sigmoid_gate
        hidden_state = (silu_gate * up_part).astype(jnp.bfloat16)
        ffn_branch = line_scatter(
            jnp.dot(hidden_state, full_down, preferred_element_type=jnp.float32), tensor_count
        )
        layer_rows = (middle + branch_scale * ffn_branch).astype(jnp.bfloat16)
        upstream = cot_rows.astype(jnp.float32)
        ffn_grad = (branch_scale * upstream).astype(jnp.bfloat16)
        ffn_grad_all = line_gather(ffn_grad, tensor_count)
        grad_down = contract_rows(hidden_state, ffn_grad_all)
        hidden_grad = contract_cols(ffn_grad_all, full_down)
        gate_grad = hidden_grad * up_part * sigmoid_gate * (1.0 + gate_part * (1.0 - sigmoid_gate))
        up_grad = hidden_grad * silu_gate
        gateup_grad = jnp.stack([gate_grad, up_grad], axis=1).astype(jnp.bfloat16)
        grad_gateup = jnp.einsum(
            "rd,rcf->dcf", rows_two, gateup_grad, preferred_element_type=jnp.float32
        )
        normed_two_grad = line_scatter(
            jnp.einsum(
                "rcf,dcf->rd", gateup_grad, full_gateup, preferred_element_type=jnp.float32
            ),
            tensor_count,
        )
        middle_back, gain_two = norm_back(normed_two_grad, hat_two, scale_two, gain_values[1])
        middle_grad = upstream + middle_back
        attn_grad = (branch_scale * middle_grad).astype(jnp.bfloat16)
        attn_grad_all = line_gather(attn_grad, tensor_count)
        grad_output = contract_rows(mixed, attn_grad_all)
        mixed_grad = (
            contract_cols(attn_grad_all, full_output)
            .astype(jnp.bfloat16)
            .reshape(group_rows, keyval_heads, head_repeat, HD)
        )
        query_grad, key_grad, value_grad = attend_back(
            queries, key_rows, values, visible, log_totals, mixed_grad, block_rows
        )
        query_raw_grad = (
            rotate_back(query_grad.reshape(group_rows, query_heads, HD), cos_table, sin_table)
            .astype(jnp.bfloat16)
            .reshape(group_rows, query_heads * HD)
        )
        keyval_raw_grad = jnp.concatenate(
            [rotate_back(key_grad, cos_table, sin_table), value_grad], axis=2
        ).astype(jnp.bfloat16)
        grad_query = contract_rows(rows_one, query_raw_grad)
        grad_keyval = jnp.einsum(
            "rd,rhk->dhk", rows_one, keyval_raw_grad, preferred_element_type=jnp.float32
        )
        normed_one_grad = line_scatter(
            contract_cols(query_raw_grad, full_query)
            + jnp.einsum(
                "rhk,dhk->rd", keyval_raw_grad, full_keyval, preferred_element_type=jnp.float32
            ),
            tensor_count,
        )
        start_back, gain_one = norm_back(normed_one_grad, hat_one, scale_one, gain_values[0])
        input_rows = middle_grad + start_back
        gain_grad = jnp.stack([gain_one, gain_two])
        return (
            layer_rows,
            input_rows,
            (grad_query, grad_keyval, grad_output, grad_gateup, grad_down, gain_grad),
        )

    out_list = []
    grad_list = []
    totals = None
    for step_index in range(tokens.shape[0]):
        layer_rows, input_rows, grads = micro_step(
            tokens[step_index, 0], cotangent[step_index, 0], cont_lengths[step_index, 0]
        )
        out_list.append(layer_rows)
        grad_list.append(input_rows)
        if totals is None:
            totals = grads
        else:
            totals = tuple((old_sum + new_term for old_sum, new_term in zip(totals, grads)))
    layer_output = jnp.stack(out_list)[:, None]
    input_grad = jnp.stack(grad_list)[:, None]
    width = totals[0].shape[0]
    gain_total = lax.psum(totals[5], "tensor")
    summed = (
        lax.psum_scatter(
            totals[0].astype(jnp.bfloat16), "dp", scatter_dimension=0, tiled=True
        ).astype(jnp.float32),
        lax.psum_scatter(
            totals[1].reshape(width, -1).astype(jnp.bfloat16), "dp", scatter_dimension=0, tiled=True
        )
        .astype(jnp.float32)
        .reshape(-1, *totals[1].shape[1:]),
        lax.psum_scatter(
            totals[2].astype(jnp.bfloat16), "dp", scatter_dimension=1, tiled=True
        ).astype(jnp.float32),
        lax.psum_scatter(
            totals[3].reshape(width, -1).astype(jnp.bfloat16), "dp", scatter_dimension=0, tiled=True
        )
        .astype(jnp.float32)
        .reshape(-1, *totals[3].shape[1:]),
        lax.psum_scatter(
            totals[4].astype(jnp.bfloat16), "dp", scatter_dimension=1, tiled=True
        ).astype(jnp.float32),
        lax.psum_scatter(
            gain_total.astype(jnp.bfloat16), "dp", scatter_dimension=1, tiled=True
        ).astype(jnp.float32),
    )
    correction = 1.0 - moment_decay**STEP
    new_firsts = []
    new_seconds = []
    directions = []
    for grad, first, second in zip(summed, firsts, seconds):
        first_new = moment_decay * first + (1.0 - moment_decay) * grad
        second_new = moment_decay * second + (1.0 - moment_decay) * grad * grad
        direction = first_new / correction / (jnp.sqrt(second_new / correction) + ratio_eps)
        new_firsts.append(first_new)
        new_seconds.append(second_new)
        directions.append(direction)
    weight_part = jnp.concatenate(
        [
            jnp.stack([jnp.sum(masters[slot] * masters[slot]) for slot in range(5)]),
            jnp.sum(norm_gains * norm_gains, axis=1) / tensor_count,
        ]
    )
    update_part = jnp.concatenate(
        [
            jnp.stack([jnp.sum(directions[slot] * directions[slot]) for slot in range(5)]),
            jnp.sum(directions[5] * directions[5], axis=1) / tensor_count,
        ]
    )
    square_totals = lax.psum(jnp.stack([weight_part, update_part]), ("dp", "tensor"))
    trust_norms = jnp.sqrt(square_totals)
    ratio = trust_norms[0] / (trust_norms[1] + ratio_eps)
    new_weights = [masters[slot] - learn_rate * ratio[slot] * directions[slot] for slot in range(5)]
    new_gains = norm_gains - learn_rate * ratio[5:7][:, None] * directions[5]
    return (
        layer_output,
        input_grad,
        new_weights[0],
        new_weights[1],
        new_weights[2],
        new_weights[3],
        new_weights[4],
        new_gains,
        new_firsts[0],
        new_firsts[1],
        new_firsts[2],
        new_firsts[3],
        new_firsts[4],
        new_firsts[5],
        new_seconds[0],
        new_seconds[1],
        new_seconds[2],
        new_seconds[3],
        new_seconds[4],
        new_seconds[5],
        trust_norms,
    )


def solution(mesh):
    return jax.shard_map(
        per_device,
        mesh=mesh,
        in_specs=(
            P(None, "dp", "tensor", None),
            P(None, "dp", "tensor", None),
            P(None, "dp", None),
            P("dp", "tensor"),
            P("dp", "tensor", None),
            P("tensor", "dp"),
            P("dp", None, "tensor"),
            P("tensor", "dp"),
            P(None, "dp"),
            P("dp", "tensor"),
            P("dp", "tensor", None),
            P("tensor", "dp"),
            P("dp", None, "tensor"),
            P("tensor", "dp"),
            P(None, "dp"),
            P("dp", "tensor"),
            P("dp", "tensor", None),
            P("tensor", "dp"),
            P("dp", None, "tensor"),
            P("tensor", "dp"),
            P(None, "dp"),
        ),
        out_specs=(
            P(None, "dp", "tensor", None),
            P(None, "dp", "tensor", None),
            P("dp", "tensor"),
            P("dp", "tensor", None),
            P("tensor", "dp"),
            P("dp", None, "tensor"),
            P("tensor", "dp"),
            P(None, "dp"),
            P("dp", "tensor"),
            P("dp", "tensor", None),
            P("tensor", "dp"),
            P("dp", None, "tensor"),
            P("tensor", "dp"),
            P(None, "dp"),
            P("dp", "tensor"),
            P("dp", "tensor", None),
            P("tensor", "dp"),
            P("dp", None, "tensor"),
            P("tensor", "dp"),
            P(None, "dp"),
            P(),
        ),
        check_vma=False,
    )
```

```python
import jax
import jax.numpy as jnp
from jax import lax
from jax.sharding import PartitionSpec as P

HD = 64
PROMPT = 1024
CONTS = 3
STEP = 3


norm_eps = 1e-05
branch_scale = 0.22
score_scale = 0.015625
rope_base = 10000000.0
moment_decay = 0.5
learn_rate = 0.25
ratio_eps = 1e-06
masked_fill = -1e30


def layout(lengths, group_rows):
    row_index = jnp.arange(group_rows, dtype=jnp.int32)
    ends = jnp.cumsum(lengths)
    starts = ends - lengths
    within = row_index - PROMPT
    inside = (within[:, None] >= starts[None, :]) & (within[:, None] < ends[None, :])
    labels = jnp.arange(1, CONTS + 1, dtype=jnp.int32)
    segment = jnp.sum(jnp.where(inside, labels[None, :], 0), axis=1)
    offsets = jnp.sum(jnp.where(inside, starts[None, :], 0), axis=1)
    position = row_index - offsets
    causal = row_index[None, :] <= row_index[:, None]
    shared = (segment[None, :] == segment[:, None]) | (segment[None, :] == 0)
    return (causal & shared, position)


def rope_tables(position):
    half_size = HD // 2
    inverse = rope_base ** (-2.0 * jnp.arange(half_size, dtype=jnp.float32) / HD)
    angle = position.astype(jnp.float32)[:, None] * inverse[None, :]
    return (jnp.cos(angle)[:, None, :], jnp.sin(angle)[:, None, :])


def rotate(field, cos_table, sin_table):
    half_size = field.shape[-1] // 2
    first_half = field[..., :half_size]
    second_half = field[..., half_size:]
    return jnp.concatenate(
        [
            first_half * cos_table - second_half * sin_table,
            second_half * cos_table + first_half * sin_table,
        ],
        axis=-1,
    )


def rotate_back(grad_field, cos_table, sin_table):
    half_size = grad_field.shape[-1] // 2
    first_half = grad_field[..., :half_size]
    second_half = grad_field[..., half_size:]
    return jnp.concatenate(
        [
            first_half * cos_table + second_half * sin_table,
            second_half * cos_table - first_half * sin_table,
        ],
        axis=-1,
    )


def attend(queries, key_rows, values, visible, block_rows):
    outputs = []
    log_totals = []
    for block in range(2):
        begin = block * block_rows
        stop = begin + block_rows
        scores = (
            jnp.einsum(
                "ikrd,jkd->krij",
                queries[begin:stop],
                key_rows[:stop],
                preferred_element_type=jnp.float32,
            )
            * score_scale
        )
        scores = jnp.where(visible[begin:stop, :stop][None, None], scores, masked_fill)
        row_peak = jnp.max(scores, axis=-1, keepdims=True)
        shifted_exp = jnp.exp(scores - row_peak)
        row_total = jnp.sum(shifted_exp, axis=-1, keepdims=True)
        attn_prob = (shifted_exp / row_total).astype(jnp.bfloat16)
        outputs.append(
            jnp.einsum(
                "krij,jkd->ikrd", attn_prob, values[:stop], preferred_element_type=jnp.float32
            )
        )
        log_totals.append(row_peak + jnp.log(row_total))
    return (jnp.concatenate(outputs, axis=0), jnp.concatenate(log_totals, axis=2))


def attend_back(queries, key_rows, values, visible, log_totals, mixed_grad, block_rows):
    query_grads = []
    key_grad = jnp.zeros(key_rows.shape, jnp.float32)
    value_grad = jnp.zeros(values.shape, jnp.float32)
    for block in range(2):
        begin = block * block_rows
        stop = begin + block_rows
        query_block = queries[begin:stop]
        grad_block = mixed_grad[begin:stop]
        scores = (
            jnp.einsum(
                "ikrd,jkd->krij", query_block, key_rows[:stop], preferred_element_type=jnp.float32
            )
            * score_scale
        )
        attn_prob = jnp.where(
            visible[begin:stop, :stop][None, None],
            jnp.exp(scores - log_totals[:, :, begin:stop]),
            0.0,
        )
        prob_grad = jnp.einsum(
            "ikrd,jkd->krij", grad_block, values[:stop], preferred_element_type=jnp.float32
        )
        row_dot = jnp.sum(attn_prob * prob_grad, axis=-1, keepdims=True)
        score_grad = (attn_prob * (prob_grad - row_dot)).astype(jnp.bfloat16)
        query_grads.append(
            jnp.einsum(
                "krij,jkd->ikrd", score_grad, key_rows[:stop], preferred_element_type=jnp.float32
            )
            * score_scale
        )
        key_grad = key_grad.at[:stop].add(
            jnp.einsum(
                "krij,ikrd->jkd", score_grad, query_block, preferred_element_type=jnp.float32
            )
            * score_scale
        )
        value_grad = value_grad.at[:stop].add(
            jnp.einsum(
                "krij,ikrd->jkd",
                attn_prob.astype(jnp.bfloat16),
                grad_block,
                preferred_element_type=jnp.float32,
            )
        )
    return (jnp.concatenate(query_grads, axis=0), key_grad, value_grad)


def norm_back(upstream, normed_hat, scale_rows, gain_row):
    scaled = upstream * gain_row[None, :]
    through = scale_rows * (
        scaled - normed_hat * jnp.mean(scaled * normed_hat, axis=1, keepdims=True)
    )
    return (through, jnp.sum(upstream * normed_hat, axis=0))


def contract_rows(left, right):
    return lax.dot_general(
        left, right, (((0,), (0,)), ((), ())), preferred_element_type=jnp.float32
    )


def contract_cols(left, right):
    return lax.dot_general(
        left, right, (((1,), (1,)), ((), ())), preferred_element_type=jnp.float32
    )


def line_gather(x, count):
    place = lax.axis_index("tensor")
    rows = x.shape[0]
    out = jnp.zeros((count * rows,) + x.shape[1:], x.dtype)
    from_left = x
    from_right = x
    received = []
    for step in range(1, count):
        from_left = lax.ppermute(
            from_left, "tensor", [(i, i + 1) for i in range(step - 1, count - 1)]
        )
        from_right = lax.ppermute(
            from_right, "tensor", [(i, i - 1) for i in range(1, count - step + 1)]
        )
        received.append((from_left, place - step, place - step >= 0))
        received.append((from_right, place + step, place + step <= count - 1))
    for piece, slot, valid in received:
        out = lax.dynamic_update_slice_in_dim(out, piece, jnp.where(valid, slot, place) * rows, 0)
    return lax.dynamic_update_slice_in_dim(out, x, place * rows, 0)


def line_scatter(partial, count):
    place = lax.axis_index("tensor")
    rows = partial.shape[0] // count

    def chunk(index):
        return lax.dynamic_slice_in_dim(partial, jnp.clip(index, 0, count - 1) * rows, rows, 0)

    to_right = None
    to_left = None
    for step in range(1, count):
        send = chunk(place + count - step)
        if to_right is not None:
            send = send + to_right
        to_right = lax.ppermute(
            send.astype(jnp.bfloat16), "tensor", [(i, i + 1) for i in range(step)]
        ).astype(jnp.float32)
        send = chunk(place - count + step)
        if to_left is not None:
            send = send + to_left
        to_left = lax.ppermute(
            send.astype(jnp.bfloat16), "tensor", [(i, i - 1) for i in range(count - step, count)]
        ).astype(jnp.float32)
    total = chunk(place)
    if to_right is not None:
        total = total + to_right + to_left
    return total


def line_all_to_all(x, count, split_axis, concat_axis):
    place = lax.axis_index("tensor")
    size = x.shape[split_axis] // count

    def block(index):
        return lax.dynamic_slice_in_dim(
            x, jnp.clip(index, 0, count - 1) * size, size, split_axis
        )

    own = block(place)
    width = own.shape[concat_axis]
    shape = list(own.shape)
    shape[concat_axis] = width * count
    out = jnp.zeros(shape, x.dtype)
    received = []
    for step in range(1, count):
        from_left = lax.ppermute(
            block(place + step), "tensor", [(i, i + step) for i in range(count - step)]
        )
        from_right = lax.ppermute(
            block(place - step), "tensor", [(i, i - step) for i in range(step, count)]
        )
        received.append((from_left, place - step, place - step >= 0))
        received.append((from_right, place + step, place + step <= count - 1))
    for piece, source, valid in received:
        out = lax.dynamic_update_slice_in_dim(
            out, piece, jnp.where(valid, source, place) * width, concat_axis
        )
    return lax.dynamic_update_slice_in_dim(out, own, place * width, concat_axis)


def per_device(
    tokens,
    cotangent,
    cont_lengths,
    query_weight,
    keyval_weight,
    output_weight,
    gateup_weight,
    down_weight,
    norm_gains,
    query_moment,
    keyval_moment,
    output_moment,
    gateup_moment,
    down_moment,
    gains_moment,
    query_square,
    keyval_square,
    output_square,
    gateup_square,
    down_square,
    gains_square,
):
    masters = (query_weight, keyval_weight, output_weight, gateup_weight, down_weight, norm_gains)
    firsts = (query_moment, keyval_moment, output_moment, gateup_moment, down_moment, gains_moment)
    seconds = (query_square, keyval_square, output_square, gateup_square, down_square, gains_square)
    rounded = tuple((master.astype(jnp.bfloat16) for master in masters))
    gathered = (
        lax.all_gather(
            lax.all_gather(rounded[0], "tensor", axis=1, tiled=True), "dp", axis=0, tiled=True
        ),
        lax.all_gather(
            lax.all_gather(rounded[1], "tensor", axis=1, tiled=True), "dp", axis=0, tiled=True
        ),
        lax.all_gather(
            lax.all_gather(rounded[2], "tensor", axis=0, tiled=True), "dp", axis=1, tiled=True
        ),
        lax.all_gather(rounded[3], "dp", axis=0, tiled=True),
        lax.all_gather(rounded[4], "dp", axis=1, tiled=True),
        lax.all_gather(rounded[5], "dp", axis=1, tiled=True),
    )
    full_query, full_keyval, full_output, full_gateup, full_down, full_gains = gathered
    gain_values = full_gains.astype(jnp.float32)
    tensor_count = lax.axis_size("tensor")
    group_rows = tokens.shape[2] * tensor_count
    block_rows = group_rows // 2
    place = lax.axis_index("tensor")
    rows = tokens.shape[2]
    all_query_heads = full_query.shape[1] // HD
    keyval_heads = full_keyval.shape[1] // tensor_count
    query_heads = all_query_heads // tensor_count
    head_repeat = query_heads // keyval_heads

    def micro_step(token_rows, cot_rows, lengths):
        visible, position = layout(lengths, group_rows)
        cos_table, sin_table = rope_tables(position)
        cos_own, sin_own = rope_tables(lax.dynamic_slice_in_dim(position, place * rows, rows))
        start_rows = token_rows.astype(jnp.float32)
        scale_one = lax.rsqrt(jnp.mean(start_rows * start_rows, axis=1, keepdims=True) + norm_eps)
        hat_one = start_rows * scale_one
        normed_one = (hat_one * gain_values[0][None, :]).astype(jnp.bfloat16)
        query_raw = jnp.dot(normed_one, full_query, preferred_element_type=jnp.float32).reshape(
            rows, all_query_heads, HD
        )
        keyval_raw = jnp.einsum(
            "rd,dhk->rhk", normed_one, full_keyval, preferred_element_type=jnp.float32
        )
        queries_own = rotate(query_raw, cos_own, sin_own).astype(jnp.bfloat16)
        keyval_own = jnp.concatenate(
            [rotate(keyval_raw[:, :, :HD], cos_own, sin_own), keyval_raw[:, :, HD:]], axis=2
        ).astype(jnp.bfloat16)
        queries = line_all_to_all(queries_own, tensor_count, 1, 0).reshape(
            group_rows, keyval_heads, head_repeat, HD
        )
        keyval_rows = line_all_to_all(keyval_own, tensor_count, 1, 0)
        key_rows = keyval_rows[:, :, :HD]
        values = keyval_rows[:, :, HD:]
        mixed_full, log_totals = attend(queries, key_rows, values, visible, block_rows)
        mixed = line_all_to_all(
            mixed_full.astype(jnp.bfloat16).reshape(group_rows, query_heads, HD),
            tensor_count,
            0,
            1,
        ).reshape(rows, all_query_heads * HD)
        attn_branch = jnp.dot(mixed, full_output, preferred_element_type=jnp.float32)
        middle = start_rows + branch_scale * attn_branch
        scale_two = lax.rsqrt(jnp.mean(middle * middle, axis=1, keepdims=True) + norm_eps)
        hat_two = middle * scale_two
        normed_two = (hat_two * gain_values[1][None, :]).astype(jnp.bfloat16)
        rows_two = line_gather(normed_two, tensor_count)
        gate_up = jnp.einsum(
            "rd,dcf->rcf", rows_two, full_gateup, preferred_element_type=jnp.float32
        )
        gate_part = gate_up[:, 0]
        up_part = gate_up[:, 1]
        sigmoid_gate = jax.nn.sigmoid(gate_part)
        silu_gate = gate_part * sigmoid_gate
        hidden_state = (silu_gate * up_part).astype(jnp.bfloat16)
        ffn_branch = line_scatter(
            jnp.dot(hidden_state, full_down, preferred_element_type=jnp.float32), tensor_count
        )
        layer_rows = (middle + branch_scale * ffn_branch).astype(jnp.bfloat16)
        upstream = cot_rows.astype(jnp.float32)
        ffn_grad = (branch_scale * upstream).astype(jnp.bfloat16)
        ffn_grad_all = line_gather(ffn_grad, tensor_count)
        grad_down = contract_rows(hidden_state, ffn_grad_all)
        hidden_grad = contract_cols(ffn_grad_all, full_down)
        gate_grad = hidden_grad * up_part * sigmoid_gate * (1.0 + gate_part * (1.0 - sigmoid_gate))
        up_grad = hidden_grad * silu_gate
        gateup_grad = jnp.stack([gate_grad, up_grad], axis=1).astype(jnp.bfloat16)
        grad_gateup = jnp.einsum(
            "rd,rcf->dcf", rows_two, gateup_grad, preferred_element_type=jnp.float32
        )
        normed_two_grad = line_scatter(
            jnp.einsum(
                "rcf,dcf->rd", gateup_grad, full_gateup, preferred_element_type=jnp.float32
            ),
            tensor_count,
        )
        middle_back, gain_two = norm_back(normed_two_grad, hat_two, scale_two, gain_values[1])
        middle_grad = upstream + middle_back
        attn_grad = (branch_scale * middle_grad).astype(jnp.bfloat16)
        grad_output = contract_rows(mixed, attn_grad)
        mixed_grad = line_all_to_all(
            contract_cols(attn_grad, full_output)
            .astype(jnp.bfloat16)
            .reshape(rows, all_query_heads, HD),
            tensor_count,
            1,
            0,
        ).reshape(group_rows, keyval_heads, head_repeat, HD)
        query_grad, key_grad, value_grad = attend_back(
            queries, key_rows, values, visible, log_totals, mixed_grad, block_rows
        )
        query_raw_grad = line_all_to_all(
            rotate_back(query_grad.reshape(group_rows, query_heads, HD), cos_table, sin_table)
            .astype(jnp.bfloat16),
            tensor_count,
            0,
            1,
        ).reshape(rows, all_query_heads * HD)
        keyval_raw_grad = line_all_to_all(
            jnp.concatenate(
                [rotate_back(key_grad, cos_table, sin_table), value_grad], axis=2
            ).astype(jnp.bfloat16),
            tensor_count,
            0,
            1,
        )
        grad_query = contract_rows(normed_one, query_raw_grad)
        grad_keyval = jnp.einsum(
            "rd,rhk->dhk", normed_one, keyval_raw_grad, preferred_element_type=jnp.float32
        )
        normed_one_grad = contract_cols(query_raw_grad, full_query) + jnp.einsum(
            "rhk,dhk->rd", keyval_raw_grad, full_keyval, preferred_element_type=jnp.float32
        )
        start_back, gain_one = norm_back(normed_one_grad, hat_one, scale_one, gain_values[0])
        input_rows = middle_grad + start_back
        gain_grad = jnp.stack([gain_one, gain_two])
        return (
            layer_rows,
            input_rows,
            (grad_query, grad_keyval, grad_output, grad_gateup, grad_down, gain_grad),
        )

    out_list = []
    grad_list = []
    totals = None
    for step_index in range(tokens.shape[0]):
        layer_rows, input_rows, grads = micro_step(
            tokens[step_index, 0], cotangent[step_index, 0], cont_lengths[step_index, 0]
        )
        out_list.append(layer_rows)
        grad_list.append(input_rows)
        if totals is None:
            totals = grads
        else:
            totals = tuple((old_sum + new_term for old_sum, new_term in zip(totals, grads)))
    layer_output = jnp.stack(out_list)[:, None]
    input_grad = jnp.stack(grad_list)[:, None]
    width = totals[0].shape[0]
    gain_total = lax.psum(totals[5], "tensor")
    summed = (
        lax.psum_scatter(
            lax.psum_scatter(
                totals[0].astype(jnp.bfloat16), "dp", scatter_dimension=0, tiled=True
            ),
            "tensor",
            scatter_dimension=1,
            tiled=True,
        ).astype(jnp.float32),
        lax.psum_scatter(
            lax.psum_scatter(
                totals[1].reshape(width, -1).astype(jnp.bfloat16),
                "dp",
                scatter_dimension=0,
                tiled=True,
            ),
            "tensor",
            scatter_dimension=1,
            tiled=True,
        )
        .astype(jnp.float32)
        .reshape(-1, keyval_heads, totals[1].shape[2]),
        lax.psum_scatter(
            lax.psum_scatter(
                totals[2].astype(jnp.bfloat16), "dp", scatter_dimension=1, tiled=True
            ),
            "tensor",
            scatter_dimension=0,
            tiled=True,
        ).astype(jnp.float32),
        lax.psum_scatter(
            totals[3].reshape(width, -1).astype(jnp.bfloat16), "dp", scatter_dimension=0, tiled=True
        )
        .astype(jnp.float32)
        .reshape(-1, *totals[3].shape[1:]),
        lax.psum_scatter(
            totals[4].astype(jnp.bfloat16), "dp", scatter_dimension=1, tiled=True
        ).astype(jnp.float32),
        lax.psum_scatter(
            gain_total.astype(jnp.bfloat16), "dp", scatter_dimension=1, tiled=True
        ).astype(jnp.float32),
    )
    correction = 1.0 - moment_decay**STEP
    new_firsts = []
    new_seconds = []
    directions = []
    for grad, first, second in zip(summed, firsts, seconds):
        first_new = moment_decay * first + (1.0 - moment_decay) * grad
        second_new = moment_decay * second + (1.0 - moment_decay) * grad * grad
        direction = first_new / correction / (jnp.sqrt(second_new / correction) + ratio_eps)
        new_firsts.append(first_new)
        new_seconds.append(second_new)
        directions.append(direction)
    weight_part = jnp.concatenate(
        [
            jnp.stack([jnp.sum(masters[slot] * masters[slot]) for slot in range(5)]),
            jnp.sum(norm_gains * norm_gains, axis=1) / tensor_count,
        ]
    )
    update_part = jnp.concatenate(
        [
            jnp.stack([jnp.sum(directions[slot] * directions[slot]) for slot in range(5)]),
            jnp.sum(directions[5] * directions[5], axis=1) / tensor_count,
        ]
    )
    square_totals = lax.psum(jnp.stack([weight_part, update_part]), ("dp", "tensor"))
    trust_norms = jnp.sqrt(square_totals)
    ratio = trust_norms[0] / (trust_norms[1] + ratio_eps)
    new_weights = [masters[slot] - learn_rate * ratio[slot] * directions[slot] for slot in range(5)]
    new_gains = norm_gains - learn_rate * ratio[5:7][:, None] * directions[5]
    return (
        layer_output,
        input_grad,
        new_weights[0],
        new_weights[1],
        new_weights[2],
        new_weights[3],
        new_weights[4],
        new_gains,
        new_firsts[0],
        new_firsts[1],
        new_firsts[2],
        new_firsts[3],
        new_firsts[4],
        new_firsts[5],
        new_seconds[0],
        new_seconds[1],
        new_seconds[2],
        new_seconds[3],
        new_seconds[4],
        new_seconds[5],
        trust_norms,
    )


def solution(mesh):
    return jax.shard_map(
        per_device,
        mesh=mesh,
        in_specs=(
            P(None, "dp", "tensor", None),
            P(None, "dp", "tensor", None),
            P(None, "dp", None),
            P("dp", "tensor"),
            P("dp", "tensor", None),
            P("tensor", "dp"),
            P("dp", None, "tensor"),
            P("tensor", "dp"),
            P(None, "dp"),
            P("dp", "tensor"),
            P("dp", "tensor", None),
            P("tensor", "dp"),
            P("dp", None, "tensor"),
            P("tensor", "dp"),
            P(None, "dp"),
            P("dp", "tensor"),
            P("dp", "tensor", None),
            P("tensor", "dp"),
            P("dp", None, "tensor"),
            P("tensor", "dp"),
            P(None, "dp"),
        ),
        out_specs=(
            P(None, "dp", "tensor", None),
            P(None, "dp", "tensor", None),
            P("dp", "tensor"),
            P("dp", "tensor", None),
            P("tensor", "dp"),
            P("dp", None, "tensor"),
            P("tensor", "dp"),
            P(None, "dp"),
            P("dp", "tensor"),
            P("dp", "tensor", None),
            P("tensor", "dp"),
            P("dp", None, "tensor"),
            P("tensor", "dp"),
            P(None, "dp"),
            P("dp", "tensor"),
            P("dp", "tensor", None),
            P("tensor", "dp"),
            P("dp", None, "tensor"),
            P("tensor", "dp"),
            P(None, "dp"),
            P(),
        ),
        check_vma=False,
    )
```

```python
import jax
import jax.numpy as jnp
from jax import lax
from jax.sharding import PartitionSpec as P

HD = 64
PROMPT = 1024
CONTS = 3
STEP = 3


norm_eps = 1e-05
branch_scale = 0.22
score_scale = 0.015625
rope_base = 10000000.0
moment_decay = 0.5
learn_rate = 0.25
ratio_eps = 1e-06
masked_fill = -1e30


def layout(lengths, group_rows):
    row_index = jnp.arange(group_rows, dtype=jnp.int32)
    ends = jnp.cumsum(lengths)
    starts = ends - lengths
    within = row_index - PROMPT
    inside = (within[:, None] >= starts[None, :]) & (within[:, None] < ends[None, :])
    labels = jnp.arange(1, CONTS + 1, dtype=jnp.int32)
    segment = jnp.sum(jnp.where(inside, labels[None, :], 0), axis=1)
    offsets = jnp.sum(jnp.where(inside, starts[None, :], 0), axis=1)
    position = row_index - offsets
    causal = row_index[None, :] <= row_index[:, None]
    shared = (segment[None, :] == segment[:, None]) | (segment[None, :] == 0)
    return (causal & shared, position)


def rope_tables(position):
    half_size = HD // 2
    inverse = rope_base ** (-2.0 * jnp.arange(half_size, dtype=jnp.float32) / HD)
    angle = position.astype(jnp.float32)[:, None] * inverse[None, :]
    return (jnp.cos(angle)[:, None, :], jnp.sin(angle)[:, None, :])


def rotate(field, cos_table, sin_table):
    half_size = field.shape[-1] // 2
    first_half = field[..., :half_size]
    second_half = field[..., half_size:]
    return jnp.concatenate(
        [
            first_half * cos_table - second_half * sin_table,
            second_half * cos_table + first_half * sin_table,
        ],
        axis=-1,
    )


def rotate_back(grad_field, cos_table, sin_table):
    half_size = grad_field.shape[-1] // 2
    first_half = grad_field[..., :half_size]
    second_half = grad_field[..., half_size:]
    return jnp.concatenate(
        [
            first_half * cos_table + second_half * sin_table,
            second_half * cos_table - first_half * sin_table,
        ],
        axis=-1,
    )


def attend(queries, key_rows, values, visible, block_rows):
    outputs = []
    log_totals = []
    for block in range(2):
        begin = block * block_rows
        stop = begin + block_rows
        scores = (
            jnp.einsum(
                "ikrd,jkd->krij",
                queries[begin:stop],
                key_rows[:stop],
                preferred_element_type=jnp.float32,
            )
            * score_scale
        )
        scores = jnp.where(visible[begin:stop, :stop][None, None], scores, masked_fill)
        row_peak = jnp.max(scores, axis=-1, keepdims=True)
        shifted_exp = jnp.exp(scores - row_peak)
        row_total = jnp.sum(shifted_exp, axis=-1, keepdims=True)
        attn_prob = (shifted_exp / row_total).astype(jnp.bfloat16)
        outputs.append(
            jnp.einsum(
                "krij,jkd->ikrd", attn_prob, values[:stop], preferred_element_type=jnp.float32
            )
        )
        log_totals.append(row_peak + jnp.log(row_total))
    return (jnp.concatenate(outputs, axis=0), jnp.concatenate(log_totals, axis=2))


def attend_back(queries, key_rows, values, visible, log_totals, mixed_grad, block_rows):
    query_grads = []
    key_grad = jnp.zeros(key_rows.shape, jnp.float32)
    value_grad = jnp.zeros(values.shape, jnp.float32)
    for block in range(2):
        begin = block * block_rows
        stop = begin + block_rows
        query_block = queries[begin:stop]
        grad_block = mixed_grad[begin:stop]
        scores = (
            jnp.einsum(
                "ikrd,jkd->krij", query_block, key_rows[:stop], preferred_element_type=jnp.float32
            )
            * score_scale
        )
        attn_prob = jnp.where(
            visible[begin:stop, :stop][None, None],
            jnp.exp(scores - log_totals[:, :, begin:stop]),
            0.0,
        )
        prob_grad = jnp.einsum(
            "ikrd,jkd->krij", grad_block, values[:stop], preferred_element_type=jnp.float32
        )
        row_dot = jnp.sum(attn_prob * prob_grad, axis=-1, keepdims=True)
        score_grad = (attn_prob * (prob_grad - row_dot)).astype(jnp.bfloat16)
        query_grads.append(
            jnp.einsum(
                "krij,jkd->ikrd", score_grad, key_rows[:stop], preferred_element_type=jnp.float32
            )
            * score_scale
        )
        key_grad = key_grad.at[:stop].add(
            jnp.einsum(
                "krij,ikrd->jkd", score_grad, query_block, preferred_element_type=jnp.float32
            )
            * score_scale
        )
        value_grad = value_grad.at[:stop].add(
            jnp.einsum(
                "krij,ikrd->jkd",
                attn_prob.astype(jnp.bfloat16),
                grad_block,
                preferred_element_type=jnp.float32,
            )
        )
    return (jnp.concatenate(query_grads, axis=0), key_grad, value_grad)


def norm_back(upstream, normed_hat, scale_rows, gain_row):
    scaled = upstream * gain_row[None, :]
    through = scale_rows * (
        scaled - normed_hat * jnp.mean(scaled * normed_hat, axis=1, keepdims=True)
    )
    return (through, jnp.sum(upstream * normed_hat, axis=0))


def contract_rows(left, right):
    return lax.dot_general(
        left, right, (((0,), (0,)), ((), ())), preferred_element_type=jnp.float32
    )


def contract_cols(left, right):
    return lax.dot_general(
        left, right, (((1,), (1,)), ((), ())), preferred_element_type=jnp.float32
    )


def line_gather(x, count):
    place = lax.axis_index("tensor")
    rows = x.shape[0]
    out = jnp.zeros((count * rows,) + x.shape[1:], x.dtype)
    from_left = x
    from_right = x
    received = []
    for step in range(1, count):
        from_left = lax.ppermute(
            from_left, "tensor", [(i, i + 1) for i in range(step - 1, count - 1)]
        )
        from_right = lax.ppermute(
            from_right, "tensor", [(i, i - 1) for i in range(1, count - step + 1)]
        )
        received.append((from_left, place - step, place - step >= 0))
        received.append((from_right, place + step, place + step <= count - 1))
    for piece, slot, valid in received:
        out = lax.dynamic_update_slice_in_dim(out, piece, jnp.where(valid, slot, place) * rows, 0)
    return lax.dynamic_update_slice_in_dim(out, x, place * rows, 0)


def line_scatter(partial, count):
    place = lax.axis_index("tensor")
    rows = partial.shape[0] // count

    def chunk(index):
        return lax.dynamic_slice_in_dim(partial, jnp.clip(index, 0, count - 1) * rows, rows, 0)

    to_right = None
    to_left = None
    for step in range(1, count):
        send = chunk(place + count - step)
        if to_right is not None:
            send = send + to_right
        to_right = lax.ppermute(
            send.astype(jnp.bfloat16), "tensor", [(i, i + 1) for i in range(step)]
        ).astype(jnp.float32)
        send = chunk(place - count + step)
        if to_left is not None:
            send = send + to_left
        to_left = lax.ppermute(
            send.astype(jnp.bfloat16), "tensor", [(i, i - 1) for i in range(count - step, count)]
        ).astype(jnp.float32)
    total = chunk(place)
    if to_right is not None:
        total = total + to_right + to_left
    return total


def line_all_to_all(x, count, split_axis, concat_axis):
    return lax.all_to_all(x, "tensor", split_axis, concat_axis, tiled=True)


def shifted_all_to_all(x, count, split_axis, concat_axis):
    place = lax.axis_index("tensor")
    size = x.shape[split_axis] // count

    def block(index):
        return lax.dynamic_slice_in_dim(
            x, jnp.clip(index, 0, count - 1) * size, size, split_axis
        )

    own = block(place)
    width = own.shape[concat_axis]
    shape = list(own.shape)
    shape[concat_axis] = width * count
    out = jnp.zeros(shape, x.dtype)
    received = []
    for step in range(1, count):
        from_left = lax.ppermute(
            block(place + step), "tensor", [(i, i + step) for i in range(count - step)]
        )
        from_right = lax.ppermute(
            block(place - step), "tensor", [(i, i - step) for i in range(step, count)]
        )
        received.append((from_left, place - step, place - step >= 0))
        received.append((from_right, place + step, place + step <= count - 1))
    for piece, source, valid in received:
        out = lax.dynamic_update_slice_in_dim(
            out, piece, jnp.where(valid, source, place) * width, concat_axis
        )
    return lax.dynamic_update_slice_in_dim(out, own, place * width, concat_axis)


def per_device(
    tokens,
    cotangent,
    cont_lengths,
    query_weight,
    keyval_weight,
    output_weight,
    gateup_weight,
    down_weight,
    norm_gains,
    query_moment,
    keyval_moment,
    output_moment,
    gateup_moment,
    down_moment,
    gains_moment,
    query_square,
    keyval_square,
    output_square,
    gateup_square,
    down_square,
    gains_square,
):
    masters = (query_weight, keyval_weight, output_weight, gateup_weight, down_weight, norm_gains)
    firsts = (query_moment, keyval_moment, output_moment, gateup_moment, down_moment, gains_moment)
    seconds = (query_square, keyval_square, output_square, gateup_square, down_square, gains_square)
    rounded = tuple((master.astype(jnp.bfloat16) for master in masters))
    gathered = (
        lax.all_gather(
            lax.all_gather(rounded[0], "tensor", axis=1, tiled=True), "dp", axis=0, tiled=True
        ),
        lax.all_gather(
            lax.all_gather(rounded[1], "tensor", axis=1, tiled=True), "dp", axis=0, tiled=True
        ),
        lax.all_gather(
            lax.all_gather(rounded[2], "tensor", axis=0, tiled=True), "dp", axis=1, tiled=True
        ),
        lax.all_gather(rounded[3], "dp", axis=0, tiled=True),
        lax.all_gather(rounded[4], "dp", axis=1, tiled=True),
        lax.all_gather(rounded[5], "dp", axis=1, tiled=True),
    )
    full_query, full_keyval, full_output, full_gateup, full_down, full_gains = gathered
    gain_values = full_gains.astype(jnp.float32)
    tensor_count = lax.axis_size("tensor")
    group_rows = tokens.shape[2] * tensor_count
    block_rows = group_rows // 2
    place = lax.axis_index("tensor")
    rows = tokens.shape[2]
    all_query_heads = full_query.shape[1] // HD
    keyval_heads = full_keyval.shape[1] // tensor_count
    query_heads = all_query_heads // tensor_count
    head_repeat = query_heads // keyval_heads

    def micro_step(token_rows, cot_rows, lengths):
        visible, position = layout(lengths, group_rows)
        cos_table, sin_table = rope_tables(position)
        cos_own, sin_own = rope_tables(lax.dynamic_slice_in_dim(position, place * rows, rows))
        start_rows = token_rows.astype(jnp.float32)
        scale_one = lax.rsqrt(jnp.mean(start_rows * start_rows, axis=1, keepdims=True) + norm_eps)
        hat_one = start_rows * scale_one
        normed_one = (hat_one * gain_values[0][None, :]).astype(jnp.bfloat16)
        query_raw = jnp.dot(normed_one, full_query, preferred_element_type=jnp.float32).reshape(
            rows, all_query_heads, HD
        )
        keyval_raw = jnp.einsum(
            "rd,dhk->rhk", normed_one, full_keyval, preferred_element_type=jnp.float32
        )
        queries_own = rotate(query_raw, cos_own, sin_own).astype(jnp.bfloat16)
        keyval_own = jnp.concatenate(
            [rotate(keyval_raw[:, :, :HD], cos_own, sin_own), keyval_raw[:, :, HD:]], axis=2
        ).astype(jnp.bfloat16)
        queries = line_all_to_all(queries_own, tensor_count, 1, 0).reshape(
            group_rows, keyval_heads, head_repeat, HD
        )
        keyval_rows = line_all_to_all(keyval_own, tensor_count, 1, 0)
        key_rows = keyval_rows[:, :, :HD]
        values = keyval_rows[:, :, HD:]
        mixed_full, log_totals = attend(queries, key_rows, values, visible, block_rows)
        mixed = line_all_to_all(
            mixed_full.astype(jnp.bfloat16).reshape(group_rows, query_heads, HD),
            tensor_count,
            0,
            1,
        ).reshape(rows, all_query_heads * HD)
        attn_branch = jnp.dot(mixed, full_output, preferred_element_type=jnp.float32)
        middle = start_rows + branch_scale * attn_branch
        scale_two = lax.rsqrt(jnp.mean(middle * middle, axis=1, keepdims=True) + norm_eps)
        hat_two = middle * scale_two
        normed_two = (hat_two * gain_values[1][None, :]).astype(jnp.bfloat16)
        rows_two = line_gather(normed_two, tensor_count)
        gate_up = jnp.einsum(
            "rd,dcf->rcf", rows_two, full_gateup, preferred_element_type=jnp.float32
        )
        gate_part = gate_up[:, 0]
        up_part = gate_up[:, 1]
        sigmoid_gate = jax.nn.sigmoid(gate_part)
        silu_gate = gate_part * sigmoid_gate
        hidden_state = (silu_gate * up_part).astype(jnp.bfloat16)
        ffn_branch = line_scatter(
            jnp.dot(hidden_state, full_down, preferred_element_type=jnp.float32), tensor_count
        )
        layer_rows = (middle + branch_scale * ffn_branch).astype(jnp.bfloat16)
        upstream = cot_rows.astype(jnp.float32)
        ffn_grad = (branch_scale * upstream).astype(jnp.bfloat16)
        ffn_grad_all = line_gather(ffn_grad, tensor_count)
        grad_down = contract_rows(hidden_state, ffn_grad_all)
        hidden_grad = contract_cols(ffn_grad_all, full_down)
        gate_grad = hidden_grad * up_part * sigmoid_gate * (1.0 + gate_part * (1.0 - sigmoid_gate))
        up_grad = hidden_grad * silu_gate
        gateup_grad = jnp.stack([gate_grad, up_grad], axis=1).astype(jnp.bfloat16)
        grad_gateup = jnp.einsum(
            "rd,rcf->dcf", rows_two, gateup_grad, preferred_element_type=jnp.float32
        )
        normed_two_grad = line_scatter(
            jnp.einsum(
                "rcf,dcf->rd", gateup_grad, full_gateup, preferred_element_type=jnp.float32
            ),
            tensor_count,
        )
        middle_back, gain_two = norm_back(normed_two_grad, hat_two, scale_two, gain_values[1])
        middle_grad = upstream + middle_back
        attn_grad = (branch_scale * middle_grad).astype(jnp.bfloat16)
        grad_output = contract_rows(mixed, attn_grad)
        mixed_grad = line_all_to_all(
            contract_cols(attn_grad, full_output)
            .astype(jnp.bfloat16)
            .reshape(rows, all_query_heads, HD),
            tensor_count,
            1,
            0,
        ).reshape(group_rows, keyval_heads, head_repeat, HD)
        query_grad, key_grad, value_grad = attend_back(
            queries, key_rows, values, visible, log_totals, mixed_grad, block_rows
        )
        query_raw_grad = line_all_to_all(
            rotate_back(query_grad.reshape(group_rows, query_heads, HD), cos_table, sin_table)
            .astype(jnp.bfloat16),
            tensor_count,
            0,
            1,
        ).reshape(rows, all_query_heads * HD)
        keyval_raw_grad = line_all_to_all(
            jnp.concatenate(
                [rotate_back(key_grad, cos_table, sin_table), value_grad], axis=2
            ).astype(jnp.bfloat16),
            tensor_count,
            0,
            1,
        )
        grad_query = contract_rows(normed_one, query_raw_grad)
        grad_keyval = jnp.einsum(
            "rd,rhk->dhk", normed_one, keyval_raw_grad, preferred_element_type=jnp.float32
        )
        normed_one_grad = contract_cols(query_raw_grad, full_query) + jnp.einsum(
            "rhk,dhk->rd", keyval_raw_grad, full_keyval, preferred_element_type=jnp.float32
        )
        start_back, gain_one = norm_back(normed_one_grad, hat_one, scale_one, gain_values[0])
        input_rows = middle_grad + start_back
        gain_grad = jnp.stack([gain_one, gain_two])
        return (
            layer_rows,
            input_rows,
            (grad_query, grad_keyval, grad_output, grad_gateup, grad_down, gain_grad),
        )

    out_list = []
    grad_list = []
    totals = None
    for step_index in range(tokens.shape[0]):
        layer_rows, input_rows, grads = micro_step(
            tokens[step_index, 0], cotangent[step_index, 0], cont_lengths[step_index, 0]
        )
        out_list.append(layer_rows)
        grad_list.append(input_rows)
        if totals is None:
            totals = grads
        else:
            totals = tuple((old_sum + new_term for old_sum, new_term in zip(totals, grads)))
    layer_output = jnp.stack(out_list)[:, None]
    input_grad = jnp.stack(grad_list)[:, None]
    width = totals[0].shape[0]
    gain_total = lax.psum(totals[5], "tensor")
    summed = (
        lax.psum_scatter(
            lax.psum_scatter(
                totals[0].astype(jnp.bfloat16), "dp", scatter_dimension=0, tiled=True
            ),
            "tensor",
            scatter_dimension=1,
            tiled=True,
        ).astype(jnp.float32),
        lax.psum_scatter(
            lax.psum_scatter(
                totals[1].reshape(width, -1).astype(jnp.bfloat16),
                "dp",
                scatter_dimension=0,
                tiled=True,
            ),
            "tensor",
            scatter_dimension=1,
            tiled=True,
        )
        .astype(jnp.float32)
        .reshape(-1, keyval_heads, totals[1].shape[2]),
        lax.psum_scatter(
            lax.psum_scatter(
                totals[2].astype(jnp.bfloat16), "dp", scatter_dimension=1, tiled=True
            ),
            "tensor",
            scatter_dimension=0,
            tiled=True,
        ).astype(jnp.float32),
        lax.psum_scatter(
            totals[3].reshape(width, -1).astype(jnp.bfloat16), "dp", scatter_dimension=0, tiled=True
        )
        .astype(jnp.float32)
        .reshape(-1, *totals[3].shape[1:]),
        lax.psum_scatter(
            totals[4].astype(jnp.bfloat16), "dp", scatter_dimension=1, tiled=True
        ).astype(jnp.float32),
        lax.psum_scatter(
            gain_total.astype(jnp.bfloat16), "dp", scatter_dimension=1, tiled=True
        ).astype(jnp.float32),
    )
    correction = 1.0 - moment_decay**STEP
    new_firsts = []
    new_seconds = []
    directions = []
    for grad, first, second in zip(summed, firsts, seconds):
        first_new = moment_decay * first + (1.0 - moment_decay) * grad
        second_new = moment_decay * second + (1.0 - moment_decay) * grad * grad
        direction = first_new / correction / (jnp.sqrt(second_new / correction) + ratio_eps)
        new_firsts.append(first_new)
        new_seconds.append(second_new)
        directions.append(direction)
    weight_part = jnp.concatenate(
        [
            jnp.stack([jnp.sum(masters[slot] * masters[slot]) for slot in range(5)]),
            jnp.sum(norm_gains * norm_gains, axis=1) / tensor_count,
        ]
    )
    update_part = jnp.concatenate(
        [
            jnp.stack([jnp.sum(directions[slot] * directions[slot]) for slot in range(5)]),
            jnp.sum(directions[5] * directions[5], axis=1) / tensor_count,
        ]
    )
    square_totals = lax.psum(jnp.stack([weight_part, update_part]), ("dp", "tensor"))
    trust_norms = jnp.sqrt(square_totals)
    ratio = trust_norms[0] / (trust_norms[1] + ratio_eps)
    new_weights = [masters[slot] - learn_rate * ratio[slot] * directions[slot] for slot in range(5)]
    new_gains = norm_gains - learn_rate * ratio[5:7][:, None] * directions[5]
    return (
        layer_output,
        input_grad,
        new_weights[0],
        new_weights[1],
        new_weights[2],
        new_weights[3],
        new_weights[4],
        new_gains,
        new_firsts[0],
        new_firsts[1],
        new_firsts[2],
        new_firsts[3],
        new_firsts[4],
        new_firsts[5],
        new_seconds[0],
        new_seconds[1],
        new_seconds[2],
        new_seconds[3],
        new_seconds[4],
        new_seconds[5],
        trust_norms,
    )


def solution(mesh):
    return jax.shard_map(
        per_device,
        mesh=mesh,
        in_specs=(
            P(None, "dp", "tensor", None),
            P(None, "dp", "tensor", None),
            P(None, "dp", None),
            P("dp", "tensor"),
            P("dp", "tensor", None),
            P("tensor", "dp"),
            P("dp", None, "tensor"),
            P("tensor", "dp"),
            P(None, "dp"),
            P("dp", "tensor"),
            P("dp", "tensor", None),
            P("tensor", "dp"),
            P("dp", None, "tensor"),
            P("tensor", "dp"),
            P(None, "dp"),
            P("dp", "tensor"),
            P("dp", "tensor", None),
            P("tensor", "dp"),
            P("dp", None, "tensor"),
            P("tensor", "dp"),
            P(None, "dp"),
        ),
        out_specs=(
            P(None, "dp", "tensor", None),
            P(None, "dp", "tensor", None),
            P("dp", "tensor"),
            P("dp", "tensor", None),
            P("tensor", "dp"),
            P("dp", None, "tensor"),
            P("tensor", "dp"),
            P(None, "dp"),
            P("dp", "tensor"),
            P("dp", "tensor", None),
            P("tensor", "dp"),
            P("dp", None, "tensor"),
            P("tensor", "dp"),
            P(None, "dp"),
            P("dp", "tensor"),
            P("dp", "tensor", None),
            P("tensor", "dp"),
            P("dp", None, "tensor"),
            P("tensor", "dp"),
            P(None, "dp"),
            P(),
        ),
        check_vma=False,
    )
```

```python
import jax
import jax.numpy as jnp
from jax import lax
from jax.sharding import PartitionSpec as P

HD = 64
PROMPT = 1024
CONTS = 3
STEP = 3


norm_eps = 1e-05
branch_scale = 0.22
score_scale = 0.015625
rope_base = 10000000.0
moment_decay = 0.5
learn_rate = 0.25
ratio_eps = 1e-06
masked_fill = -1e30


def layout(lengths, group_rows):
    row_index = jnp.arange(group_rows, dtype=jnp.int32)
    ends = jnp.cumsum(lengths)
    starts = ends - lengths
    within = row_index - PROMPT
    inside = (within[:, None] >= starts[None, :]) & (within[:, None] < ends[None, :])
    labels = jnp.arange(1, CONTS + 1, dtype=jnp.int32)
    segment = jnp.sum(jnp.where(inside, labels[None, :], 0), axis=1)
    offsets = jnp.sum(jnp.where(inside, starts[None, :], 0), axis=1)
    position = row_index - offsets
    causal = row_index[None, :] <= row_index[:, None]
    shared = (segment[None, :] == segment[:, None]) | (segment[None, :] == 0)
    return (causal & shared, position)


def rope_tables(position):
    half_size = HD // 2
    inverse = rope_base ** (-2.0 * jnp.arange(half_size, dtype=jnp.float32) / HD)
    angle = position.astype(jnp.float32)[:, None] * inverse[None, :]
    return (jnp.cos(angle)[:, None, :], jnp.sin(angle)[:, None, :])


def rotate(field, cos_table, sin_table):
    half_size = field.shape[-1] // 2
    first_half = field[..., :half_size]
    second_half = field[..., half_size:]
    return jnp.concatenate(
        [
            first_half * cos_table - second_half * sin_table,
            second_half * cos_table + first_half * sin_table,
        ],
        axis=-1,
    )


def rotate_back(grad_field, cos_table, sin_table):
    half_size = grad_field.shape[-1] // 2
    first_half = grad_field[..., :half_size]
    second_half = grad_field[..., half_size:]
    return jnp.concatenate(
        [
            first_half * cos_table + second_half * sin_table,
            second_half * cos_table - first_half * sin_table,
        ],
        axis=-1,
    )


def attend(queries, key_rows, values, visible, block_rows):
    outputs = []
    log_totals = []
    for block in range(2):
        begin = block * block_rows
        stop = begin + block_rows
        scores = (
            jnp.einsum(
                "ikrd,jkd->krij",
                queries[begin:stop],
                key_rows[:stop],
                preferred_element_type=jnp.float32,
            )
            * score_scale
        )
        scores = jnp.where(visible[begin:stop, :stop][None, None], scores, masked_fill)
        row_peak = jnp.max(scores, axis=-1, keepdims=True)
        shifted_exp = jnp.exp(scores - row_peak)
        row_total = jnp.sum(shifted_exp, axis=-1, keepdims=True)
        attn_prob = (shifted_exp / row_total).astype(jnp.bfloat16)
        outputs.append(
            jnp.einsum(
                "krij,jkd->ikrd", attn_prob, values[:stop], preferred_element_type=jnp.float32
            )
        )
        log_totals.append(row_peak + jnp.log(row_total))
    return (jnp.concatenate(outputs, axis=0), jnp.concatenate(log_totals, axis=2))


def attend_back(queries, key_rows, values, visible, log_totals, mixed_grad, block_rows):
    query_grads = []
    key_grad = jnp.zeros(key_rows.shape, jnp.float32)
    value_grad = jnp.zeros(values.shape, jnp.float32)
    for block in range(2):
        begin = block * block_rows
        stop = begin + block_rows
        query_block = queries[begin:stop]
        grad_block = mixed_grad[begin:stop]
        scores = (
            jnp.einsum(
                "ikrd,jkd->krij", query_block, key_rows[:stop], preferred_element_type=jnp.float32
            )
            * score_scale
        )
        attn_prob = jnp.where(
            visible[begin:stop, :stop][None, None],
            jnp.exp(scores - log_totals[:, :, begin:stop]),
            0.0,
        )
        prob_grad = jnp.einsum(
            "ikrd,jkd->krij", grad_block, values[:stop], preferred_element_type=jnp.float32
        )
        row_dot = jnp.sum(attn_prob * prob_grad, axis=-1, keepdims=True)
        score_grad = (attn_prob * (prob_grad - row_dot)).astype(jnp.bfloat16)
        query_grads.append(
            jnp.einsum(
                "krij,jkd->ikrd", score_grad, key_rows[:stop], preferred_element_type=jnp.float32
            )
            * score_scale
        )
        key_grad = key_grad.at[:stop].add(
            jnp.einsum(
                "krij,ikrd->jkd", score_grad, query_block, preferred_element_type=jnp.float32
            )
            * score_scale
        )
        value_grad = value_grad.at[:stop].add(
            jnp.einsum(
                "krij,ikrd->jkd",
                attn_prob.astype(jnp.bfloat16),
                grad_block,
                preferred_element_type=jnp.float32,
            )
        )
    return (jnp.concatenate(query_grads, axis=0), key_grad, value_grad)


def norm_back(upstream, normed_hat, scale_rows, gain_row):
    scaled = upstream * gain_row[None, :]
    through = scale_rows * (
        scaled - normed_hat * jnp.mean(scaled * normed_hat, axis=1, keepdims=True)
    )
    return (through, jnp.sum(upstream * normed_hat, axis=0))


def contract_rows(left, right):
    return lax.dot_general(
        left, right, (((0,), (0,)), ((), ())), preferred_element_type=jnp.float32
    )


def contract_cols(left, right):
    return lax.dot_general(
        left, right, (((1,), (1,)), ((), ())), preferred_element_type=jnp.float32
    )


def line_gather(x, count):
    place = lax.axis_index("tensor")
    rows = x.shape[0]
    out = jnp.zeros((count * rows,) + x.shape[1:], x.dtype)
    from_left = x
    from_right = x
    received = []
    for step in range(1, count):
        from_left = lax.ppermute(
            from_left, "tensor", [(i, i + 1) for i in range(step - 1, count - 1)]
        )
        from_right = lax.ppermute(
            from_right, "tensor", [(i, i - 1) for i in range(1, count - step + 1)]
        )
        received.append((from_left, place - step, place - step >= 0))
        received.append((from_right, place + step, place + step <= count - 1))
    for piece, slot, valid in received:
        out = lax.dynamic_update_slice_in_dim(out, piece, jnp.where(valid, slot, place) * rows, 0)
    return lax.dynamic_update_slice_in_dim(out, x, place * rows, 0)


def line_scatter(partial, count):
    place = lax.axis_index("tensor")
    rows = partial.shape[0] // count

    def chunk(index):
        return lax.dynamic_slice_in_dim(partial, jnp.clip(index, 0, count - 1) * rows, rows, 0)

    to_right = None
    to_left = None
    for step in range(1, count):
        send = chunk(place + count - step)
        if to_right is not None:
            send = send + to_right
        to_right = lax.ppermute(
            send.astype(jnp.bfloat16), "tensor", [(i, i + 1) for i in range(step)]
        ).astype(jnp.float32)
        send = chunk(place - count + step)
        if to_left is not None:
            send = send + to_left
        to_left = lax.ppermute(
            send.astype(jnp.bfloat16), "tensor", [(i, i - 1) for i in range(count - step, count)]
        ).astype(jnp.float32)
    total = chunk(place)
    if to_right is not None:
        total = total + to_right + to_left
    return total


def per_device(
    tokens,
    cotangent,
    cont_lengths,
    query_weight,
    keyval_weight,
    output_weight,
    gateup_weight,
    down_weight,
    norm_gains,
    query_moment,
    keyval_moment,
    output_moment,
    gateup_moment,
    down_moment,
    gains_moment,
    query_square,
    keyval_square,
    output_square,
    gateup_square,
    down_square,
    gains_square,
):
    masters = (query_weight, keyval_weight, output_weight, gateup_weight, down_weight, norm_gains)
    firsts = (query_moment, keyval_moment, output_moment, gateup_moment, down_moment, gains_moment)
    seconds = (query_square, keyval_square, output_square, gateup_square, down_square, gains_square)
    rounded = tuple((master.astype(jnp.bfloat16) for master in masters))
    gathered = (
        lax.all_gather(rounded[0], "dp", axis=0, tiled=True),
        lax.all_gather(rounded[1], "dp", axis=0, tiled=True),
        lax.all_gather(rounded[2], "dp", axis=1, tiled=True),
        lax.all_gather(rounded[3], "dp", axis=0, tiled=True),
        lax.all_gather(rounded[4], "dp", axis=1, tiled=True),
        lax.all_gather(rounded[5], "dp", axis=1, tiled=True),
    )
    full_query, full_keyval, full_output, full_gateup, full_down, full_gains = gathered
    gain_values = full_gains.astype(jnp.float32)
    tensor_count = lax.axis_size("tensor")
    group_rows = tokens.shape[2] * tensor_count
    block_rows = group_rows // 2
    keyval_heads = full_keyval.shape[1]
    query_heads = full_query.shape[1] // HD
    head_repeat = query_heads // keyval_heads

    def micro_step(token_rows, cot_rows, lengths):
        visible, position = layout(lengths, group_rows)
        cos_table, sin_table = rope_tables(position)
        start_rows = token_rows.astype(jnp.float32)
        scale_one = lax.rsqrt(jnp.mean(start_rows * start_rows, axis=1, keepdims=True) + norm_eps)
        hat_one = start_rows * scale_one
        normed_one = (hat_one * gain_values[0][None, :]).astype(jnp.bfloat16)
        rows_one = line_gather(normed_one, tensor_count)
        query_raw = jnp.dot(rows_one, full_query, preferred_element_type=jnp.float32).reshape(
            group_rows, query_heads, HD
        )
        keyval_raw = jnp.einsum(
            "rd,dhk->rhk", rows_one, full_keyval, preferred_element_type=jnp.float32
        )
        queries = (
            rotate(query_raw, cos_table, sin_table)
            .astype(jnp.bfloat16)
            .reshape(group_rows, keyval_heads, head_repeat, HD)
        )
        key_rows = rotate(keyval_raw[:, :, :HD], cos_table, sin_table).astype(jnp.bfloat16)
        values = keyval_raw[:, :, HD:].astype(jnp.bfloat16)
        mixed_full, log_totals = attend(queries, key_rows, values, visible, block_rows)
        mixed = mixed_full.astype(jnp.bfloat16).reshape(group_rows, query_heads * HD)
        attn_branch = line_scatter(
            jnp.dot(mixed, full_output, preferred_element_type=jnp.float32), tensor_count
        )
        middle = start_rows + branch_scale * attn_branch
        scale_two = lax.rsqrt(jnp.mean(middle * middle, axis=1, keepdims=True) + norm_eps)
        hat_two = middle * scale_two
        normed_two = (hat_two * gain_values[1][None, :]).astype(jnp.bfloat16)
        rows_two = line_gather(normed_two, tensor_count)
        gate_up = jnp.einsum(
            "rd,dcf->rcf", rows_two, full_gateup, preferred_element_type=jnp.float32
        )
        gate_part = gate_up[:, 0]
        up_part = gate_up[:, 1]
        sigmoid_gate = jax.nn.sigmoid(gate_part)
        silu_gate = gate_part * sigmoid_gate
        hidden_state = (silu_gate * up_part).astype(jnp.bfloat16)
        ffn_branch = lax.psum_scatter(
            jnp.dot(hidden_state, full_down, preferred_element_type=jnp.float32).astype(
                jnp.bfloat16
            ),
            "tensor",
            scatter_dimension=0,
            tiled=True,
        ).astype(jnp.float32)
        layer_rows = (middle + branch_scale * ffn_branch).astype(jnp.bfloat16)
        upstream = cot_rows.astype(jnp.float32)
        ffn_grad = (branch_scale * upstream).astype(jnp.bfloat16)
        ffn_grad_all = lax.all_gather(ffn_grad, "tensor", axis=0, tiled=True)
        grad_down = contract_rows(hidden_state, ffn_grad_all)
        hidden_grad = contract_cols(ffn_grad_all, full_down)
        gate_grad = hidden_grad * up_part * sigmoid_gate * (1.0 + gate_part * (1.0 - sigmoid_gate))
        up_grad = hidden_grad * silu_gate
        gateup_grad = jnp.stack([gate_grad, up_grad], axis=1).astype(jnp.bfloat16)
        grad_gateup = jnp.einsum(
            "rd,rcf->dcf", rows_two, gateup_grad, preferred_element_type=jnp.float32
        )
        normed_two_grad = line_scatter(
            jnp.einsum(
                "rcf,dcf->rd", gateup_grad, full_gateup, preferred_element_type=jnp.float32
            ),
            tensor_count,
        )
        middle_back, gain_two = norm_back(normed_two_grad, hat_two, scale_two, gain_values[1])
        middle_grad = upstream + middle_back
        attn_grad = (branch_scale * middle_grad).astype(jnp.bfloat16)
        attn_grad_all = line_gather(attn_grad, tensor_count)
        grad_output = contract_rows(mixed, attn_grad_all)
        mixed_grad = (
            contract_cols(attn_grad_all, full_output)
            .astype(jnp.bfloat16)
            .reshape(group_rows, keyval_heads, head_repeat, HD)
        )
        query_grad, key_grad, value_grad = attend_back(
            queries, key_rows, values, visible, log_totals, mixed_grad, block_rows
        )
        query_raw_grad = (
            rotate_back(query_grad.reshape(group_rows, query_heads, HD), cos_table, sin_table)
            .astype(jnp.bfloat16)
            .reshape(group_rows, query_heads * HD)
        )
        keyval_raw_grad = jnp.concatenate(
            [rotate_back(key_grad, cos_table, sin_table), value_grad], axis=2
        ).astype(jnp.bfloat16)
        grad_query = contract_rows(rows_one, query_raw_grad)
        grad_keyval = jnp.einsum(
            "rd,rhk->dhk", rows_one, keyval_raw_grad, preferred_element_type=jnp.float32
        )
        normed_one_grad = line_scatter(
            contract_cols(query_raw_grad, full_query)
            + jnp.einsum(
                "rhk,dhk->rd", keyval_raw_grad, full_keyval, preferred_element_type=jnp.float32
            ),
            tensor_count,
        )
        start_back, gain_one = norm_back(normed_one_grad, hat_one, scale_one, gain_values[0])
        input_rows = middle_grad + start_back
        gain_grad = jnp.stack([gain_one, gain_two])
        return (
            layer_rows,
            input_rows,
            (grad_query, grad_keyval, grad_output, grad_gateup, grad_down, gain_grad),
        )

    out_list = []
    grad_list = []
    totals = None
    for step_index in range(tokens.shape[0]):
        layer_rows, input_rows, grads = micro_step(
            tokens[step_index, 0], cotangent[step_index, 0], cont_lengths[step_index, 0]
        )
        out_list.append(layer_rows)
        grad_list.append(input_rows)
        if totals is None:
            totals = grads
        else:
            totals = tuple((old_sum + new_term for old_sum, new_term in zip(totals, grads)))
    layer_output = jnp.stack(out_list)[:, None]
    input_grad = jnp.stack(grad_list)[:, None]
    width = totals[0].shape[0]
    gain_total = lax.psum(totals[5], "tensor")
    summed = (
        lax.psum_scatter(
            totals[0].astype(jnp.bfloat16), "dp", scatter_dimension=0, tiled=True
        ).astype(jnp.float32),
        lax.psum_scatter(
            totals[1].reshape(width, -1).astype(jnp.bfloat16), "dp", scatter_dimension=0, tiled=True
        )
        .astype(jnp.float32)
        .reshape(-1, *totals[1].shape[1:]),
        lax.psum_scatter(
            totals[2].astype(jnp.bfloat16), "dp", scatter_dimension=1, tiled=True
        ).astype(jnp.float32),
        lax.psum_scatter(
            totals[3].reshape(width, -1).astype(jnp.bfloat16), "dp", scatter_dimension=0, tiled=True
        )
        .astype(jnp.float32)
        .reshape(-1, *totals[3].shape[1:]),
        lax.psum_scatter(
            totals[4].astype(jnp.bfloat16), "dp", scatter_dimension=1, tiled=True
        ).astype(jnp.float32),
        lax.psum_scatter(
            gain_total.astype(jnp.bfloat16), "dp", scatter_dimension=1, tiled=True
        ).astype(jnp.float32),
    )
    correction = 1.0 - moment_decay**STEP
    new_firsts = []
    new_seconds = []
    directions = []
    for grad, first, second in zip(summed, firsts, seconds):
        first_new = moment_decay * first + (1.0 - moment_decay) * grad
        second_new = moment_decay * second + (1.0 - moment_decay) * grad * grad
        direction = first_new / correction / (jnp.sqrt(second_new / correction) + ratio_eps)
        new_firsts.append(first_new)
        new_seconds.append(second_new)
        directions.append(direction)
    weight_part = jnp.concatenate(
        [
            jnp.stack([jnp.sum(masters[slot] * masters[slot]) for slot in range(5)]),
            jnp.sum(norm_gains * norm_gains, axis=1) / tensor_count,
        ]
    )
    update_part = jnp.concatenate(
        [
            jnp.stack([jnp.sum(directions[slot] * directions[slot]) for slot in range(5)]),
            jnp.sum(directions[5] * directions[5], axis=1) / tensor_count,
        ]
    )
    square_totals = lax.psum(jnp.stack([weight_part, update_part]), ("dp", "tensor"))
    trust_norms = jnp.sqrt(square_totals)
    ratio = trust_norms[0] / (trust_norms[1] + ratio_eps)
    new_weights = [masters[slot] - learn_rate * ratio[slot] * directions[slot] for slot in range(5)]
    new_gains = norm_gains - learn_rate * ratio[5:7][:, None] * directions[5]
    return (
        layer_output,
        input_grad,
        new_weights[0],
        new_weights[1],
        new_weights[2],
        new_weights[3],
        new_weights[4],
        new_gains,
        new_firsts[0],
        new_firsts[1],
        new_firsts[2],
        new_firsts[3],
        new_firsts[4],
        new_firsts[5],
        new_seconds[0],
        new_seconds[1],
        new_seconds[2],
        new_seconds[3],
        new_seconds[4],
        new_seconds[5],
        trust_norms,
    )


def solution(mesh):
    return jax.shard_map(
        per_device,
        mesh=mesh,
        in_specs=(
            P(None, "dp", "tensor", None),
            P(None, "dp", "tensor", None),
            P(None, "dp", None),
            P("dp", "tensor"),
            P("dp", "tensor", None),
            P("tensor", "dp"),
            P("dp", None, "tensor"),
            P("tensor", "dp"),
            P(None, "dp"),
            P("dp", "tensor"),
            P("dp", "tensor", None),
            P("tensor", "dp"),
            P("dp", None, "tensor"),
            P("tensor", "dp"),
            P(None, "dp"),
            P("dp", "tensor"),
            P("dp", "tensor", None),
            P("tensor", "dp"),
            P("dp", None, "tensor"),
            P("tensor", "dp"),
            P(None, "dp"),
        ),
        out_specs=(
            P(None, "dp", "tensor", None),
            P(None, "dp", "tensor", None),
            P("dp", "tensor"),
            P("dp", "tensor", None),
            P("tensor", "dp"),
            P("dp", None, "tensor"),
            P("tensor", "dp"),
            P(None, "dp"),
            P("dp", "tensor"),
            P("dp", "tensor", None),
            P("tensor", "dp"),
            P("dp", None, "tensor"),
            P("tensor", "dp"),
            P(None, "dp"),
            P("dp", "tensor"),
            P("dp", "tensor", None),
            P("tensor", "dp"),
            P("dp", None, "tensor"),
            P("tensor", "dp"),
            P(None, "dp"),
            P(),
        ),
        check_vma=False,
    )
```

```python
import jax
import jax.numpy as jnp
from jax import lax
from jax.sharding import PartitionSpec as P

HD = 64
PROMPT = 1024
CONTS = 3
STEP = 3


norm_eps = 1e-05
branch_scale = 0.22
score_scale = 0.015625
rope_base = 10000000.0
moment_decay = 0.5
learn_rate = 0.25
ratio_eps = 1e-06
masked_fill = -1e30


def layout(lengths, group_rows):
    row_index = jnp.arange(group_rows, dtype=jnp.int32)
    ends = jnp.cumsum(lengths)
    starts = ends - lengths
    within = row_index - PROMPT
    inside = (within[:, None] >= starts[None, :]) & (within[:, None] < ends[None, :])
    labels = jnp.arange(1, CONTS + 1, dtype=jnp.int32)
    segment = jnp.sum(jnp.where(inside, labels[None, :], 0), axis=1)
    offsets = jnp.sum(jnp.where(inside, starts[None, :], 0), axis=1)
    position = row_index - offsets
    causal = row_index[None, :] <= row_index[:, None]
    shared = (segment[None, :] == segment[:, None]) | (segment[None, :] == 0)
    return (causal & shared, position)


def rope_tables(position):
    half_size = HD // 2
    inverse = rope_base ** (-2.0 * jnp.arange(half_size, dtype=jnp.float32) / HD)
    angle = position.astype(jnp.float32)[:, None] * inverse[None, :]
    return (jnp.cos(angle)[:, None, :], jnp.sin(angle)[:, None, :])


def rotate(field, cos_table, sin_table):
    half_size = field.shape[-1] // 2
    first_half = field[..., :half_size]
    second_half = field[..., half_size:]
    return jnp.concatenate(
        [
            first_half * cos_table - second_half * sin_table,
            second_half * cos_table + first_half * sin_table,
        ],
        axis=-1,
    )


def rotate_back(grad_field, cos_table, sin_table):
    half_size = grad_field.shape[-1] // 2
    first_half = grad_field[..., :half_size]
    second_half = grad_field[..., half_size:]
    return jnp.concatenate(
        [
            first_half * cos_table + second_half * sin_table,
            second_half * cos_table - first_half * sin_table,
        ],
        axis=-1,
    )


def attend(queries, key_rows, values, visible, block_rows):
    outputs = []
    log_totals = []
    for block in range(2):
        begin = block * block_rows
        stop = begin + block_rows
        scores = (
            jnp.einsum(
                "ikrd,jkd->krij",
                queries[begin:stop],
                key_rows[:stop],
                preferred_element_type=jnp.float32,
            )
            * score_scale
        )
        scores = jnp.where(visible[begin:stop, :stop][None, None], scores, masked_fill)
        row_peak = jnp.max(scores, axis=-1, keepdims=True)
        shifted_exp = jnp.exp(scores - row_peak)
        row_total = jnp.sum(shifted_exp, axis=-1, keepdims=True)
        attn_prob = (shifted_exp / row_total).astype(jnp.bfloat16)
        outputs.append(
            jnp.einsum(
                "krij,jkd->ikrd", attn_prob, values[:stop], preferred_element_type=jnp.float32
            )
        )
        log_totals.append(row_peak + jnp.log(row_total))
    return (jnp.concatenate(outputs, axis=0), jnp.concatenate(log_totals, axis=2))


def attend_back(queries, key_rows, values, visible, log_totals, mixed_grad, block_rows):
    query_grads = []
    key_grad = jnp.zeros(key_rows.shape, jnp.float32)
    value_grad = jnp.zeros(values.shape, jnp.float32)
    for block in range(2):
        begin = block * block_rows
        stop = begin + block_rows
        query_block = queries[begin:stop]
        grad_block = mixed_grad[begin:stop]
        scores = (
            jnp.einsum(
                "ikrd,jkd->krij", query_block, key_rows[:stop], preferred_element_type=jnp.float32
            )
            * score_scale
        )
        attn_prob = jnp.where(
            visible[begin:stop, :stop][None, None],
            jnp.exp(scores - log_totals[:, :, begin:stop]),
            0.0,
        )
        prob_grad = jnp.einsum(
            "ikrd,jkd->krij", grad_block, values[:stop], preferred_element_type=jnp.float32
        )
        row_dot = jnp.sum(attn_prob * prob_grad, axis=-1, keepdims=True)
        score_grad = (attn_prob * (prob_grad - row_dot)).astype(jnp.bfloat16)
        query_grads.append(
            jnp.einsum(
                "krij,jkd->ikrd", score_grad, key_rows[:stop], preferred_element_type=jnp.float32
            )
            * score_scale
        )
        key_grad = key_grad.at[:stop].add(
            jnp.einsum(
                "krij,ikrd->jkd", score_grad, query_block, preferred_element_type=jnp.float32
            )
            * score_scale
        )
        value_grad = value_grad.at[:stop].add(
            jnp.einsum(
                "krij,ikrd->jkd",
                attn_prob.astype(jnp.bfloat16),
                grad_block,
                preferred_element_type=jnp.float32,
            )
        )
    return (jnp.concatenate(query_grads, axis=0), key_grad, value_grad)


def norm_back(upstream, normed_hat, scale_rows, gain_row):
    scaled = upstream * gain_row[None, :]
    through = scale_rows * (
        scaled - normed_hat * jnp.mean(scaled * normed_hat, axis=1, keepdims=True)
    )
    return (through, jnp.sum(upstream * normed_hat, axis=0))


def contract_rows(left, right):
    return lax.dot_general(
        left, right, (((0,), (0,)), ((), ())), preferred_element_type=jnp.float32
    )


def contract_cols(left, right):
    return lax.dot_general(
        left, right, (((1,), (1,)), ((), ())), preferred_element_type=jnp.float32
    )


def line_gather(x, count):
    place = lax.axis_index("tensor")
    rows = x.shape[0]
    out = jnp.zeros((count * rows,) + x.shape[1:], x.dtype)
    from_left = x
    from_right = x
    received = []
    for step in range(1, count):
        from_left = lax.ppermute(
            from_left, "tensor", [(i, i + 1) for i in range(step - 1, count - 1)]
        )
        from_right = lax.ppermute(
            from_right, "tensor", [(i, i - 1) for i in range(1, count - step + 1)]
        )
        received.append((from_left, place - step, place - step >= 0))
        received.append((from_right, place + step, place + step <= count - 1))
    for piece, slot, valid in received:
        out = lax.dynamic_update_slice_in_dim(out, piece, jnp.where(valid, slot, place) * rows, 0)
    return lax.dynamic_update_slice_in_dim(out, x, place * rows, 0)


def line_scatter(partial, count):
    place = lax.axis_index("tensor")
    rows = partial.shape[0] // count

    def chunk(index):
        return lax.dynamic_slice_in_dim(partial, jnp.clip(index, 0, count - 1) * rows, rows, 0)

    to_right = None
    to_left = None
    for step in range(1, count):
        send = chunk(place + count - step)
        if to_right is not None:
            send = send + to_right
        to_right = lax.ppermute(
            send.astype(jnp.bfloat16), "tensor", [(i, i + 1) for i in range(step)]
        ).astype(jnp.float32)
        send = chunk(place - count + step)
        if to_left is not None:
            send = send + to_left
        to_left = lax.ppermute(
            send.astype(jnp.bfloat16), "tensor", [(i, i - 1) for i in range(count - step, count)]
        ).astype(jnp.float32)
    total = chunk(place)
    if to_right is not None:
        total = total + to_right + to_left
    return total


def per_device(
    tokens,
    cotangent,
    cont_lengths,
    query_weight,
    keyval_weight,
    output_weight,
    gateup_weight,
    down_weight,
    norm_gains,
    query_moment,
    keyval_moment,
    output_moment,
    gateup_moment,
    down_moment,
    gains_moment,
    query_square,
    keyval_square,
    output_square,
    gateup_square,
    down_square,
    gains_square,
):
    masters = (query_weight, keyval_weight, output_weight, gateup_weight, down_weight, norm_gains)
    firsts = (query_moment, keyval_moment, output_moment, gateup_moment, down_moment, gains_moment)
    seconds = (query_square, keyval_square, output_square, gateup_square, down_square, gains_square)
    rounded = tuple((master.astype(jnp.bfloat16) for master in masters))
    gathered = (
        lax.all_gather(rounded[0], "dp", axis=0, tiled=True),
        lax.all_gather(rounded[1], "dp", axis=0, tiled=True),
        lax.all_gather(rounded[2], "dp", axis=1, tiled=True),
        lax.all_gather(rounded[3], "dp", axis=0, tiled=True),
        lax.all_gather(rounded[4], "dp", axis=1, tiled=True),
        lax.all_gather(rounded[5], "dp", axis=1, tiled=True),
    )
    full_query, full_keyval, full_output, full_gateup, full_down, full_gains = gathered
    gain_values = full_gains.astype(jnp.float32)
    tensor_count = lax.axis_size("tensor")
    group_rows = tokens.shape[2] * tensor_count
    block_rows = group_rows // 2
    keyval_heads = full_keyval.shape[1]
    query_heads = full_query.shape[1] // HD
    head_repeat = query_heads // keyval_heads

    def micro_step(token_rows, cot_rows, lengths):
        visible, position = layout(lengths, group_rows)
        cos_table, sin_table = rope_tables(position)
        start_rows = token_rows.astype(jnp.float32)
        scale_one = lax.rsqrt(jnp.mean(start_rows * start_rows, axis=1, keepdims=True) + norm_eps)
        hat_one = start_rows * scale_one
        normed_one = (hat_one * gain_values[0][None, :]).astype(jnp.bfloat16)
        rows_one = yield ("gather", normed_one)
        query_raw = jnp.dot(rows_one, full_query, preferred_element_type=jnp.float32).reshape(
            group_rows, query_heads, HD
        )
        keyval_raw = jnp.einsum(
            "rd,dhk->rhk", rows_one, full_keyval, preferred_element_type=jnp.float32
        )
        queries = (
            rotate(query_raw, cos_table, sin_table)
            .astype(jnp.bfloat16)
            .reshape(group_rows, keyval_heads, head_repeat, HD)
        )
        key_rows = rotate(keyval_raw[:, :, :HD], cos_table, sin_table).astype(jnp.bfloat16)
        values = keyval_raw[:, :, HD:].astype(jnp.bfloat16)
        mixed_full, log_totals = attend(queries, key_rows, values, visible, block_rows)
        mixed = mixed_full.astype(jnp.bfloat16).reshape(group_rows, query_heads * HD)
        attn_branch = yield (
            "scatter", jnp.dot(mixed, full_output, preferred_element_type=jnp.float32)
        )
        middle = start_rows + branch_scale * attn_branch
        scale_two = lax.rsqrt(jnp.mean(middle * middle, axis=1, keepdims=True) + norm_eps)
        hat_two = middle * scale_two
        normed_two = (hat_two * gain_values[1][None, :]).astype(jnp.bfloat16)
        rows_two = yield ("gather", normed_two)
        gate_up = jnp.einsum(
            "rd,dcf->rcf", rows_two, full_gateup, preferred_element_type=jnp.float32
        )
        gate_part = gate_up[:, 0]
        up_part = gate_up[:, 1]
        sigmoid_gate = jax.nn.sigmoid(gate_part)
        silu_gate = gate_part * sigmoid_gate
        hidden_state = (silu_gate * up_part).astype(jnp.bfloat16)
        upstream = cot_rows.astype(jnp.float32)
        ffn_grad = (branch_scale * upstream).astype(jnp.bfloat16)
        ffn_grad_all = yield ("gather", ffn_grad)
        ffn_branch = yield (
            "scatter", jnp.dot(hidden_state, full_down, preferred_element_type=jnp.float32)
        )
        layer_rows = (middle + branch_scale * ffn_branch).astype(jnp.bfloat16)
        grad_down = contract_rows(hidden_state, ffn_grad_all)
        hidden_grad = contract_cols(ffn_grad_all, full_down)
        gate_grad = hidden_grad * up_part * sigmoid_gate * (1.0 + gate_part * (1.0 - sigmoid_gate))
        up_grad = hidden_grad * silu_gate
        gateup_grad = jnp.stack([gate_grad, up_grad], axis=1).astype(jnp.bfloat16)
        grad_gateup = jnp.einsum(
            "rd,rcf->dcf", rows_two, gateup_grad, preferred_element_type=jnp.float32
        )
        normed_two_grad = yield (
            "scatter",
            jnp.einsum(
                "rcf,dcf->rd", gateup_grad, full_gateup, preferred_element_type=jnp.float32
            ),
        )
        middle_back, gain_two = norm_back(normed_two_grad, hat_two, scale_two, gain_values[1])
        middle_grad = upstream + middle_back
        attn_grad = (branch_scale * middle_grad).astype(jnp.bfloat16)
        attn_grad_all = yield ("gather", attn_grad)
        grad_output = contract_rows(mixed, attn_grad_all)
        mixed_grad = (
            contract_cols(attn_grad_all, full_output)
            .astype(jnp.bfloat16)
            .reshape(group_rows, keyval_heads, head_repeat, HD)
        )
        query_grad, key_grad, value_grad = attend_back(
            queries, key_rows, values, visible, log_totals, mixed_grad, block_rows
        )
        query_raw_grad = (
            rotate_back(query_grad.reshape(group_rows, query_heads, HD), cos_table, sin_table)
            .astype(jnp.bfloat16)
            .reshape(group_rows, query_heads * HD)
        )
        keyval_raw_grad = jnp.concatenate(
            [rotate_back(key_grad, cos_table, sin_table), value_grad], axis=2
        ).astype(jnp.bfloat16)
        grad_query = contract_rows(rows_one, query_raw_grad)
        grad_keyval = jnp.einsum(
            "rd,rhk->dhk", rows_one, keyval_raw_grad, preferred_element_type=jnp.float32
        )
        normed_one_grad = yield (
            "scatter",
            contract_cols(query_raw_grad, full_query)
            + jnp.einsum(
                "rhk,dhk->rd", keyval_raw_grad, full_keyval, preferred_element_type=jnp.float32
            ),
        )
        start_back, gain_one = norm_back(normed_one_grad, hat_one, scale_one, gain_values[0])
        input_rows = middle_grad + start_back
        gain_grad = jnp.stack([gain_one, gain_two])
        return (
            layer_rows,
            input_rows,
            (grad_query, grad_keyval, grad_output, grad_gateup, grad_down, gain_grad),
        )

    streams = [
        micro_step(tokens[index, 0], cotangent[index, 0], cont_lengths[index, 0])
        for index in range(tokens.shape[0])
    ]
    requests = [next(stream) for stream in streams]
    finished = [None] * len(streams)
    previous = None
    while any(result is None for result in finished):
        for index, stream in enumerate(streams):
            if finished[index] is not None:
                continue
            kind, value = requests[index]
            if previous is not None:
                previous, value = lax.optimization_barrier((previous, value))
            if kind == "gather":
                previous = line_gather(value, tensor_count)
            else:
                previous = line_scatter(value, tensor_count)
            try:
                requests[index] = stream.send(previous)
            except StopIteration as stop:
                finished[index] = stop.value
    out_list = [result[0] for result in finished]
    grad_list = [result[1] for result in finished]
    totals = finished[0][2]
    for result in finished[1:]:
        totals = tuple((old_sum + new_term for old_sum, new_term in zip(totals, result[2])))
    layer_output = jnp.stack(out_list)[:, None]
    input_grad = jnp.stack(grad_list)[:, None]
    width = totals[0].shape[0]
    gain_total = lax.psum(totals[5], "tensor")
    summed = (
        lax.psum_scatter(
            totals[0].astype(jnp.bfloat16), "dp", scatter_dimension=0, tiled=True
        ).astype(jnp.float32),
        lax.psum_scatter(
            totals[1].reshape(width, -1).astype(jnp.bfloat16), "dp", scatter_dimension=0, tiled=True
        )
        .astype(jnp.float32)
        .reshape(-1, *totals[1].shape[1:]),
        lax.psum_scatter(
            totals[2].astype(jnp.bfloat16), "dp", scatter_dimension=1, tiled=True
        ).astype(jnp.float32),
        lax.psum_scatter(
            totals[3].reshape(width, -1).astype(jnp.bfloat16), "dp", scatter_dimension=0, tiled=True
        )
        .astype(jnp.float32)
        .reshape(-1, *totals[3].shape[1:]),
        lax.psum_scatter(
            totals[4].astype(jnp.bfloat16), "dp", scatter_dimension=1, tiled=True
        ).astype(jnp.float32),
        lax.psum_scatter(
            gain_total.astype(jnp.bfloat16), "dp", scatter_dimension=1, tiled=True
        ).astype(jnp.float32),
    )
    correction = 1.0 - moment_decay**STEP
    new_firsts = []
    new_seconds = []
    directions = []
    for grad, first, second in zip(summed, firsts, seconds):
        first_new = moment_decay * first + (1.0 - moment_decay) * grad
        second_new = moment_decay * second + (1.0 - moment_decay) * grad * grad
        direction = first_new / correction / (jnp.sqrt(second_new / correction) + ratio_eps)
        new_firsts.append(first_new)
        new_seconds.append(second_new)
        directions.append(direction)
    weight_part = jnp.concatenate(
        [
            jnp.stack([jnp.sum(masters[slot] * masters[slot]) for slot in range(5)]),
            jnp.sum(norm_gains * norm_gains, axis=1) / tensor_count,
        ]
    )
    update_part = jnp.concatenate(
        [
            jnp.stack([jnp.sum(directions[slot] * directions[slot]) for slot in range(5)]),
            jnp.sum(directions[5] * directions[5], axis=1) / tensor_count,
        ]
    )
    square_totals = lax.psum(jnp.stack([weight_part, update_part]), ("dp", "tensor"))
    trust_norms = jnp.sqrt(square_totals)
    ratio = trust_norms[0] / (trust_norms[1] + ratio_eps)
    new_weights = [masters[slot] - learn_rate * ratio[slot] * directions[slot] for slot in range(5)]
    new_gains = norm_gains - learn_rate * ratio[5:7][:, None] * directions[5]
    return (
        layer_output,
        input_grad,
        new_weights[0],
        new_weights[1],
        new_weights[2],
        new_weights[3],
        new_weights[4],
        new_gains,
        new_firsts[0],
        new_firsts[1],
        new_firsts[2],
        new_firsts[3],
        new_firsts[4],
        new_firsts[5],
        new_seconds[0],
        new_seconds[1],
        new_seconds[2],
        new_seconds[3],
        new_seconds[4],
        new_seconds[5],
        trust_norms,
    )


def solution(mesh):
    return jax.shard_map(
        per_device,
        mesh=mesh,
        in_specs=(
            P(None, "dp", "tensor", None),
            P(None, "dp", "tensor", None),
            P(None, "dp", None),
            P("dp", "tensor"),
            P("dp", "tensor", None),
            P("tensor", "dp"),
            P("dp", None, "tensor"),
            P("tensor", "dp"),
            P(None, "dp"),
            P("dp", "tensor"),
            P("dp", "tensor", None),
            P("tensor", "dp"),
            P("dp", None, "tensor"),
            P("tensor", "dp"),
            P(None, "dp"),
            P("dp", "tensor"),
            P("dp", "tensor", None),
            P("tensor", "dp"),
            P("dp", None, "tensor"),
            P("tensor", "dp"),
            P(None, "dp"),
        ),
        out_specs=(
            P(None, "dp", "tensor", None),
            P(None, "dp", "tensor", None),
            P("dp", "tensor"),
            P("dp", "tensor", None),
            P("tensor", "dp"),
            P("dp", None, "tensor"),
            P("tensor", "dp"),
            P(None, "dp"),
            P("dp", "tensor"),
            P("dp", "tensor", None),
            P("tensor", "dp"),
            P("dp", None, "tensor"),
            P("tensor", "dp"),
            P(None, "dp"),
            P("dp", "tensor"),
            P("dp", "tensor", None),
            P("tensor", "dp"),
            P("dp", None, "tensor"),
            P("tensor", "dp"),
            P(None, "dp"),
            P(),
        ),
        check_vma=False,
    )
```

```python
import jax
import jax.numpy as jnp
from jax import lax
from jax.sharding import PartitionSpec as P

HD = 64
PROMPT = 1024
CONTS = 3
STEP = 3


norm_eps = 1e-05
branch_scale = 0.22
score_scale = 0.015625
rope_base = 10000000.0
moment_decay = 0.5
learn_rate = 0.25
ratio_eps = 1e-06
masked_fill = -1e30


def layout(lengths, group_rows):
    row_index = jnp.arange(group_rows, dtype=jnp.int32)
    ends = jnp.cumsum(lengths)
    starts = ends - lengths
    within = row_index - PROMPT
    inside = (within[:, None] >= starts[None, :]) & (within[:, None] < ends[None, :])
    labels = jnp.arange(1, CONTS + 1, dtype=jnp.int32)
    segment = jnp.sum(jnp.where(inside, labels[None, :], 0), axis=1)
    offsets = jnp.sum(jnp.where(inside, starts[None, :], 0), axis=1)
    position = row_index - offsets
    causal = row_index[None, :] <= row_index[:, None]
    shared = (segment[None, :] == segment[:, None]) | (segment[None, :] == 0)
    return (causal & shared, position)


def rope_tables(position):
    half_size = HD // 2
    inverse = rope_base ** (-2.0 * jnp.arange(half_size, dtype=jnp.float32) / HD)
    angle = position.astype(jnp.float32)[:, None] * inverse[None, :]
    return (jnp.cos(angle)[:, None, :], jnp.sin(angle)[:, None, :])


def rotate(field, cos_table, sin_table):
    half_size = field.shape[-1] // 2
    first_half = field[..., :half_size]
    second_half = field[..., half_size:]
    return jnp.concatenate(
        [
            first_half * cos_table - second_half * sin_table,
            second_half * cos_table + first_half * sin_table,
        ],
        axis=-1,
    )


def rotate_back(grad_field, cos_table, sin_table):
    half_size = grad_field.shape[-1] // 2
    first_half = grad_field[..., :half_size]
    second_half = grad_field[..., half_size:]
    return jnp.concatenate(
        [
            first_half * cos_table + second_half * sin_table,
            second_half * cos_table - first_half * sin_table,
        ],
        axis=-1,
    )


def attend(queries, key_rows, values, visible, block_rows):
    outputs = []
    log_totals = []
    for block in range(2):
        begin = block * block_rows
        stop = begin + block_rows
        scores = (
            jnp.einsum(
                "ikrd,jkd->krij",
                queries[begin:stop],
                key_rows[:stop],
                preferred_element_type=jnp.float32,
            )
            * score_scale
        )
        scores = jnp.where(visible[begin:stop, :stop][None, None], scores, masked_fill)
        row_peak = jnp.max(scores, axis=-1, keepdims=True)
        shifted_exp = jnp.exp(scores - row_peak)
        row_total = jnp.sum(shifted_exp, axis=-1, keepdims=True)
        attn_prob = (shifted_exp / row_total).astype(jnp.bfloat16)
        outputs.append(
            jnp.einsum(
                "krij,jkd->ikrd", attn_prob, values[:stop], preferred_element_type=jnp.float32
            )
        )
        log_totals.append(row_peak + jnp.log(row_total))
    return (jnp.concatenate(outputs, axis=0), jnp.concatenate(log_totals, axis=2))


def attend_back(queries, key_rows, values, visible, log_totals, mixed_grad, block_rows):
    query_grads = []
    key_grad = jnp.zeros(key_rows.shape, jnp.float32)
    value_grad = jnp.zeros(values.shape, jnp.float32)
    for block in range(2):
        begin = block * block_rows
        stop = begin + block_rows
        query_block = queries[begin:stop]
        grad_block = mixed_grad[begin:stop]
        scores = (
            jnp.einsum(
                "ikrd,jkd->krij", query_block, key_rows[:stop], preferred_element_type=jnp.float32
            )
            * score_scale
        )
        attn_prob = jnp.where(
            visible[begin:stop, :stop][None, None],
            jnp.exp(scores - log_totals[:, :, begin:stop]),
            0.0,
        )
        prob_grad = jnp.einsum(
            "ikrd,jkd->krij", grad_block, values[:stop], preferred_element_type=jnp.float32
        )
        row_dot = jnp.sum(attn_prob * prob_grad, axis=-1, keepdims=True)
        score_grad = (attn_prob * (prob_grad - row_dot)).astype(jnp.bfloat16)
        query_grads.append(
            jnp.einsum(
                "krij,jkd->ikrd", score_grad, key_rows[:stop], preferred_element_type=jnp.float32
            )
            * score_scale
        )
        key_grad = key_grad.at[:stop].add(
            jnp.einsum(
                "krij,ikrd->jkd", score_grad, query_block, preferred_element_type=jnp.float32
            )
            * score_scale
        )
        value_grad = value_grad.at[:stop].add(
            jnp.einsum(
                "krij,ikrd->jkd",
                attn_prob.astype(jnp.bfloat16),
                grad_block,
                preferred_element_type=jnp.float32,
            )
        )
    return (jnp.concatenate(query_grads, axis=0), key_grad, value_grad)


def norm_back(upstream, normed_hat, scale_rows, gain_row):
    scaled = upstream * gain_row[None, :]
    through = scale_rows * (
        scaled - normed_hat * jnp.mean(scaled * normed_hat, axis=1, keepdims=True)
    )
    return (through, jnp.sum(upstream * normed_hat, axis=0))


def contract_rows(left, right):
    return lax.dot_general(
        left, right, (((0,), (0,)), ((), ())), preferred_element_type=jnp.float32
    )


def contract_cols(left, right):
    return lax.dot_general(
        left, right, (((1,), (1,)), ((), ())), preferred_element_type=jnp.float32
    )


def line_gather(x, count):
    place = lax.axis_index("tensor")
    rows = x.shape[0]
    out = jnp.zeros((count * rows,) + x.shape[1:], x.dtype)
    from_left = x
    from_right = x
    received = []
    for step in range(1, count):
        from_left = lax.ppermute(
            from_left, "tensor", [(i, i + 1) for i in range(step - 1, count - 1)]
        )
        from_right = lax.ppermute(
            from_right, "tensor", [(i, i - 1) for i in range(1, count - step + 1)]
        )
        received.append((from_left, place - step, place - step >= 0))
        received.append((from_right, place + step, place + step <= count - 1))
    for piece, slot, valid in received:
        out = lax.dynamic_update_slice_in_dim(out, piece, jnp.where(valid, slot, place) * rows, 0)
    return lax.dynamic_update_slice_in_dim(out, x, place * rows, 0)


def line_scatter(partial, count):
    place = lax.axis_index("tensor")
    rows = partial.shape[0] // count

    def chunk(index):
        return lax.dynamic_slice_in_dim(partial, jnp.clip(index, 0, count - 1) * rows, rows, 0)

    to_right = None
    to_left = None
    for step in range(1, count):
        send = chunk(place + count - step)
        if to_right is not None:
            send = send + to_right
        to_right = lax.ppermute(
            send.astype(jnp.bfloat16), "tensor", [(i, i + 1) for i in range(step)]
        ).astype(jnp.float32)
        send = chunk(place - count + step)
        if to_left is not None:
            send = send + to_left
        to_left = lax.ppermute(
            send.astype(jnp.bfloat16), "tensor", [(i, i - 1) for i in range(count - step, count)]
        ).astype(jnp.float32)
    total = chunk(place)
    if to_right is not None:
        total = total + to_right + to_left
    return total


def per_device(
    tokens,
    cotangent,
    cont_lengths,
    query_weight,
    keyval_weight,
    output_weight,
    gateup_weight,
    down_weight,
    norm_gains,
    query_moment,
    keyval_moment,
    output_moment,
    gateup_moment,
    down_moment,
    gains_moment,
    query_square,
    keyval_square,
    output_square,
    gateup_square,
    down_square,
    gains_square,
):
    masters = (query_weight, keyval_weight, output_weight, gateup_weight, down_weight, norm_gains)
    firsts = (query_moment, keyval_moment, output_moment, gateup_moment, down_moment, gains_moment)
    seconds = (query_square, keyval_square, output_square, gateup_square, down_square, gains_square)
    rounded = tuple((master.astype(jnp.bfloat16) for master in masters))
    gathered = (
        lax.all_gather(rounded[0], "dp", axis=0, tiled=True),
        lax.all_gather(rounded[1], "dp", axis=0, tiled=True),
        lax.all_gather(rounded[2], "dp", axis=1, tiled=True),
        lax.all_gather(rounded[3], "dp", axis=0, tiled=True),
        lax.all_gather(rounded[4], "dp", axis=1, tiled=True),
        lax.all_gather(rounded[5], "dp", axis=1, tiled=True),
    )
    full_query, full_keyval, full_output, full_gateup, full_down, full_gains = gathered
    gain_values = full_gains.astype(jnp.float32)
    tensor_count = lax.axis_size("tensor")
    group_rows = tokens.shape[2] * tensor_count
    block_rows = group_rows // 2
    keyval_heads = full_keyval.shape[1]
    query_heads = full_query.shape[1] // HD
    head_repeat = query_heads // keyval_heads

    def micro_step(token_rows, cot_rows, lengths):
        visible, position = layout(lengths, group_rows)
        cos_table, sin_table = rope_tables(position)
        start_rows = token_rows.astype(jnp.float32)
        scale_one = lax.rsqrt(jnp.mean(start_rows * start_rows, axis=1, keepdims=True) + norm_eps)
        hat_one = start_rows * scale_one
        normed_one = (hat_one * gain_values[0][None, :]).astype(jnp.bfloat16)
        rows_one = yield ("gather", normed_one)
        query_raw = jnp.dot(rows_one, full_query, preferred_element_type=jnp.float32).reshape(
            group_rows, query_heads, HD
        )
        keyval_raw = jnp.einsum(
            "rd,dhk->rhk", rows_one, full_keyval, preferred_element_type=jnp.float32
        )
        queries = (
            rotate(query_raw, cos_table, sin_table)
            .astype(jnp.bfloat16)
            .reshape(group_rows, keyval_heads, head_repeat, HD)
        )
        key_rows = rotate(keyval_raw[:, :, :HD], cos_table, sin_table).astype(jnp.bfloat16)
        values = keyval_raw[:, :, HD:].astype(jnp.bfloat16)
        mixed_full, log_totals = attend(queries, key_rows, values, visible, block_rows)
        mixed = mixed_full.astype(jnp.bfloat16).reshape(group_rows, query_heads * HD)
        attn_branch = yield (
            "scatter", jnp.dot(mixed, full_output, preferred_element_type=jnp.float32)
        )
        middle = start_rows + branch_scale * attn_branch
        scale_two = lax.rsqrt(jnp.mean(middle * middle, axis=1, keepdims=True) + norm_eps)
        hat_two = middle * scale_two
        normed_two = (hat_two * gain_values[1][None, :]).astype(jnp.bfloat16)
        rows_two = yield ("gather", normed_two)
        gate_up = jnp.einsum(
            "rd,dcf->rcf", rows_two, full_gateup, preferred_element_type=jnp.float32
        )
        gate_part = gate_up[:, 0]
        up_part = gate_up[:, 1]
        sigmoid_gate = jax.nn.sigmoid(gate_part)
        silu_gate = gate_part * sigmoid_gate
        hidden_state = (silu_gate * up_part).astype(jnp.bfloat16)
        upstream = cot_rows.astype(jnp.float32)
        ffn_grad = (branch_scale * upstream).astype(jnp.bfloat16)
        ffn_grad, _ = lax.optimization_barrier((ffn_grad, hidden_state))
        ffn_grad_all = yield ("gather", ffn_grad)
        ffn_branch = yield (
            "scatter", jnp.dot(hidden_state, full_down, preferred_element_type=jnp.float32)
        )
        layer_rows = (middle + branch_scale * ffn_branch).astype(jnp.bfloat16)
        grad_down = contract_rows(hidden_state, ffn_grad_all)
        hidden_grad = contract_cols(ffn_grad_all, full_down)
        gate_grad = hidden_grad * up_part * sigmoid_gate * (1.0 + gate_part * (1.0 - sigmoid_gate))
        up_grad = hidden_grad * silu_gate
        gateup_grad = jnp.stack([gate_grad, up_grad], axis=1).astype(jnp.bfloat16)
        grad_gateup = jnp.einsum(
            "rd,rcf->dcf", rows_two, gateup_grad, preferred_element_type=jnp.float32
        )
        normed_two_grad = yield (
            "scatter",
            jnp.einsum(
                "rcf,dcf->rd", gateup_grad, full_gateup, preferred_element_type=jnp.float32
            ),
        )
        middle_back, gain_two = norm_back(normed_two_grad, hat_two, scale_two, gain_values[1])
        middle_grad = upstream + middle_back
        attn_grad = (branch_scale * middle_grad).astype(jnp.bfloat16)
        attn_grad_all = yield ("gather", attn_grad)
        grad_output = contract_rows(mixed, attn_grad_all)
        mixed_grad = (
            contract_cols(attn_grad_all, full_output)
            .astype(jnp.bfloat16)
            .reshape(group_rows, keyval_heads, head_repeat, HD)
        )
        query_grad, key_grad, value_grad = attend_back(
            queries, key_rows, values, visible, log_totals, mixed_grad, block_rows
        )
        query_raw_grad = (
            rotate_back(query_grad.reshape(group_rows, query_heads, HD), cos_table, sin_table)
            .astype(jnp.bfloat16)
            .reshape(group_rows, query_heads * HD)
        )
        keyval_raw_grad = jnp.concatenate(
            [rotate_back(key_grad, cos_table, sin_table), value_grad], axis=2
        ).astype(jnp.bfloat16)
        grad_query = contract_rows(rows_one, query_raw_grad)
        grad_keyval = jnp.einsum(
            "rd,rhk->dhk", rows_one, keyval_raw_grad, preferred_element_type=jnp.float32
        )
        normed_one_grad = yield (
            "scatter",
            contract_cols(query_raw_grad, full_query)
            + jnp.einsum(
                "rhk,dhk->rd", keyval_raw_grad, full_keyval, preferred_element_type=jnp.float32
            ),
        )
        start_back, gain_one = norm_back(normed_one_grad, hat_one, scale_one, gain_values[0])
        input_rows = middle_grad + start_back
        gain_grad = jnp.stack([gain_one, gain_two])
        return (
            layer_rows,
            input_rows,
            (grad_query, grad_keyval, grad_output, grad_gateup, grad_down, gain_grad),
        )

    streams = [
        micro_step(tokens[index, 0], cotangent[index, 0], cont_lengths[index, 0])
        for index in range(tokens.shape[0])
    ]
    requests = [next(stream) for stream in streams]
    finished = [None] * len(streams)
    previous = None
    while any(result is None for result in finished):
        for index, stream in enumerate(streams):
            if finished[index] is not None:
                continue
            kind, value = requests[index]
            if previous is not None:
                previous, value = lax.optimization_barrier((previous, value))
            if kind == "gather":
                previous = line_gather(value, tensor_count)
            else:
                previous = line_scatter(value, tensor_count)
            try:
                requests[index] = stream.send(previous)
            except StopIteration as stop:
                finished[index] = stop.value
    out_list = [result[0] for result in finished]
    grad_list = [result[1] for result in finished]
    totals = finished[0][2]
    for result in finished[1:]:
        totals = tuple((old_sum + new_term for old_sum, new_term in zip(totals, result[2])))
    layer_output = jnp.stack(out_list)[:, None]
    input_grad = jnp.stack(grad_list)[:, None]
    width = totals[0].shape[0]
    gain_total = lax.psum(totals[5], "tensor")
    summed = (
        lax.psum_scatter(
            totals[0].astype(jnp.bfloat16), "dp", scatter_dimension=0, tiled=True
        ).astype(jnp.float32),
        lax.psum_scatter(
            totals[1].reshape(width, -1).astype(jnp.bfloat16), "dp", scatter_dimension=0, tiled=True
        )
        .astype(jnp.float32)
        .reshape(-1, *totals[1].shape[1:]),
        lax.psum_scatter(
            totals[2].astype(jnp.bfloat16), "dp", scatter_dimension=1, tiled=True
        ).astype(jnp.float32),
        lax.psum_scatter(
            totals[3].reshape(width, -1).astype(jnp.bfloat16), "dp", scatter_dimension=0, tiled=True
        )
        .astype(jnp.float32)
        .reshape(-1, *totals[3].shape[1:]),
        lax.psum_scatter(
            totals[4].astype(jnp.bfloat16), "dp", scatter_dimension=1, tiled=True
        ).astype(jnp.float32),
        lax.psum_scatter(
            gain_total.astype(jnp.bfloat16), "dp", scatter_dimension=1, tiled=True
        ).astype(jnp.float32),
    )
    correction = 1.0 - moment_decay**STEP
    new_firsts = []
    new_seconds = []
    directions = []
    for grad, first, second in zip(summed, firsts, seconds):
        first_new = moment_decay * first + (1.0 - moment_decay) * grad
        second_new = moment_decay * second + (1.0 - moment_decay) * grad * grad
        direction = first_new / correction / (jnp.sqrt(second_new / correction) + ratio_eps)
        new_firsts.append(first_new)
        new_seconds.append(second_new)
        directions.append(direction)
    weight_part = jnp.concatenate(
        [
            jnp.stack([jnp.sum(masters[slot] * masters[slot]) for slot in range(5)]),
            jnp.sum(norm_gains * norm_gains, axis=1) / tensor_count,
        ]
    )
    update_part = jnp.concatenate(
        [
            jnp.stack([jnp.sum(directions[slot] * directions[slot]) for slot in range(5)]),
            jnp.sum(directions[5] * directions[5], axis=1) / tensor_count,
        ]
    )
    square_totals = lax.psum(jnp.stack([weight_part, update_part]), ("dp", "tensor"))
    trust_norms = jnp.sqrt(square_totals)
    ratio = trust_norms[0] / (trust_norms[1] + ratio_eps)
    new_weights = [masters[slot] - learn_rate * ratio[slot] * directions[slot] for slot in range(5)]
    new_gains = norm_gains - learn_rate * ratio[5:7][:, None] * directions[5]
    return (
        layer_output,
        input_grad,
        new_weights[0],
        new_weights[1],
        new_weights[2],
        new_weights[3],
        new_weights[4],
        new_gains,
        new_firsts[0],
        new_firsts[1],
        new_firsts[2],
        new_firsts[3],
        new_firsts[4],
        new_firsts[5],
        new_seconds[0],
        new_seconds[1],
        new_seconds[2],
        new_seconds[3],
        new_seconds[4],
        new_seconds[5],
        trust_norms,
    )


def solution(mesh):
    return jax.shard_map(
        per_device,
        mesh=mesh,
        in_specs=(
            P(None, "dp", "tensor", None),
            P(None, "dp", "tensor", None),
            P(None, "dp", None),
            P("dp", "tensor"),
            P("dp", "tensor", None),
            P("tensor", "dp"),
            P("dp", None, "tensor"),
            P("tensor", "dp"),
            P(None, "dp"),
            P("dp", "tensor"),
            P("dp", "tensor", None),
            P("tensor", "dp"),
            P("dp", None, "tensor"),
            P("tensor", "dp"),
            P(None, "dp"),
            P("dp", "tensor"),
            P("dp", "tensor", None),
            P("tensor", "dp"),
            P("dp", None, "tensor"),
            P("tensor", "dp"),
            P(None, "dp"),
        ),
        out_specs=(
            P(None, "dp", "tensor", None),
            P(None, "dp", "tensor", None),
            P("dp", "tensor"),
            P("dp", "tensor", None),
            P("tensor", "dp"),
            P("dp", None, "tensor"),
            P("tensor", "dp"),
            P(None, "dp"),
            P("dp", "tensor"),
            P("dp", "tensor", None),
            P("tensor", "dp"),
            P("dp", None, "tensor"),
            P("tensor", "dp"),
            P(None, "dp"),
            P("dp", "tensor"),
            P("dp", "tensor", None),
            P("tensor", "dp"),
            P("dp", None, "tensor"),
            P("tensor", "dp"),
            P(None, "dp"),
            P(),
        ),
        check_vma=False,
    )
```

```python
import jax
import jax.numpy as jnp
from jax import lax
from jax.sharding import PartitionSpec as P

HD = 64
PROMPT = 1024
CONTS = 3
STEP = 3


norm_eps = 1e-05
branch_scale = 0.22
score_scale = 0.015625
rope_base = 10000000.0
moment_decay = 0.5
learn_rate = 0.25
ratio_eps = 1e-06
masked_fill = -1e30


def layout(lengths, group_rows):
    row_index = jnp.arange(group_rows, dtype=jnp.int32)
    ends = jnp.cumsum(lengths)
    starts = ends - lengths
    within = row_index - PROMPT
    inside = (within[:, None] >= starts[None, :]) & (within[:, None] < ends[None, :])
    labels = jnp.arange(1, CONTS + 1, dtype=jnp.int32)
    segment = jnp.sum(jnp.where(inside, labels[None, :], 0), axis=1)
    offsets = jnp.sum(jnp.where(inside, starts[None, :], 0), axis=1)
    position = row_index - offsets
    causal = row_index[None, :] <= row_index[:, None]
    shared = (segment[None, :] == segment[:, None]) | (segment[None, :] == 0)
    return (causal & shared, position)


def rope_tables(position):
    half_size = HD // 2
    inverse = rope_base ** (-2.0 * jnp.arange(half_size, dtype=jnp.float32) / HD)
    angle = position.astype(jnp.float32)[:, None] * inverse[None, :]
    return (jnp.cos(angle)[:, None, :], jnp.sin(angle)[:, None, :])


def rotate(field, cos_table, sin_table):
    half_size = field.shape[-1] // 2
    first_half = field[..., :half_size]
    second_half = field[..., half_size:]
    return jnp.concatenate(
        [
            first_half * cos_table - second_half * sin_table,
            second_half * cos_table + first_half * sin_table,
        ],
        axis=-1,
    )


def rotate_back(grad_field, cos_table, sin_table):
    half_size = grad_field.shape[-1] // 2
    first_half = grad_field[..., :half_size]
    second_half = grad_field[..., half_size:]
    return jnp.concatenate(
        [
            first_half * cos_table + second_half * sin_table,
            second_half * cos_table - first_half * sin_table,
        ],
        axis=-1,
    )


def attend(queries, key_rows, values, visible, block_rows):
    outputs = []
    log_totals = []
    for block in range(2):
        begin = block * block_rows
        stop = begin + block_rows
        scores = (
            jnp.einsum(
                "ikrd,jkd->krij",
                queries[begin:stop],
                key_rows[:stop],
                preferred_element_type=jnp.float32,
            )
            * score_scale
        )
        scores = jnp.where(visible[begin:stop, :stop][None, None], scores, masked_fill)
        row_peak = jnp.max(scores, axis=-1, keepdims=True)
        shifted_exp = jnp.exp(scores - row_peak)
        row_total = jnp.sum(shifted_exp, axis=-1, keepdims=True)
        attn_prob = (shifted_exp / row_total).astype(jnp.bfloat16)
        outputs.append(
            jnp.einsum(
                "krij,jkd->ikrd", attn_prob, values[:stop], preferred_element_type=jnp.float32
            )
        )
        log_totals.append(row_peak + jnp.log(row_total))
    return (jnp.concatenate(outputs, axis=0), jnp.concatenate(log_totals, axis=2))


def attend_back(queries, key_rows, values, visible, log_totals, mixed_grad, block_rows):
    query_grads = []
    key_grad = jnp.zeros(key_rows.shape, jnp.float32)
    value_grad = jnp.zeros(values.shape, jnp.float32)
    for block in range(2):
        begin = block * block_rows
        stop = begin + block_rows
        query_block = queries[begin:stop]
        grad_block = mixed_grad[begin:stop]
        scores = (
            jnp.einsum(
                "ikrd,jkd->krij", query_block, key_rows[:stop], preferred_element_type=jnp.float32
            )
            * score_scale
        )
        attn_prob = jnp.where(
            visible[begin:stop, :stop][None, None],
            jnp.exp(scores - log_totals[:, :, begin:stop]),
            0.0,
        )
        prob_grad = jnp.einsum(
            "ikrd,jkd->krij", grad_block, values[:stop], preferred_element_type=jnp.float32
        )
        row_dot = jnp.sum(attn_prob * prob_grad, axis=-1, keepdims=True)
        score_grad = (attn_prob * (prob_grad - row_dot)).astype(jnp.bfloat16)
        query_grads.append(
            jnp.einsum(
                "krij,jkd->ikrd", score_grad, key_rows[:stop], preferred_element_type=jnp.float32
            )
            * score_scale
        )
        key_grad = key_grad.at[:stop].add(
            jnp.einsum(
                "krij,ikrd->jkd", score_grad, query_block, preferred_element_type=jnp.float32
            )
            * score_scale
        )
        value_grad = value_grad.at[:stop].add(
            jnp.einsum(
                "krij,ikrd->jkd",
                attn_prob.astype(jnp.bfloat16),
                grad_block,
                preferred_element_type=jnp.float32,
            )
        )
    return (jnp.concatenate(query_grads, axis=0), key_grad, value_grad)


def norm_back(upstream, normed_hat, scale_rows, gain_row):
    scaled = upstream * gain_row[None, :]
    through = scale_rows * (
        scaled - normed_hat * jnp.mean(scaled * normed_hat, axis=1, keepdims=True)
    )
    return (through, jnp.sum(upstream * normed_hat, axis=0))


def contract_rows(left, right):
    return lax.dot_general(
        left, right, (((0,), (0,)), ((), ())), preferred_element_type=jnp.float32
    )


def contract_cols(left, right):
    return lax.dot_general(
        left, right, (((1,), (1,)), ((), ())), preferred_element_type=jnp.float32
    )


def line_gather(x, count):
    place = lax.axis_index("tensor")
    rows = x.shape[0]
    out = jnp.zeros((count * rows,) + x.shape[1:], x.dtype)
    from_left = x
    from_right = x
    received = []
    for step in range(1, count):
        from_left = lax.ppermute(
            from_left, "tensor", [(i, i + 1) for i in range(step - 1, count - 1)]
        )
        from_right = lax.ppermute(
            from_right, "tensor", [(i, i - 1) for i in range(1, count - step + 1)]
        )
        received.append((from_left, place - step, place - step >= 0))
        received.append((from_right, place + step, place + step <= count - 1))
    for piece, slot, valid in received:
        out = lax.dynamic_update_slice_in_dim(out, piece, jnp.where(valid, slot, place) * rows, 0)
    return lax.dynamic_update_slice_in_dim(out, x, place * rows, 0)


def line_scatter(partial, count):
    place = lax.axis_index("tensor")
    rows = partial.shape[0] // count

    def chunk(index):
        return lax.dynamic_slice_in_dim(partial, jnp.clip(index, 0, count - 1) * rows, rows, 0)

    to_right = None
    to_left = None
    for step in range(1, count):
        send = chunk(place + count - step)
        if to_right is not None:
            send = send + to_right
        to_right = lax.ppermute(
            send.astype(jnp.bfloat16), "tensor", [(i, i + 1) for i in range(step)]
        ).astype(jnp.float32)
        send = chunk(place - count + step)
        if to_left is not None:
            send = send + to_left
        to_left = lax.ppermute(
            send.astype(jnp.bfloat16), "tensor", [(i, i - 1) for i in range(count - step, count)]
        ).astype(jnp.float32)
    total = chunk(place)
    if to_right is not None:
        total = total + to_right + to_left
    return total


def per_device(
    tokens,
    cotangent,
    cont_lengths,
    query_weight,
    keyval_weight,
    output_weight,
    gateup_weight,
    down_weight,
    norm_gains,
    query_moment,
    keyval_moment,
    output_moment,
    gateup_moment,
    down_moment,
    gains_moment,
    query_square,
    keyval_square,
    output_square,
    gateup_square,
    down_square,
    gains_square,
):
    masters = (query_weight, keyval_weight, output_weight, gateup_weight, down_weight, norm_gains)
    firsts = (query_moment, keyval_moment, output_moment, gateup_moment, down_moment, gains_moment)
    seconds = (query_square, keyval_square, output_square, gateup_square, down_square, gains_square)
    rounded = tuple((master.astype(jnp.bfloat16) for master in masters))
    gathered = (
        lax.all_gather(
            lax.all_gather(rounded[0], "tensor", axis=1, tiled=True), "dp", axis=0, tiled=True
        ),
        lax.all_gather(
            lax.all_gather(rounded[1], "tensor", axis=1, tiled=True), "dp", axis=0, tiled=True
        ),
        lax.all_gather(
            lax.all_gather(rounded[2], "tensor", axis=0, tiled=True), "dp", axis=1, tiled=True
        ),
        lax.all_gather(rounded[3], "dp", axis=0, tiled=True),
        lax.all_gather(rounded[4], "dp", axis=1, tiled=True),
        lax.all_gather(rounded[5], "dp", axis=1, tiled=True),
    )
    full_query, full_keyval, full_output, full_gateup, full_down, full_gains = gathered
    gain_values = full_gains.astype(jnp.float32)
    tensor_count = lax.axis_size("tensor")
    group_rows = tokens.shape[2] * tensor_count
    block_rows = group_rows // 2
    place = lax.axis_index("tensor")
    rows = tokens.shape[2]
    all_query_heads = full_query.shape[1] // HD
    keyval_heads = full_keyval.shape[1] // tensor_count
    query_heads = all_query_heads // tensor_count
    head_repeat = query_heads // keyval_heads

    def micro_step(token_rows, cot_rows, lengths):
        visible, position = layout(lengths, group_rows)
        cos_table, sin_table = rope_tables(position)
        cos_own, sin_own = rope_tables(lax.dynamic_slice_in_dim(position, place * rows, rows))
        start_rows = token_rows.astype(jnp.float32)
        scale_one = lax.rsqrt(jnp.mean(start_rows * start_rows, axis=1, keepdims=True) + norm_eps)
        hat_one = start_rows * scale_one
        normed_one = (hat_one * gain_values[0][None, :]).astype(jnp.bfloat16)
        query_raw = jnp.dot(normed_one, full_query, preferred_element_type=jnp.float32).reshape(
            rows, all_query_heads, HD
        )
        keyval_raw = jnp.einsum(
            "rd,dhk->rhk", normed_one, full_keyval, preferred_element_type=jnp.float32
        )
        queries_own = rotate(query_raw, cos_own, sin_own).astype(jnp.bfloat16)
        keyval_own = jnp.concatenate(
            [rotate(keyval_raw[:, :, :HD], cos_own, sin_own), keyval_raw[:, :, HD:]], axis=2
        ).astype(jnp.bfloat16)
        query_width = query_heads * HD
        projected = yield (
            "to_heads",
            jnp.concatenate(
                [
                    queries_own.reshape(rows, tensor_count, query_width),
                    keyval_own.reshape(rows, tensor_count, -1),
                ],
                axis=2,
            ),
        )
        projected = projected.reshape(group_rows, -1)
        queries = projected[:, :query_width].reshape(group_rows, keyval_heads, head_repeat, HD)
        keyval_rows = projected[:, query_width:].reshape(group_rows, keyval_heads, 2 * HD)
        key_rows = keyval_rows[:, :, :HD]
        values = keyval_rows[:, :, HD:]
        mixed_full, log_totals = attend(queries, key_rows, values, visible, block_rows)
        mixed = yield (
            "to_rows", mixed_full.astype(jnp.bfloat16).reshape(group_rows, query_width)
        )
        attn_branch = jnp.dot(mixed, full_output, preferred_element_type=jnp.float32)
        middle = start_rows + branch_scale * attn_branch
        scale_two = lax.rsqrt(jnp.mean(middle * middle, axis=1, keepdims=True) + norm_eps)
        hat_two = middle * scale_two
        normed_two = (hat_two * gain_values[1][None, :]).astype(jnp.bfloat16)
        rows_two = yield ("gather", normed_two)
        gate_up = jnp.einsum(
            "rd,dcf->rcf", rows_two, full_gateup, preferred_element_type=jnp.float32
        )
        gate_part = gate_up[:, 0]
        up_part = gate_up[:, 1]
        sigmoid_gate = jax.nn.sigmoid(gate_part)
        silu_gate = gate_part * sigmoid_gate
        hidden_state = (silu_gate * up_part).astype(jnp.bfloat16)
        upstream = cot_rows.astype(jnp.float32)
        ffn_grad = (branch_scale * upstream).astype(jnp.bfloat16)
        ffn_grad_all = yield ("gather", ffn_grad)
        ffn_branch = yield (
            "scatter", jnp.dot(hidden_state, full_down, preferred_element_type=jnp.float32)
        )
        layer_rows = (middle + branch_scale * ffn_branch).astype(jnp.bfloat16)
        grad_down = contract_rows(hidden_state, ffn_grad_all)
        hidden_grad = contract_cols(ffn_grad_all, full_down)
        gate_grad = hidden_grad * up_part * sigmoid_gate * (1.0 + gate_part * (1.0 - sigmoid_gate))
        up_grad = hidden_grad * silu_gate
        gateup_grad = jnp.stack([gate_grad, up_grad], axis=1).astype(jnp.bfloat16)
        grad_gateup = jnp.einsum(
            "rd,rcf->dcf", rows_two, gateup_grad, preferred_element_type=jnp.float32
        )
        normed_two_grad = yield (
            "scatter",
            jnp.einsum(
                "rcf,dcf->rd", gateup_grad, full_gateup, preferred_element_type=jnp.float32
            ),
        )
        middle_back, gain_two = norm_back(normed_two_grad, hat_two, scale_two, gain_values[1])
        middle_grad = upstream + middle_back
        attn_grad = (branch_scale * middle_grad).astype(jnp.bfloat16)
        grad_output = contract_rows(mixed, attn_grad)
        mixed_grad = yield (
            "to_heads",
            contract_cols(attn_grad, full_output)
            .astype(jnp.bfloat16)
            .reshape(rows, tensor_count, query_width),
        )
        mixed_grad = mixed_grad.reshape(group_rows, keyval_heads, head_repeat, HD)
        query_grad, key_grad, value_grad = attend_back(
            queries, key_rows, values, visible, log_totals, mixed_grad, block_rows
        )
        raw_grads = yield (
            "to_rows",
            jnp.concatenate(
                [
                    rotate_back(
                        query_grad.reshape(group_rows, query_heads, HD), cos_table, sin_table
                    ).reshape(group_rows, query_width),
                    jnp.concatenate(
                        [rotate_back(key_grad, cos_table, sin_table), value_grad], axis=2
                    ).reshape(group_rows, -1),
                ],
                axis=1,
            ).astype(jnp.bfloat16),
        )
        raw_grads = raw_grads.reshape(rows, tensor_count, -1)
        query_raw_grad = raw_grads[:, :, :query_width].reshape(rows, all_query_heads * HD)
        keyval_raw_grad = raw_grads[:, :, query_width:].reshape(
            rows, tensor_count * keyval_heads, 2 * HD
        )
        grad_query = contract_rows(normed_one, query_raw_grad)
        grad_keyval = jnp.einsum(
            "rd,rhk->dhk", normed_one, keyval_raw_grad, preferred_element_type=jnp.float32
        )
        normed_one_grad = contract_cols(query_raw_grad, full_query) + jnp.einsum(
            "rhk,dhk->rd", keyval_raw_grad, full_keyval, preferred_element_type=jnp.float32
        )
        start_back, gain_one = norm_back(normed_one_grad, hat_one, scale_one, gain_values[0])
        input_rows = middle_grad + start_back
        gain_grad = jnp.stack([gain_one, gain_two])
        return (
            layer_rows,
            input_rows,
            (grad_query, grad_keyval, grad_output, grad_gateup, grad_down, gain_grad),
        )

    streams = [
        micro_step(tokens[index, 0], cotangent[index, 0], cont_lengths[index, 0])
        for index in range(tokens.shape[0])
    ]
    requests = [next(stream) for stream in streams]
    finished = [None] * len(streams)
    previous = None
    while any(result is None for result in finished):
        for index, stream in enumerate(streams):
            if finished[index] is not None:
                continue
            kind, value = requests[index]
            if previous is not None:
                previous, value = lax.optimization_barrier((previous, value))
            if kind == "gather":
                previous = line_gather(value, tensor_count)
            elif kind == "scatter":
                previous = line_scatter(value, tensor_count)
            elif kind == "to_heads":
                previous = lax.all_to_all(value, "tensor", 1, 0, tiled=True)
            else:
                previous = lax.all_to_all(value, "tensor", 0, 1, tiled=True)
            try:
                requests[index] = stream.send(previous)
            except StopIteration as stop:
                finished[index] = stop.value
    out_list = [result[0] for result in finished]
    grad_list = [result[1] for result in finished]
    totals = finished[0][2]
    for result in finished[1:]:
        totals = tuple((old_sum + new_term for old_sum, new_term in zip(totals, result[2])))
    layer_output = jnp.stack(out_list)[:, None]
    input_grad = jnp.stack(grad_list)[:, None]
    width = totals[0].shape[0]
    gain_total = lax.psum(totals[5], "tensor")
    gateup_sum = (
        lax.psum_scatter(
            totals[3].reshape(width, -1).astype(jnp.bfloat16), "dp", scatter_dimension=0, tiled=True
        )
        .astype(jnp.float32)
        .reshape(-1, *totals[3].shape[1:])
    )
    down_sum = lax.psum_scatter(
        totals[4].astype(jnp.bfloat16), "dp", scatter_dimension=1, tiled=True
    ).astype(jnp.float32)
    query_low, keyval_low, output_low, _, _ = lax.optimization_barrier(
        (
            totals[0].astype(jnp.bfloat16),
            totals[1].reshape(width, -1).astype(jnp.bfloat16),
            totals[2].astype(jnp.bfloat16),
            gateup_sum,
            down_sum,
        )
    )
    summed = (
        lax.psum_scatter(
            lax.psum_scatter(query_low, "dp", scatter_dimension=0, tiled=True),
            "tensor",
            scatter_dimension=1,
            tiled=True,
        ).astype(jnp.float32),
        lax.psum_scatter(
            lax.psum_scatter(keyval_low, "dp", scatter_dimension=0, tiled=True),
            "tensor",
            scatter_dimension=1,
            tiled=True,
        )
        .astype(jnp.float32)
        .reshape(-1, keyval_heads, totals[1].shape[2]),
        lax.psum_scatter(
            lax.psum_scatter(output_low, "dp", scatter_dimension=1, tiled=True),
            "tensor",
            scatter_dimension=0,
            tiled=True,
        ).astype(jnp.float32),
        gateup_sum,
        down_sum,
        lax.psum_scatter(
            gain_total.astype(jnp.bfloat16), "dp", scatter_dimension=1, tiled=True
        ).astype(jnp.float32),
    )
    correction = 1.0 - moment_decay**STEP
    new_firsts = []
    new_seconds = []
    directions = []
    for grad, first, second in zip(summed, firsts, seconds):
        first_new = moment_decay * first + (1.0 - moment_decay) * grad
        second_new = moment_decay * second + (1.0 - moment_decay) * grad * grad
        direction = first_new / correction / (jnp.sqrt(second_new / correction) + ratio_eps)
        new_firsts.append(first_new)
        new_seconds.append(second_new)
        directions.append(direction)
    weight_part = jnp.concatenate(
        [
            jnp.stack([jnp.sum(masters[slot] * masters[slot]) for slot in range(5)]),
            jnp.sum(norm_gains * norm_gains, axis=1) / tensor_count,
        ]
    )
    update_part = jnp.concatenate(
        [
            jnp.stack([jnp.sum(directions[slot] * directions[slot]) for slot in range(5)]),
            jnp.sum(directions[5] * directions[5], axis=1) / tensor_count,
        ]
    )
    square_totals = lax.psum(jnp.stack([weight_part, update_part]), ("dp", "tensor"))
    trust_norms = jnp.sqrt(square_totals)
    ratio = trust_norms[0] / (trust_norms[1] + ratio_eps)
    new_weights = [masters[slot] - learn_rate * ratio[slot] * directions[slot] for slot in range(5)]
    new_gains = norm_gains - learn_rate * ratio[5:7][:, None] * directions[5]
    return (
        layer_output,
        input_grad,
        new_weights[0],
        new_weights[1],
        new_weights[2],
        new_weights[3],
        new_weights[4],
        new_gains,
        new_firsts[0],
        new_firsts[1],
        new_firsts[2],
        new_firsts[3],
        new_firsts[4],
        new_firsts[5],
        new_seconds[0],
        new_seconds[1],
        new_seconds[2],
        new_seconds[3],
        new_seconds[4],
        new_seconds[5],
        trust_norms,
    )


def solution(mesh):
    return jax.shard_map(
        per_device,
        mesh=mesh,
        in_specs=(
            P(None, "dp", "tensor", None),
            P(None, "dp", "tensor", None),
            P(None, "dp", None),
            P("dp", "tensor"),
            P("dp", "tensor", None),
            P("tensor", "dp"),
            P("dp", None, "tensor"),
            P("tensor", "dp"),
            P(None, "dp"),
            P("dp", "tensor"),
            P("dp", "tensor", None),
            P("tensor", "dp"),
            P("dp", None, "tensor"),
            P("tensor", "dp"),
            P(None, "dp"),
            P("dp", "tensor"),
            P("dp", "tensor", None),
            P("tensor", "dp"),
            P("dp", None, "tensor"),
            P("tensor", "dp"),
            P(None, "dp"),
        ),
        out_specs=(
            P(None, "dp", "tensor", None),
            P(None, "dp", "tensor", None),
            P("dp", "tensor"),
            P("dp", "tensor", None),
            P("tensor", "dp"),
            P("dp", None, "tensor"),
            P("tensor", "dp"),
            P(None, "dp"),
            P("dp", "tensor"),
            P("dp", "tensor", None),
            P("tensor", "dp"),
            P("dp", None, "tensor"),
            P("tensor", "dp"),
            P(None, "dp"),
            P("dp", "tensor"),
            P("dp", "tensor", None),
            P("tensor", "dp"),
            P("dp", None, "tensor"),
            P("tensor", "dp"),
            P(None, "dp"),
            P(),
        ),
        check_vma=False,
    )
```

```python
import jax
import jax.numpy as jnp
from jax import lax
from jax.sharding import PartitionSpec as P

HD = 64
PROMPT = 1024
CONTS = 3
STEP = 3


norm_eps = 1e-05
branch_scale = 0.22
score_scale = 0.015625
rope_base = 10000000.0
moment_decay = 0.5
learn_rate = 0.25
ratio_eps = 1e-06
masked_fill = -1e30


def layout(lengths, group_rows):
    row_index = jnp.arange(group_rows, dtype=jnp.int32)
    ends = jnp.cumsum(lengths)
    starts = ends - lengths
    within = row_index - PROMPT
    inside = (within[:, None] >= starts[None, :]) & (within[:, None] < ends[None, :])
    labels = jnp.arange(1, CONTS + 1, dtype=jnp.int32)
    segment = jnp.sum(jnp.where(inside, labels[None, :], 0), axis=1)
    offsets = jnp.sum(jnp.where(inside, starts[None, :], 0), axis=1)
    position = row_index - offsets
    causal = row_index[None, :] <= row_index[:, None]
    shared = (segment[None, :] == segment[:, None]) | (segment[None, :] == 0)
    return (causal & shared, position)


def rope_tables(position):
    half_size = HD // 2
    inverse = rope_base ** (-2.0 * jnp.arange(half_size, dtype=jnp.float32) / HD)
    angle = position.astype(jnp.float32)[:, None] * inverse[None, :]
    return (jnp.cos(angle)[:, None, :], jnp.sin(angle)[:, None, :])


def rotate(field, cos_table, sin_table):
    half_size = field.shape[-1] // 2
    first_half = field[..., :half_size]
    second_half = field[..., half_size:]
    return jnp.concatenate(
        [
            first_half * cos_table - second_half * sin_table,
            second_half * cos_table + first_half * sin_table,
        ],
        axis=-1,
    )


def rotate_back(grad_field, cos_table, sin_table):
    half_size = grad_field.shape[-1] // 2
    first_half = grad_field[..., :half_size]
    second_half = grad_field[..., half_size:]
    return jnp.concatenate(
        [
            first_half * cos_table + second_half * sin_table,
            second_half * cos_table - first_half * sin_table,
        ],
        axis=-1,
    )


def attend(queries, key_rows, values, visible, block_rows):
    outputs = []
    log_totals = []
    for block in range(2):
        begin = block * block_rows
        stop = begin + block_rows
        scores = (
            jnp.einsum(
                "ikrd,jkd->krij",
                queries[begin:stop],
                key_rows[:stop],
                preferred_element_type=jnp.float32,
            )
            * score_scale
        )
        scores = jnp.where(visible[begin:stop, :stop][None, None], scores, masked_fill)
        row_peak = jnp.max(scores, axis=-1, keepdims=True)
        shifted_exp = jnp.exp(scores - row_peak)
        row_total = jnp.sum(shifted_exp, axis=-1, keepdims=True)
        attn_prob = (shifted_exp / row_total).astype(jnp.bfloat16)
        outputs.append(
            jnp.einsum(
                "krij,jkd->ikrd", attn_prob, values[:stop], preferred_element_type=jnp.float32
            )
        )
        log_totals.append(row_peak + jnp.log(row_total))
    return (jnp.concatenate(outputs, axis=0), jnp.concatenate(log_totals, axis=2))


def attend_back(queries, key_rows, values, visible, log_totals, mixed_grad, block_rows):
    query_grads = []
    key_grad = jnp.zeros(key_rows.shape, jnp.float32)
    value_grad = jnp.zeros(values.shape, jnp.float32)
    for block in range(2):
        begin = block * block_rows
        stop = begin + block_rows
        query_block = queries[begin:stop]
        grad_block = mixed_grad[begin:stop]
        scores = (
            jnp.einsum(
                "ikrd,jkd->krij", query_block, key_rows[:stop], preferred_element_type=jnp.float32
            )
            * score_scale
        )
        attn_prob = jnp.where(
            visible[begin:stop, :stop][None, None],
            jnp.exp(scores - log_totals[:, :, begin:stop]),
            0.0,
        )
        prob_grad = jnp.einsum(
            "ikrd,jkd->krij", grad_block, values[:stop], preferred_element_type=jnp.float32
        )
        row_dot = jnp.sum(attn_prob * prob_grad, axis=-1, keepdims=True)
        score_grad = (attn_prob * (prob_grad - row_dot)).astype(jnp.bfloat16)
        query_grads.append(
            jnp.einsum(
                "krij,jkd->ikrd", score_grad, key_rows[:stop], preferred_element_type=jnp.float32
            )
            * score_scale
        )
        key_grad = key_grad.at[:stop].add(
            jnp.einsum(
                "krij,ikrd->jkd", score_grad, query_block, preferred_element_type=jnp.float32
            )
            * score_scale
        )
        value_grad = value_grad.at[:stop].add(
            jnp.einsum(
                "krij,ikrd->jkd",
                attn_prob.astype(jnp.bfloat16),
                grad_block,
                preferred_element_type=jnp.float32,
            )
        )
    return (jnp.concatenate(query_grads, axis=0), key_grad, value_grad)


def norm_back(upstream, normed_hat, scale_rows, gain_row):
    scaled = upstream * gain_row[None, :]
    through = scale_rows * (
        scaled - normed_hat * jnp.mean(scaled * normed_hat, axis=1, keepdims=True)
    )
    return (through, jnp.sum(upstream * normed_hat, axis=0))


def contract_rows(left, right):
    return lax.dot_general(
        left, right, (((0,), (0,)), ((), ())), preferred_element_type=jnp.float32
    )


def contract_cols(left, right):
    return lax.dot_general(
        left, right, (((1,), (1,)), ((), ())), preferred_element_type=jnp.float32
    )


def line_gather(x, count):
    place = lax.axis_index("tensor")
    rows = x.shape[0]
    out = jnp.zeros((count * rows,) + x.shape[1:], x.dtype)
    from_left = x
    from_right = x
    received = []
    for step in range(1, count):
        from_left = lax.ppermute(
            from_left, "tensor", [(i, i + 1) for i in range(step - 1, count - 1)]
        )
        from_right = lax.ppermute(
            from_right, "tensor", [(i, i - 1) for i in range(1, count - step + 1)]
        )
        received.append((from_left, place - step, place - step >= 0))
        received.append((from_right, place + step, place + step <= count - 1))
    for piece, slot, valid in received:
        out = lax.dynamic_update_slice_in_dim(out, piece, jnp.where(valid, slot, place) * rows, 0)
    return lax.dynamic_update_slice_in_dim(out, x, place * rows, 0)


def line_scatter(partial, count):
    place = lax.axis_index("tensor")
    rows = partial.shape[0] // count

    def chunk(index):
        return lax.dynamic_slice_in_dim(partial, jnp.clip(index, 0, count - 1) * rows, rows, 0)

    to_right = None
    to_left = None
    for step in range(1, count):
        send = chunk(place + count - step)
        if to_right is not None:
            send = send + to_right
        to_right = lax.ppermute(
            send.astype(jnp.bfloat16), "tensor", [(i, i + 1) for i in range(step)]
        ).astype(jnp.float32)
        send = chunk(place - count + step)
        if to_left is not None:
            send = send + to_left
        to_left = lax.ppermute(
            send.astype(jnp.bfloat16), "tensor", [(i, i - 1) for i in range(count - step, count)]
        ).astype(jnp.float32)
    total = chunk(place)
    if to_right is not None:
        total = total + to_right + to_left
    return total


def per_device(
    tokens,
    cotangent,
    cont_lengths,
    query_weight,
    keyval_weight,
    output_weight,
    gateup_weight,
    down_weight,
    norm_gains,
    query_moment,
    keyval_moment,
    output_moment,
    gateup_moment,
    down_moment,
    gains_moment,
    query_square,
    keyval_square,
    output_square,
    gateup_square,
    down_square,
    gains_square,
):
    masters = (query_weight, keyval_weight, output_weight, gateup_weight, down_weight, norm_gains)
    firsts = (query_moment, keyval_moment, output_moment, gateup_moment, down_moment, gains_moment)
    seconds = (query_square, keyval_square, output_square, gateup_square, down_square, gains_square)
    rounded = tuple((master.astype(jnp.bfloat16) for master in masters))
    gathered = (
        lax.all_gather(
            lax.all_gather(rounded[0], "tensor", axis=1, tiled=True), "dp", axis=0, tiled=True
        ),
        lax.all_gather(
            lax.all_gather(rounded[1], "tensor", axis=1, tiled=True), "dp", axis=0, tiled=True
        ),
        lax.all_gather(
            lax.all_gather(rounded[2], "tensor", axis=0, tiled=True), "dp", axis=1, tiled=True
        ),
        lax.all_gather(rounded[3], "dp", axis=0, tiled=True),
        lax.all_gather(rounded[4], "dp", axis=1, tiled=True),
        lax.all_gather(rounded[5], "dp", axis=1, tiled=True),
    )
    full_query, full_keyval, full_output, full_gateup, full_down, full_gains = gathered
    gain_values = full_gains.astype(jnp.float32)
    tensor_count = lax.axis_size("tensor")
    group_rows = tokens.shape[2] * tensor_count
    block_rows = group_rows // 2
    place = lax.axis_index("tensor")
    rows = tokens.shape[2]
    all_query_heads = full_query.shape[1] // HD
    keyval_heads = full_keyval.shape[1] // tensor_count
    query_heads = all_query_heads // tensor_count
    head_repeat = query_heads // keyval_heads

    def micro_step(token_rows, cot_rows, lengths):
        visible, position = layout(lengths, group_rows)
        cos_table, sin_table = rope_tables(position)
        cos_own, sin_own = rope_tables(lax.dynamic_slice_in_dim(position, place * rows, rows))
        start_rows = token_rows.astype(jnp.float32)
        scale_one = lax.rsqrt(jnp.mean(start_rows * start_rows, axis=1, keepdims=True) + norm_eps)
        hat_one = start_rows * scale_one
        normed_one = (hat_one * gain_values[0][None, :]).astype(jnp.bfloat16)
        query_raw = jnp.dot(normed_one, full_query, preferred_element_type=jnp.float32).reshape(
            rows, all_query_heads, HD
        )
        keyval_raw = jnp.einsum(
            "rd,dhk->rhk", normed_one, full_keyval, preferred_element_type=jnp.float32
        )
        queries_own = rotate(query_raw, cos_own, sin_own).astype(jnp.bfloat16)
        keyval_own = jnp.concatenate(
            [rotate(keyval_raw[:, :, :HD], cos_own, sin_own), keyval_raw[:, :, HD:]], axis=2
        ).astype(jnp.bfloat16)
        query_width = query_heads * HD
        projected = yield (
            "to_heads",
            jnp.concatenate(
                [
                    queries_own.reshape(rows, tensor_count, query_width),
                    keyval_own.reshape(rows, tensor_count, -1),
                ],
                axis=2,
            ),
        )
        projected = projected.reshape(group_rows, -1)
        queries = projected[:, :query_width].reshape(group_rows, keyval_heads, head_repeat, HD)
        keyval_rows = projected[:, query_width:].reshape(group_rows, keyval_heads, 2 * HD)
        key_rows = keyval_rows[:, :, :HD]
        values = keyval_rows[:, :, HD:]
        mixed_full, log_totals = attend(queries, key_rows, values, visible, block_rows)
        mixed = yield (
            "to_rows", mixed_full.astype(jnp.bfloat16).reshape(group_rows, query_width)
        )
        attn_branch = jnp.dot(mixed, full_output, preferred_element_type=jnp.float32)
        middle = start_rows + branch_scale * attn_branch
        scale_two = lax.rsqrt(jnp.mean(middle * middle, axis=1, keepdims=True) + norm_eps)
        hat_two = middle * scale_two
        normed_two = (hat_two * gain_values[1][None, :]).astype(jnp.bfloat16)
        rows_two = yield ("gather", normed_two)
        gate_up = jnp.einsum(
            "rd,dcf->rcf", rows_two, full_gateup, preferred_element_type=jnp.float32
        )
        gate_part = gate_up[:, 0]
        up_part = gate_up[:, 1]
        sigmoid_gate = jax.nn.sigmoid(gate_part)
        silu_gate = gate_part * sigmoid_gate
        hidden_state = (silu_gate * up_part).astype(jnp.bfloat16)
        upstream = cot_rows.astype(jnp.float32)
        ffn_grad = (branch_scale * upstream).astype(jnp.bfloat16)
        ffn_grad_all = yield ("gather", ffn_grad)
        ffn_branch = yield (
            "scatter", jnp.dot(hidden_state, full_down, preferred_element_type=jnp.float32)
        )
        layer_rows = (middle + branch_scale * ffn_branch).astype(jnp.bfloat16)
        grad_down = contract_rows(hidden_state, ffn_grad_all)
        hidden_grad = contract_cols(ffn_grad_all, full_down)
        gate_grad = hidden_grad * up_part * sigmoid_gate * (1.0 + gate_part * (1.0 - sigmoid_gate))
        up_grad = hidden_grad * silu_gate
        gateup_grad = jnp.stack([gate_grad, up_grad], axis=1).astype(jnp.bfloat16)
        grad_gateup = jnp.einsum(
            "rd,rcf->dcf", rows_two, gateup_grad, preferred_element_type=jnp.float32
        )
        normed_two_partial, grad_gateup, grad_down = lax.optimization_barrier(
            (
                jnp.einsum(
                    "rcf,dcf->rd", gateup_grad, full_gateup, preferred_element_type=jnp.float32
                ),
                grad_gateup,
                grad_down,
            )
        )
        normed_two_grad = yield ("scatter", normed_two_partial)
        middle_back, gain_two = norm_back(normed_two_grad, hat_two, scale_two, gain_values[1])
        middle_grad = upstream + middle_back
        attn_grad = (branch_scale * middle_grad).astype(jnp.bfloat16)
        mixed_grad_own, grad_output = lax.optimization_barrier(
            (
                contract_cols(attn_grad, full_output)
                .astype(jnp.bfloat16)
                .reshape(rows, tensor_count, query_width),
                contract_rows(mixed, attn_grad),
            )
        )
        mixed_grad = yield ("to_heads", mixed_grad_own)
        mixed_grad = mixed_grad.reshape(group_rows, keyval_heads, head_repeat, HD)
        query_grad, key_grad, value_grad = attend_back(
            queries, key_rows, values, visible, log_totals, mixed_grad, block_rows
        )
        raw_grads = yield (
            "to_rows",
            jnp.concatenate(
                [
                    rotate_back(
                        query_grad.reshape(group_rows, query_heads, HD), cos_table, sin_table
                    ).reshape(group_rows, query_width),
                    jnp.concatenate(
                        [rotate_back(key_grad, cos_table, sin_table), value_grad], axis=2
                    ).reshape(group_rows, -1),
                ],
                axis=1,
            ).astype(jnp.bfloat16),
        )
        raw_grads = raw_grads.reshape(rows, tensor_count, -1)
        query_raw_grad = raw_grads[:, :, :query_width].reshape(rows, all_query_heads * HD)
        keyval_raw_grad = raw_grads[:, :, query_width:].reshape(
            rows, tensor_count * keyval_heads, 2 * HD
        )
        grad_query = contract_rows(normed_one, query_raw_grad)
        grad_keyval = jnp.einsum(
            "rd,rhk->dhk", normed_one, keyval_raw_grad, preferred_element_type=jnp.float32
        )
        normed_one_grad = contract_cols(query_raw_grad, full_query) + jnp.einsum(
            "rhk,dhk->rd", keyval_raw_grad, full_keyval, preferred_element_type=jnp.float32
        )
        start_back, gain_one = norm_back(normed_one_grad, hat_one, scale_one, gain_values[0])
        input_rows = middle_grad + start_back
        gain_grad = jnp.stack([gain_one, gain_two])
        return (
            layer_rows,
            input_rows,
            (grad_query, grad_keyval, grad_output, grad_gateup, grad_down, gain_grad),
        )

    streams = [
        micro_step(tokens[index, 0], cotangent[index, 0], cont_lengths[index, 0])
        for index in range(tokens.shape[0])
    ]
    requests = [next(stream) for stream in streams]
    finished = [None] * len(streams)
    previous = None
    while any(result is None for result in finished):
        for index, stream in enumerate(streams):
            if finished[index] is not None:
                continue
            kind, value = requests[index]
            if previous is not None:
                previous, value = lax.optimization_barrier((previous, value))
            if kind == "gather":
                previous = line_gather(value, tensor_count)
            elif kind == "scatter":
                previous = line_scatter(value, tensor_count)
            elif kind == "to_heads":
                previous = lax.all_to_all(value, "tensor", 1, 0, tiled=True)
            else:
                previous = lax.all_to_all(value, "tensor", 0, 1, tiled=True)
            try:
                requests[index] = stream.send(previous)
            except StopIteration as stop:
                finished[index] = stop.value
    out_list = [result[0] for result in finished]
    grad_list = [result[1] for result in finished]
    totals = finished[0][2]
    for result in finished[1:]:
        totals = tuple((old_sum + new_term for old_sum, new_term in zip(totals, result[2])))
    layer_output = jnp.stack(out_list)[:, None]
    input_grad = jnp.stack(grad_list)[:, None]
    width = totals[0].shape[0]
    gain_total = lax.psum(totals[5], "tensor")
    gateup_sum = (
        lax.psum_scatter(
            totals[3].reshape(width, -1).astype(jnp.bfloat16), "dp", scatter_dimension=0, tiled=True
        )
        .astype(jnp.float32)
        .reshape(-1, *totals[3].shape[1:])
    )
    down_sum = lax.psum_scatter(
        totals[4].astype(jnp.bfloat16), "dp", scatter_dimension=1, tiled=True
    ).astype(jnp.float32)
    query_low, keyval_low, output_low, _, _ = lax.optimization_barrier(
        (
            totals[0].astype(jnp.bfloat16),
            totals[1].reshape(width, -1).astype(jnp.bfloat16),
            totals[2].astype(jnp.bfloat16),
            gateup_sum,
            down_sum,
        )
    )
    summed = (
        lax.psum_scatter(
            lax.psum_scatter(query_low, "dp", scatter_dimension=0, tiled=True),
            "tensor",
            scatter_dimension=1,
            tiled=True,
        ).astype(jnp.float32),
        lax.psum_scatter(
            lax.psum_scatter(keyval_low, "dp", scatter_dimension=0, tiled=True),
            "tensor",
            scatter_dimension=1,
            tiled=True,
        )
        .astype(jnp.float32)
        .reshape(-1, keyval_heads, totals[1].shape[2]),
        lax.psum_scatter(
            lax.psum_scatter(output_low, "dp", scatter_dimension=1, tiled=True),
            "tensor",
            scatter_dimension=0,
            tiled=True,
        ).astype(jnp.float32),
        gateup_sum,
        down_sum,
        lax.psum_scatter(
            gain_total.astype(jnp.bfloat16), "dp", scatter_dimension=1, tiled=True
        ).astype(jnp.float32),
    )
    correction = 1.0 - moment_decay**STEP
    new_firsts = []
    new_seconds = []
    directions = []
    for grad, first, second in zip(summed, firsts, seconds):
        first_new = moment_decay * first + (1.0 - moment_decay) * grad
        second_new = moment_decay * second + (1.0 - moment_decay) * grad * grad
        direction = first_new / correction / (jnp.sqrt(second_new / correction) + ratio_eps)
        new_firsts.append(first_new)
        new_seconds.append(second_new)
        directions.append(direction)
    weight_part = jnp.concatenate(
        [
            jnp.stack([jnp.sum(masters[slot] * masters[slot]) for slot in range(5)]),
            jnp.sum(norm_gains * norm_gains, axis=1) / tensor_count,
        ]
    )
    update_part = jnp.concatenate(
        [
            jnp.stack([jnp.sum(directions[slot] * directions[slot]) for slot in range(5)]),
            jnp.sum(directions[5] * directions[5], axis=1) / tensor_count,
        ]
    )
    square_totals = lax.psum(jnp.stack([weight_part, update_part]), ("dp", "tensor"))
    trust_norms = jnp.sqrt(square_totals)
    ratio = trust_norms[0] / (trust_norms[1] + ratio_eps)
    new_weights = [masters[slot] - learn_rate * ratio[slot] * directions[slot] for slot in range(5)]
    new_gains = norm_gains - learn_rate * ratio[5:7][:, None] * directions[5]
    return (
        layer_output,
        input_grad,
        new_weights[0],
        new_weights[1],
        new_weights[2],
        new_weights[3],
        new_weights[4],
        new_gains,
        new_firsts[0],
        new_firsts[1],
        new_firsts[2],
        new_firsts[3],
        new_firsts[4],
        new_firsts[5],
        new_seconds[0],
        new_seconds[1],
        new_seconds[2],
        new_seconds[3],
        new_seconds[4],
        new_seconds[5],
        trust_norms,
    )


def solution(mesh):
    return jax.shard_map(
        per_device,
        mesh=mesh,
        in_specs=(
            P(None, "dp", "tensor", None),
            P(None, "dp", "tensor", None),
            P(None, "dp", None),
            P("dp", "tensor"),
            P("dp", "tensor", None),
            P("tensor", "dp"),
            P("dp", None, "tensor"),
            P("tensor", "dp"),
            P(None, "dp"),
            P("dp", "tensor"),
            P("dp", "tensor", None),
            P("tensor", "dp"),
            P("dp", None, "tensor"),
            P("tensor", "dp"),
            P(None, "dp"),
            P("dp", "tensor"),
            P("dp", "tensor", None),
            P("tensor", "dp"),
            P("dp", None, "tensor"),
            P("tensor", "dp"),
            P(None, "dp"),
        ),
        out_specs=(
            P(None, "dp", "tensor", None),
            P(None, "dp", "tensor", None),
            P("dp", "tensor"),
            P("dp", "tensor", None),
            P("tensor", "dp"),
            P("dp", None, "tensor"),
            P("tensor", "dp"),
            P(None, "dp"),
            P("dp", "tensor"),
            P("dp", "tensor", None),
            P("tensor", "dp"),
            P("dp", None, "tensor"),
            P("tensor", "dp"),
            P(None, "dp"),
            P("dp", "tensor"),
            P("dp", "tensor", None),
            P("tensor", "dp"),
            P("dp", None, "tensor"),
            P("tensor", "dp"),
            P(None, "dp"),
            P(),
        ),
        check_vma=False,
    )
```

```python
import jax
import jax.numpy as jnp
from jax import lax
from jax.sharding import PartitionSpec as P

HD = 64
PROMPT = 1024
CONTS = 3
STEP = 3


norm_eps = 1e-05
branch_scale = 0.22
score_scale = 0.015625
rope_base = 10000000.0
moment_decay = 0.5
learn_rate = 0.25
ratio_eps = 1e-06
masked_fill = -1e30


def layout(lengths, group_rows):
    row_index = jnp.arange(group_rows, dtype=jnp.int32)
    ends = jnp.cumsum(lengths)
    starts = ends - lengths
    within = row_index - PROMPT
    inside = (within[:, None] >= starts[None, :]) & (within[:, None] < ends[None, :])
    labels = jnp.arange(1, CONTS + 1, dtype=jnp.int32)
    segment = jnp.sum(jnp.where(inside, labels[None, :], 0), axis=1)
    offsets = jnp.sum(jnp.where(inside, starts[None, :], 0), axis=1)
    position = row_index - offsets
    causal = row_index[None, :] <= row_index[:, None]
    shared = (segment[None, :] == segment[:, None]) | (segment[None, :] == 0)
    return (causal & shared, position)


def rope_tables(position):
    half_size = HD // 2
    inverse = rope_base ** (-2.0 * jnp.arange(half_size, dtype=jnp.float32) / HD)
    angle = position.astype(jnp.float32)[:, None] * inverse[None, :]
    return (jnp.cos(angle)[:, None, :], jnp.sin(angle)[:, None, :])


def rotate(field, cos_table, sin_table):
    half_size = field.shape[-1] // 2
    first_half = field[..., :half_size]
    second_half = field[..., half_size:]
    return jnp.concatenate(
        [
            first_half * cos_table - second_half * sin_table,
            second_half * cos_table + first_half * sin_table,
        ],
        axis=-1,
    )


def rotate_back(grad_field, cos_table, sin_table):
    half_size = grad_field.shape[-1] // 2
    first_half = grad_field[..., :half_size]
    second_half = grad_field[..., half_size:]
    return jnp.concatenate(
        [
            first_half * cos_table + second_half * sin_table,
            second_half * cos_table - first_half * sin_table,
        ],
        axis=-1,
    )


def attend(queries, key_rows, values, visible, block_rows):
    outputs = []
    log_totals = []
    for block in range(2):
        begin = block * block_rows
        stop = begin + block_rows
        scores = (
            jnp.einsum(
                "ikrd,jkd->krij",
                queries[begin:stop],
                key_rows[:stop],
                preferred_element_type=jnp.float32,
            )
            * score_scale
        )
        scores = jnp.where(visible[begin:stop, :stop][None, None], scores, masked_fill)
        row_peak = jnp.max(scores, axis=-1, keepdims=True)
        shifted_exp = jnp.exp(scores - row_peak)
        row_total = jnp.sum(shifted_exp, axis=-1, keepdims=True)
        attn_prob = (shifted_exp / row_total).astype(jnp.bfloat16)
        outputs.append(
            jnp.einsum(
                "krij,jkd->ikrd", attn_prob, values[:stop], preferred_element_type=jnp.float32
            )
        )
        log_totals.append(row_peak + jnp.log(row_total))
    return (jnp.concatenate(outputs, axis=0), jnp.concatenate(log_totals, axis=2))


def attend_back(queries, key_rows, values, visible, log_totals, mixed_grad, block_rows):
    query_grads = []
    key_grad = jnp.zeros(key_rows.shape, jnp.float32)
    value_grad = jnp.zeros(values.shape, jnp.float32)
    for block in range(2):
        begin = block * block_rows
        stop = begin + block_rows
        query_block = queries[begin:stop]
        grad_block = mixed_grad[begin:stop]
        scores = (
            jnp.einsum(
                "ikrd,jkd->krij", query_block, key_rows[:stop], preferred_element_type=jnp.float32
            )
            * score_scale
        )
        attn_prob = jnp.where(
            visible[begin:stop, :stop][None, None],
            jnp.exp(scores - log_totals[:, :, begin:stop]),
            0.0,
        )
        prob_grad = jnp.einsum(
            "ikrd,jkd->krij", grad_block, values[:stop], preferred_element_type=jnp.float32
        )
        row_dot = jnp.sum(attn_prob * prob_grad, axis=-1, keepdims=True)
        score_grad = (attn_prob * (prob_grad - row_dot)).astype(jnp.bfloat16)
        query_grads.append(
            jnp.einsum(
                "krij,jkd->ikrd", score_grad, key_rows[:stop], preferred_element_type=jnp.float32
            )
            * score_scale
        )
        key_grad = key_grad.at[:stop].add(
            jnp.einsum(
                "krij,ikrd->jkd", score_grad, query_block, preferred_element_type=jnp.float32
            )
            * score_scale
        )
        value_grad = value_grad.at[:stop].add(
            jnp.einsum(
                "krij,ikrd->jkd",
                attn_prob.astype(jnp.bfloat16),
                grad_block,
                preferred_element_type=jnp.float32,
            )
        )
    return (jnp.concatenate(query_grads, axis=0), key_grad, value_grad)


def norm_back(upstream, normed_hat, scale_rows, gain_row):
    scaled = upstream * gain_row[None, :]
    through = scale_rows * (
        scaled - normed_hat * jnp.mean(scaled * normed_hat, axis=1, keepdims=True)
    )
    return (through, jnp.sum(upstream * normed_hat, axis=0))


def contract_rows(left, right):
    return lax.dot_general(
        left, right, (((0,), (0,)), ((), ())), preferred_element_type=jnp.float32
    )


def contract_cols(left, right):
    return lax.dot_general(
        left, right, (((1,), (1,)), ((), ())), preferred_element_type=jnp.float32
    )


def line_gather(x, count):
    place = lax.axis_index("tensor")
    rows = x.shape[0]
    out = jnp.zeros((count * rows,) + x.shape[1:], x.dtype)
    from_left = x
    from_right = x
    received = []
    for step in range(1, count):
        from_left = lax.ppermute(
            from_left, "tensor", [(i, i + 1) for i in range(step - 1, count - 1)]
        )
        from_right = lax.ppermute(
            from_right, "tensor", [(i, i - 1) for i in range(1, count - step + 1)]
        )
        received.append((from_left, place - step, place - step >= 0))
        received.append((from_right, place + step, place + step <= count - 1))
    for piece, slot, valid in received:
        out = lax.dynamic_update_slice_in_dim(out, piece, jnp.where(valid, slot, place) * rows, 0)
    return lax.dynamic_update_slice_in_dim(out, x, place * rows, 0)


def line_scatter(partial, count):
    place = lax.axis_index("tensor")
    rows = partial.shape[0] // count

    def chunk(index):
        return lax.dynamic_slice_in_dim(partial, jnp.clip(index, 0, count - 1) * rows, rows, 0)

    to_right = None
    to_left = None
    for step in range(1, count):
        send = chunk(place + count - step)
        if to_right is not None:
            send = send + to_right
        to_right = lax.ppermute(
            send.astype(jnp.bfloat16), "tensor", [(i, i + 1) for i in range(step)]
        ).astype(jnp.float32)
        send = chunk(place - count + step)
        if to_left is not None:
            send = send + to_left
        to_left = lax.ppermute(
            send.astype(jnp.bfloat16), "tensor", [(i, i - 1) for i in range(count - step, count)]
        ).astype(jnp.float32)
    total = chunk(place)
    if to_right is not None:
        total = total + to_right + to_left
    return total


def per_device(
    tokens,
    cotangent,
    cont_lengths,
    query_weight,
    keyval_weight,
    output_weight,
    gateup_weight,
    down_weight,
    norm_gains,
    query_moment,
    keyval_moment,
    output_moment,
    gateup_moment,
    down_moment,
    gains_moment,
    query_square,
    keyval_square,
    output_square,
    gateup_square,
    down_square,
    gains_square,
):
    masters = (query_weight, keyval_weight, output_weight, gateup_weight, down_weight, norm_gains)
    firsts = (query_moment, keyval_moment, output_moment, gateup_moment, down_moment, gains_moment)
    seconds = (query_square, keyval_square, output_square, gateup_square, down_square, gains_square)
    rounded = tuple((master.astype(jnp.bfloat16) for master in masters))
    gathered = (
        lax.all_gather(
            lax.all_gather(rounded[0], "tensor", axis=1, tiled=True), "dp", axis=0, tiled=True
        ),
        lax.all_gather(
            lax.all_gather(rounded[1], "tensor", axis=1, tiled=True), "dp", axis=0, tiled=True
        ),
        lax.all_gather(
            lax.all_gather(rounded[2], "tensor", axis=0, tiled=True), "dp", axis=1, tiled=True
        ),
        lax.all_gather(rounded[3], "dp", axis=0, tiled=True),
        lax.all_gather(rounded[4], "dp", axis=1, tiled=True),
        lax.all_gather(rounded[5], "dp", axis=1, tiled=True),
    )
    full_query, full_keyval, full_output, full_gateup, full_down, full_gains = gathered
    gain_values = full_gains.astype(jnp.float32)
    tensor_count = lax.axis_size("tensor")
    group_rows = tokens.shape[2] * tensor_count
    block_rows = group_rows // 2
    place = lax.axis_index("tensor")
    rows = tokens.shape[2]
    all_query_heads = full_query.shape[1] // HD
    keyval_heads = full_keyval.shape[1] // tensor_count
    query_heads = all_query_heads // tensor_count
    head_repeat = query_heads // keyval_heads

    def micro_step(token_rows, cot_rows, lengths):
        visible, position = layout(lengths, group_rows)
        cos_table, sin_table = rope_tables(position)
        cos_own, sin_own = rope_tables(lax.dynamic_slice_in_dim(position, place * rows, rows))
        start_rows = token_rows.astype(jnp.float32)
        scale_one = lax.rsqrt(jnp.mean(start_rows * start_rows, axis=1, keepdims=True) + norm_eps)
        hat_one = start_rows * scale_one
        normed_one = (hat_one * gain_values[0][None, :]).astype(jnp.bfloat16)
        query_raw = jnp.dot(normed_one, full_query, preferred_element_type=jnp.float32).reshape(
            rows, all_query_heads, HD
        )
        keyval_raw = jnp.einsum(
            "rd,dhk->rhk", normed_one, full_keyval, preferred_element_type=jnp.float32
        )
        queries_own = rotate(query_raw, cos_own, sin_own).astype(jnp.bfloat16)
        keyval_own = jnp.concatenate(
            [rotate(keyval_raw[:, :, :HD], cos_own, sin_own), keyval_raw[:, :, HD:]], axis=2
        ).astype(jnp.bfloat16)
        query_width = query_heads * HD
        projected = yield (
            "to_heads",
            jnp.concatenate(
                [
                    queries_own.reshape(rows, tensor_count, query_width),
                    keyval_own.reshape(rows, tensor_count, -1),
                ],
                axis=2,
            ),
        )
        projected = projected.reshape(group_rows, -1)
        queries = projected[:, :query_width].reshape(group_rows, keyval_heads, head_repeat, HD)
        keyval_rows = projected[:, query_width:].reshape(group_rows, keyval_heads, 2 * HD)
        key_rows = keyval_rows[:, :, :HD]
        values = keyval_rows[:, :, HD:]
        mixed_full, log_totals = attend(queries, key_rows, values, visible, block_rows)
        mixed = yield (
            "to_rows", mixed_full.astype(jnp.bfloat16).reshape(group_rows, query_width)
        )
        attn_branch = jnp.dot(mixed, full_output, preferred_element_type=jnp.float32)
        middle = start_rows + branch_scale * attn_branch
        scale_two = lax.rsqrt(jnp.mean(middle * middle, axis=1, keepdims=True) + norm_eps)
        hat_two = middle * scale_two
        normed_two = (hat_two * gain_values[1][None, :]).astype(jnp.bfloat16)
        rows_two = yield ("gather", normed_two)
        gate_up = jnp.einsum(
            "rd,dcf->rcf", rows_two, full_gateup, preferred_element_type=jnp.float32
        )
        gate_part = gate_up[:, 0]
        up_part = gate_up[:, 1]
        sigmoid_gate = jax.nn.sigmoid(gate_part)
        silu_gate = gate_part * sigmoid_gate
        hidden_state = (silu_gate * up_part).astype(jnp.bfloat16)
        upstream = cot_rows.astype(jnp.float32)
        ffn_grad = (branch_scale * upstream).astype(jnp.bfloat16)
        ffn_grad_all = yield ("gather", ffn_grad)
        ffn_branch = yield (
            "scatter", jnp.dot(hidden_state, full_down, preferred_element_type=jnp.float32)
        )
        layer_rows = (middle + branch_scale * ffn_branch).astype(jnp.bfloat16)
        grad_down = contract_rows(hidden_state, ffn_grad_all)
        hidden_grad = contract_cols(ffn_grad_all, full_down)
        gate_grad = hidden_grad * up_part * sigmoid_gate * (1.0 + gate_part * (1.0 - sigmoid_gate))
        up_grad = hidden_grad * silu_gate
        gateup_grad = jnp.stack([gate_grad, up_grad], axis=1).astype(jnp.bfloat16)
        grad_gateup = jnp.einsum(
            "rd,rcf->dcf", rows_two, gateup_grad, preferred_element_type=jnp.float32
        )
        normed_two_grad = yield (
            "scatter",
            jnp.einsum(
                "rcf,dcf->rd", gateup_grad, full_gateup, preferred_element_type=jnp.float32
            ),
        )
        middle_back, gain_two = norm_back(normed_two_grad, hat_two, scale_two, gain_values[1])
        middle_grad = upstream + middle_back
        attn_grad = (branch_scale * middle_grad).astype(jnp.bfloat16)
        grad_output = contract_rows(mixed, attn_grad)
        mixed_grad_own, grad_gateup, grad_down = lax.optimization_barrier(
            (
                contract_cols(attn_grad, full_output)
                .astype(jnp.bfloat16)
                .reshape(rows, tensor_count, query_width),
                grad_gateup,
                grad_down,
            )
        )
        mixed_grad = yield ("to_heads", mixed_grad_own)
        mixed_grad = mixed_grad.reshape(group_rows, keyval_heads, head_repeat, HD)
        query_grad, key_grad, value_grad = attend_back(
            queries, key_rows, values, visible, log_totals, mixed_grad, block_rows
        )
        raw_grads = yield (
            "to_rows",
            jnp.concatenate(
                [
                    rotate_back(
                        query_grad.reshape(group_rows, query_heads, HD), cos_table, sin_table
                    ).reshape(group_rows, query_width),
                    jnp.concatenate(
                        [rotate_back(key_grad, cos_table, sin_table), value_grad], axis=2
                    ).reshape(group_rows, -1),
                ],
                axis=1,
            ).astype(jnp.bfloat16),
        )
        raw_grads = raw_grads.reshape(rows, tensor_count, -1)
        query_raw_grad = raw_grads[:, :, :query_width].reshape(rows, all_query_heads * HD)
        keyval_raw_grad = raw_grads[:, :, query_width:].reshape(
            rows, tensor_count * keyval_heads, 2 * HD
        )
        grad_query = contract_rows(normed_one, query_raw_grad)
        grad_keyval = jnp.einsum(
            "rd,rhk->dhk", normed_one, keyval_raw_grad, preferred_element_type=jnp.float32
        )
        normed_one_grad = contract_cols(query_raw_grad, full_query) + jnp.einsum(
            "rhk,dhk->rd", keyval_raw_grad, full_keyval, preferred_element_type=jnp.float32
        )
        start_back, gain_one = norm_back(normed_one_grad, hat_one, scale_one, gain_values[0])
        input_rows = middle_grad + start_back
        gain_grad = jnp.stack([gain_one, gain_two])
        return (
            layer_rows,
            input_rows,
            (grad_query, grad_keyval, grad_output, grad_gateup, grad_down, gain_grad),
        )

    streams = [
        micro_step(tokens[index, 0], cotangent[index, 0], cont_lengths[index, 0])
        for index in range(tokens.shape[0])
    ]
    requests = [next(stream) for stream in streams]
    finished = [None] * len(streams)
    previous = None
    while any(result is None for result in finished):
        for index, stream in enumerate(streams):
            if finished[index] is not None:
                continue
            kind, value = requests[index]
            if previous is not None:
                previous, value = lax.optimization_barrier((previous, value))
            if kind == "gather":
                previous = line_gather(value, tensor_count)
            elif kind == "scatter":
                previous = line_scatter(value, tensor_count)
            elif kind == "to_heads":
                previous = lax.all_to_all(value, "tensor", 1, 0, tiled=True)
            else:
                previous = lax.all_to_all(value, "tensor", 0, 1, tiled=True)
            try:
                requests[index] = stream.send(previous)
            except StopIteration as stop:
                finished[index] = stop.value
    out_list = [result[0] for result in finished]
    grad_list = [result[1] for result in finished]
    totals = finished[0][2]
    for result in finished[1:]:
        totals = tuple((old_sum + new_term for old_sum, new_term in zip(totals, result[2])))
    layer_output = jnp.stack(out_list)[:, None]
    input_grad = jnp.stack(grad_list)[:, None]
    width = totals[0].shape[0]
    gain_total = lax.psum(totals[5], "tensor")
    gateup_sum = (
        lax.psum_scatter(
            totals[3].reshape(width, -1).astype(jnp.bfloat16), "dp", scatter_dimension=0, tiled=True
        )
        .astype(jnp.float32)
        .reshape(-1, *totals[3].shape[1:])
    )
    down_sum = lax.psum_scatter(
        totals[4].astype(jnp.bfloat16), "dp", scatter_dimension=1, tiled=True
    ).astype(jnp.float32)
    query_low, keyval_low, output_low, _, _ = lax.optimization_barrier(
        (
            totals[0].astype(jnp.bfloat16),
            totals[1].reshape(width, -1).astype(jnp.bfloat16),
            totals[2].astype(jnp.bfloat16),
            gateup_sum,
            down_sum,
        )
    )
    summed = (
        lax.psum_scatter(
            lax.psum_scatter(query_low, "dp", scatter_dimension=0, tiled=True),
            "tensor",
            scatter_dimension=1,
            tiled=True,
        ).astype(jnp.float32),
        lax.psum_scatter(
            lax.psum_scatter(keyval_low, "dp", scatter_dimension=0, tiled=True),
            "tensor",
            scatter_dimension=1,
            tiled=True,
        )
        .astype(jnp.float32)
        .reshape(-1, keyval_heads, totals[1].shape[2]),
        lax.psum_scatter(
            lax.psum_scatter(output_low, "dp", scatter_dimension=1, tiled=True),
            "tensor",
            scatter_dimension=0,
            tiled=True,
        ).astype(jnp.float32),
        gateup_sum,
        down_sum,
        lax.psum_scatter(
            gain_total.astype(jnp.bfloat16), "dp", scatter_dimension=1, tiled=True
        ).astype(jnp.float32),
    )
    correction = 1.0 - moment_decay**STEP
    new_firsts = []
    new_seconds = []
    directions = []
    for grad, first, second in zip(summed, firsts, seconds):
        first_new = moment_decay * first + (1.0 - moment_decay) * grad
        second_new = moment_decay * second + (1.0 - moment_decay) * grad * grad
        direction = first_new / correction / (jnp.sqrt(second_new / correction) + ratio_eps)
        new_firsts.append(first_new)
        new_seconds.append(second_new)
        directions.append(direction)
    weight_part = jnp.concatenate(
        [
            jnp.stack([jnp.sum(masters[slot] * masters[slot]) for slot in range(5)]),
            jnp.sum(norm_gains * norm_gains, axis=1) / tensor_count,
        ]
    )
    update_part = jnp.concatenate(
        [
            jnp.stack([jnp.sum(directions[slot] * directions[slot]) for slot in range(5)]),
            jnp.sum(directions[5] * directions[5], axis=1) / tensor_count,
        ]
    )
    square_totals = lax.psum(jnp.stack([weight_part, update_part]), ("dp", "tensor"))
    trust_norms = jnp.sqrt(square_totals)
    ratio = trust_norms[0] / (trust_norms[1] + ratio_eps)
    new_weights = [masters[slot] - learn_rate * ratio[slot] * directions[slot] for slot in range(5)]
    new_gains = norm_gains - learn_rate * ratio[5:7][:, None] * directions[5]
    return (
        layer_output,
        input_grad,
        new_weights[0],
        new_weights[1],
        new_weights[2],
        new_weights[3],
        new_weights[4],
        new_gains,
        new_firsts[0],
        new_firsts[1],
        new_firsts[2],
        new_firsts[3],
        new_firsts[4],
        new_firsts[5],
        new_seconds[0],
        new_seconds[1],
        new_seconds[2],
        new_seconds[3],
        new_seconds[4],
        new_seconds[5],
        trust_norms,
    )


def solution(mesh):
    return jax.shard_map(
        per_device,
        mesh=mesh,
        in_specs=(
            P(None, "dp", "tensor", None),
            P(None, "dp", "tensor", None),
            P(None, "dp", None),
            P("dp", "tensor"),
            P("dp", "tensor", None),
            P("tensor", "dp"),
            P("dp", None, "tensor"),
            P("tensor", "dp"),
            P(None, "dp"),
            P("dp", "tensor"),
            P("dp", "tensor", None),
            P("tensor", "dp"),
            P("dp", None, "tensor"),
            P("tensor", "dp"),
            P(None, "dp"),
            P("dp", "tensor"),
            P("dp", "tensor", None),
            P("tensor", "dp"),
            P("dp", None, "tensor"),
            P("tensor", "dp"),
            P(None, "dp"),
        ),
        out_specs=(
            P(None, "dp", "tensor", None),
            P(None, "dp", "tensor", None),
            P("dp", "tensor"),
            P("dp", "tensor", None),
            P("tensor", "dp"),
            P("dp", None, "tensor"),
            P("tensor", "dp"),
            P(None, "dp"),
            P("dp", "tensor"),
            P("dp", "tensor", None),
            P("tensor", "dp"),
            P("dp", None, "tensor"),
            P("tensor", "dp"),
            P(None, "dp"),
            P("dp", "tensor"),
            P("dp", "tensor", None),
            P("tensor", "dp"),
            P("dp", None, "tensor"),
            P("tensor", "dp"),
            P(None, "dp"),
            P(),
        ),
        check_vma=False,
    )
```

```python
import jax
import jax.numpy as jnp
from jax import lax
from jax.sharding import PartitionSpec as P

HD = 64
PROMPT = 1024
CONTS = 3
STEP = 3


norm_eps = 1e-05
branch_scale = 0.22
score_scale = 0.015625
rope_base = 10000000.0
moment_decay = 0.5
learn_rate = 0.25
ratio_eps = 1e-06
masked_fill = -1e30


def layout(lengths, group_rows):
    row_index = jnp.arange(group_rows, dtype=jnp.int32)
    ends = jnp.cumsum(lengths)
    starts = ends - lengths
    within = row_index - PROMPT
    inside = (within[:, None] >= starts[None, :]) & (within[:, None] < ends[None, :])
    labels = jnp.arange(1, CONTS + 1, dtype=jnp.int32)
    segment = jnp.sum(jnp.where(inside, labels[None, :], 0), axis=1)
    offsets = jnp.sum(jnp.where(inside, starts[None, :], 0), axis=1)
    position = row_index - offsets
    causal = row_index[None, :] <= row_index[:, None]
    shared = (segment[None, :] == segment[:, None]) | (segment[None, :] == 0)
    return (causal & shared, position)


def rope_tables(position):
    half_size = HD // 2
    inverse = rope_base ** (-2.0 * jnp.arange(half_size, dtype=jnp.float32) / HD)
    angle = position.astype(jnp.float32)[:, None] * inverse[None, :]
    return (jnp.cos(angle)[:, None, :], jnp.sin(angle)[:, None, :])


def rotate(field, cos_table, sin_table):
    half_size = field.shape[-1] // 2
    first_half = field[..., :half_size]
    second_half = field[..., half_size:]
    return jnp.concatenate(
        [
            first_half * cos_table - second_half * sin_table,
            second_half * cos_table + first_half * sin_table,
        ],
        axis=-1,
    )


def rotate_back(grad_field, cos_table, sin_table):
    half_size = grad_field.shape[-1] // 2
    first_half = grad_field[..., :half_size]
    second_half = grad_field[..., half_size:]
    return jnp.concatenate(
        [
            first_half * cos_table + second_half * sin_table,
            second_half * cos_table - first_half * sin_table,
        ],
        axis=-1,
    )


def attend(queries, key_rows, values, visible, block_rows):
    outputs = []
    log_totals = []
    for block in range(2):
        begin = block * block_rows
        stop = begin + block_rows
        scores = (
            jnp.einsum(
                "ikrd,jkd->krij",
                queries[begin:stop],
                key_rows[:stop],
                preferred_element_type=jnp.float32,
            )
            * score_scale
        )
        scores = jnp.where(visible[begin:stop, :stop][None, None], scores, masked_fill)
        row_peak = jnp.max(scores, axis=-1, keepdims=True)
        shifted_exp = jnp.exp(scores - row_peak)
        row_total = jnp.sum(shifted_exp, axis=-1, keepdims=True)
        attn_prob = (shifted_exp / row_total).astype(jnp.bfloat16)
        outputs.append(
            jnp.einsum(
                "krij,jkd->ikrd", attn_prob, values[:stop], preferred_element_type=jnp.float32
            )
        )
        log_totals.append(row_peak + jnp.log(row_total))
    return (jnp.concatenate(outputs, axis=0), jnp.concatenate(log_totals, axis=2))


def attend_back(queries, key_rows, values, visible, log_totals, mixed_grad, block_rows):
    query_grads = []
    key_grad = jnp.zeros(key_rows.shape, jnp.float32)
    value_grad = jnp.zeros(values.shape, jnp.float32)
    for block in range(2):
        begin = block * block_rows
        stop = begin + block_rows
        query_block = queries[begin:stop]
        grad_block = mixed_grad[begin:stop]
        scores = (
            jnp.einsum(
                "ikrd,jkd->krij", query_block, key_rows[:stop], preferred_element_type=jnp.float32
            )
            * score_scale
        )
        attn_prob = jnp.where(
            visible[begin:stop, :stop][None, None],
            jnp.exp(scores - log_totals[:, :, begin:stop]),
            0.0,
        )
        prob_grad = jnp.einsum(
            "ikrd,jkd->krij", grad_block, values[:stop], preferred_element_type=jnp.float32
        )
        row_dot = jnp.sum(attn_prob * prob_grad, axis=-1, keepdims=True)
        score_grad = (attn_prob * (prob_grad - row_dot)).astype(jnp.bfloat16)
        query_grads.append(
            jnp.einsum(
                "krij,jkd->ikrd", score_grad, key_rows[:stop], preferred_element_type=jnp.float32
            )
            * score_scale
        )
        key_grad = key_grad.at[:stop].add(
            jnp.einsum(
                "krij,ikrd->jkd", score_grad, query_block, preferred_element_type=jnp.float32
            )
            * score_scale
        )
        value_grad = value_grad.at[:stop].add(
            jnp.einsum(
                "krij,ikrd->jkd",
                attn_prob.astype(jnp.bfloat16),
                grad_block,
                preferred_element_type=jnp.float32,
            )
        )
    return (jnp.concatenate(query_grads, axis=0), key_grad, value_grad)


def norm_back(upstream, normed_hat, scale_rows, gain_row):
    scaled = upstream * gain_row[None, :]
    through = scale_rows * (
        scaled - normed_hat * jnp.mean(scaled * normed_hat, axis=1, keepdims=True)
    )
    return (through, jnp.sum(upstream * normed_hat, axis=0))


def contract_rows(left, right):
    return lax.dot_general(
        left, right, (((0,), (0,)), ((), ())), preferred_element_type=jnp.float32
    )


def contract_cols(left, right):
    return lax.dot_general(
        left, right, (((1,), (1,)), ((), ())), preferred_element_type=jnp.float32
    )


def line_gather(x, count):
    place = lax.axis_index("tensor")
    rows = x.shape[0]
    out = jnp.zeros((count * rows,) + x.shape[1:], x.dtype)
    from_left = x
    from_right = x
    received = []
    for step in range(1, count):
        from_left = lax.ppermute(
            from_left, "tensor", [(i, i + 1) for i in range(step - 1, count - 1)]
        )
        from_right = lax.ppermute(
            from_right, "tensor", [(i, i - 1) for i in range(1, count - step + 1)]
        )
        received.append((from_left, place - step, place - step >= 0))
        received.append((from_right, place + step, place + step <= count - 1))
    for piece, slot, valid in received:
        out = lax.dynamic_update_slice_in_dim(out, piece, jnp.where(valid, slot, place) * rows, 0)
    return lax.dynamic_update_slice_in_dim(out, x, place * rows, 0)


def line_scatter(partial, count):
    place = lax.axis_index("tensor")
    rows = partial.shape[0] // count

    def chunk(index):
        return lax.dynamic_slice_in_dim(partial, jnp.clip(index, 0, count - 1) * rows, rows, 0)

    to_right = None
    to_left = None
    for step in range(1, count):
        send = chunk(place + count - step)
        if to_right is not None:
            send = send + to_right
        to_right = lax.ppermute(
            send.astype(jnp.bfloat16), "tensor", [(i, i + 1) for i in range(step)]
        ).astype(jnp.float32)
        send = chunk(place - count + step)
        if to_left is not None:
            send = send + to_left
        to_left = lax.ppermute(
            send.astype(jnp.bfloat16), "tensor", [(i, i - 1) for i in range(count - step, count)]
        ).astype(jnp.float32)
    total = chunk(place)
    if to_right is not None:
        total = total + to_right + to_left
    return total


def per_device(
    tokens,
    cotangent,
    cont_lengths,
    query_weight,
    keyval_weight,
    output_weight,
    gateup_weight,
    down_weight,
    norm_gains,
    query_moment,
    keyval_moment,
    output_moment,
    gateup_moment,
    down_moment,
    gains_moment,
    query_square,
    keyval_square,
    output_square,
    gateup_square,
    down_square,
    gains_square,
):
    masters = (query_weight, keyval_weight, output_weight, gateup_weight, down_weight, norm_gains)
    firsts = (query_moment, keyval_moment, output_moment, gateup_moment, down_moment, gains_moment)
    seconds = (query_square, keyval_square, output_square, gateup_square, down_square, gains_square)
    rounded = tuple((master.astype(jnp.bfloat16) for master in masters))
    gathered = (
        lax.all_gather(rounded[0], "dp", axis=0, tiled=True),
        lax.all_gather(rounded[1], "dp", axis=0, tiled=True),
        lax.all_gather(rounded[2], "dp", axis=1, tiled=True),
        lax.all_gather(rounded[3], "dp", axis=0, tiled=True),
        lax.all_gather(rounded[4], "dp", axis=1, tiled=True),
        lax.all_gather(rounded[5], "dp", axis=1, tiled=True),
    )
    full_query, full_keyval, full_output, full_gateup, full_down, full_gains = gathered
    gain_values = full_gains.astype(jnp.float32)
    tensor_count = lax.axis_size("tensor")
    group_rows = tokens.shape[2] * tensor_count
    block_rows = group_rows // 2
    keyval_heads = full_keyval.shape[1]
    query_heads = full_query.shape[1] // HD
    head_repeat = query_heads // keyval_heads

    def micro_step(token_rows, cot_rows, lengths):
        visible, position = layout(lengths, group_rows)
        cos_table, sin_table = rope_tables(position)
        start_rows = token_rows.astype(jnp.float32)
        scale_one = lax.rsqrt(jnp.mean(start_rows * start_rows, axis=1, keepdims=True) + norm_eps)
        hat_one = start_rows * scale_one
        normed_one = (hat_one * gain_values[0][None, :]).astype(jnp.bfloat16)
        rows_one = yield ("gather", normed_one)
        query_raw = jnp.dot(rows_one, full_query, preferred_element_type=jnp.float32).reshape(
            group_rows, query_heads, HD
        )
        keyval_raw = jnp.einsum(
            "rd,dhk->rhk", rows_one, full_keyval, preferred_element_type=jnp.float32
        )
        queries = (
            rotate(query_raw, cos_table, sin_table)
            .astype(jnp.bfloat16)
            .reshape(group_rows, keyval_heads, head_repeat, HD)
        )
        key_rows = rotate(keyval_raw[:, :, :HD], cos_table, sin_table).astype(jnp.bfloat16)
        values = keyval_raw[:, :, HD:].astype(jnp.bfloat16)
        mixed_full, log_totals = attend(queries, key_rows, values, visible, block_rows)
        mixed = mixed_full.astype(jnp.bfloat16).reshape(group_rows, query_heads * HD)
        attn_branch = yield (
            "scatter", jnp.dot(mixed, full_output, preferred_element_type=jnp.float32)
        )
        middle = start_rows + branch_scale * attn_branch
        scale_two = lax.rsqrt(jnp.mean(middle * middle, axis=1, keepdims=True) + norm_eps)
        hat_two = middle * scale_two
        normed_two = (hat_two * gain_values[1][None, :]).astype(jnp.bfloat16)
        rows_two = yield ("gather", normed_two)
        gate_up = jnp.einsum(
            "rd,dcf->rcf", rows_two, full_gateup, preferred_element_type=jnp.float32
        )
        gate_part = gate_up[:, 0]
        up_part = gate_up[:, 1]
        sigmoid_gate = jax.nn.sigmoid(gate_part)
        silu_gate = gate_part * sigmoid_gate
        hidden_state = (silu_gate * up_part).astype(jnp.bfloat16)
        upstream = cot_rows.astype(jnp.float32)
        ffn_grad = (branch_scale * upstream).astype(jnp.bfloat16)
        ffn_grad_all = yield ("gather", ffn_grad)
        ffn_branch = yield (
            "scatter", jnp.dot(hidden_state, full_down, preferred_element_type=jnp.float32)
        )
        layer_rows = (middle + branch_scale * ffn_branch).astype(jnp.bfloat16)
        grad_down = contract_rows(hidden_state, ffn_grad_all)
        hidden_grad = contract_cols(ffn_grad_all, full_down)
        gate_grad = hidden_grad * up_part * sigmoid_gate * (1.0 + gate_part * (1.0 - sigmoid_gate))
        up_grad = hidden_grad * silu_gate
        gateup_grad = jnp.stack([gate_grad, up_grad], axis=1).astype(jnp.bfloat16)
        grad_gateup = jnp.einsum(
            "rd,rcf->dcf", rows_two, gateup_grad, preferred_element_type=jnp.float32
        )
        normed_two_grad = yield (
            "scatter",
            jnp.einsum(
                "rcf,dcf->rd", gateup_grad, full_gateup, preferred_element_type=jnp.float32
            ),
        )
        middle_back, gain_two = norm_back(normed_two_grad, hat_two, scale_two, gain_values[1])
        middle_grad = upstream + middle_back
        attn_grad = (branch_scale * middle_grad).astype(jnp.bfloat16)
        attn_grad_all = yield ("gather", attn_grad)
        grad_output = contract_rows(mixed, attn_grad_all)
        mixed_grad = (
            contract_cols(attn_grad_all, full_output)
            .astype(jnp.bfloat16)
            .reshape(group_rows, keyval_heads, head_repeat, HD)
        )
        query_grad, key_grad, value_grad = attend_back(
            queries, key_rows, values, visible, log_totals, mixed_grad, block_rows
        )
        query_raw_grad = (
            rotate_back(query_grad.reshape(group_rows, query_heads, HD), cos_table, sin_table)
            .astype(jnp.bfloat16)
            .reshape(group_rows, query_heads * HD)
        )
        keyval_raw_grad = jnp.concatenate(
            [rotate_back(key_grad, cos_table, sin_table), value_grad], axis=2
        ).astype(jnp.bfloat16)
        grad_query = contract_rows(rows_one, query_raw_grad)
        grad_keyval = jnp.einsum(
            "rd,rhk->dhk", rows_one, keyval_raw_grad, preferred_element_type=jnp.float32
        )
        normed_one_grad = yield (
            "scatter",
            contract_cols(query_raw_grad, full_query)
            + jnp.einsum(
                "rhk,dhk->rd", keyval_raw_grad, full_keyval, preferred_element_type=jnp.float32
            ),
        )
        start_back, gain_one = norm_back(normed_one_grad, hat_one, scale_one, gain_values[0])
        input_rows = middle_grad + start_back
        gain_grad = jnp.stack([gain_one, gain_two])
        return (
            layer_rows,
            input_rows,
            (grad_query, grad_keyval, grad_output, grad_gateup, grad_down, gain_grad),
        )

    streams = [
        micro_step(tokens[index, 0], cotangent[index, 0], cont_lengths[index, 0])
        for index in range(tokens.shape[0])
    ]
    requests = [next(stream) for stream in streams]
    finished = [None] * len(streams)
    previous = None
    while any(result is None for result in finished):
        for index, stream in enumerate(streams):
            if finished[index] is not None:
                continue
            kind, value = requests[index]
            if previous is not None:
                previous, value = lax.optimization_barrier((previous, value))
            if kind == "gather":
                previous = line_gather(value, tensor_count)
            else:
                previous = lax.psum_scatter(
                    value.astype(jnp.bfloat16), "tensor", scatter_dimension=0, tiled=True
                ).astype(jnp.float32)
            try:
                requests[index] = stream.send(previous)
            except StopIteration as stop:
                finished[index] = stop.value
    out_list = [result[0] for result in finished]
    grad_list = [result[1] for result in finished]
    totals = finished[0][2]
    for result in finished[1:]:
        totals = tuple((old_sum + new_term for old_sum, new_term in zip(totals, result[2])))
    layer_output = jnp.stack(out_list)[:, None]
    input_grad = jnp.stack(grad_list)[:, None]
    width = totals[0].shape[0]
    gain_total = lax.psum(totals[5], "tensor")
    summed = (
        lax.psum_scatter(
            totals[0].astype(jnp.bfloat16), "dp", scatter_dimension=0, tiled=True
        ).astype(jnp.float32),
        lax.psum_scatter(
            totals[1].reshape(width, -1).astype(jnp.bfloat16), "dp", scatter_dimension=0, tiled=True
        )
        .astype(jnp.float32)
        .reshape(-1, *totals[1].shape[1:]),
        lax.psum_scatter(
            totals[2].astype(jnp.bfloat16), "dp", scatter_dimension=1, tiled=True
        ).astype(jnp.float32),
        lax.psum_scatter(
            totals[3].reshape(width, -1).astype(jnp.bfloat16), "dp", scatter_dimension=0, tiled=True
        )
        .astype(jnp.float32)
        .reshape(-1, *totals[3].shape[1:]),
        lax.psum_scatter(
            totals[4].astype(jnp.bfloat16), "dp", scatter_dimension=1, tiled=True
        ).astype(jnp.float32),
        lax.psum_scatter(
            gain_total.astype(jnp.bfloat16), "dp", scatter_dimension=1, tiled=True
        ).astype(jnp.float32),
    )
    correction = 1.0 - moment_decay**STEP
    new_firsts = []
    new_seconds = []
    directions = []
    for grad, first, second in zip(summed, firsts, seconds):
        first_new = moment_decay * first + (1.0 - moment_decay) * grad
        second_new = moment_decay * second + (1.0 - moment_decay) * grad * grad
        direction = first_new / correction / (jnp.sqrt(second_new / correction) + ratio_eps)
        new_firsts.append(first_new)
        new_seconds.append(second_new)
        directions.append(direction)
    weight_part = jnp.concatenate(
        [
            jnp.stack([jnp.sum(masters[slot] * masters[slot]) for slot in range(5)]),
            jnp.sum(norm_gains * norm_gains, axis=1) / tensor_count,
        ]
    )
    update_part = jnp.concatenate(
        [
            jnp.stack([jnp.sum(directions[slot] * directions[slot]) for slot in range(5)]),
            jnp.sum(directions[5] * directions[5], axis=1) / tensor_count,
        ]
    )
    square_totals = lax.psum(jnp.stack([weight_part, update_part]), ("dp", "tensor"))
    trust_norms = jnp.sqrt(square_totals)
    ratio = trust_norms[0] / (trust_norms[1] + ratio_eps)
    new_weights = [masters[slot] - learn_rate * ratio[slot] * directions[slot] for slot in range(5)]
    new_gains = norm_gains - learn_rate * ratio[5:7][:, None] * directions[5]
    return (
        layer_output,
        input_grad,
        new_weights[0],
        new_weights[1],
        new_weights[2],
        new_weights[3],
        new_weights[4],
        new_gains,
        new_firsts[0],
        new_firsts[1],
        new_firsts[2],
        new_firsts[3],
        new_firsts[4],
        new_firsts[5],
        new_seconds[0],
        new_seconds[1],
        new_seconds[2],
        new_seconds[3],
        new_seconds[4],
        new_seconds[5],
        trust_norms,
    )


def solution(mesh):
    return jax.shard_map(
        per_device,
        mesh=mesh,
        in_specs=(
            P(None, "dp", "tensor", None),
            P(None, "dp", "tensor", None),
            P(None, "dp", None),
            P("dp", "tensor"),
            P("dp", "tensor", None),
            P("tensor", "dp"),
            P("dp", None, "tensor"),
            P("tensor", "dp"),
            P(None, "dp"),
            P("dp", "tensor"),
            P("dp", "tensor", None),
            P("tensor", "dp"),
            P("dp", None, "tensor"),
            P("tensor", "dp"),
            P(None, "dp"),
            P("dp", "tensor"),
            P("dp", "tensor", None),
            P("tensor", "dp"),
            P("dp", None, "tensor"),
            P("tensor", "dp"),
            P(None, "dp"),
        ),
        out_specs=(
            P(None, "dp", "tensor", None),
            P(None, "dp", "tensor", None),
            P("dp", "tensor"),
            P("dp", "tensor", None),
            P("tensor", "dp"),
            P("dp", None, "tensor"),
            P("tensor", "dp"),
            P(None, "dp"),
            P("dp", "tensor"),
            P("dp", "tensor", None),
            P("tensor", "dp"),
            P("dp", None, "tensor"),
            P("tensor", "dp"),
            P(None, "dp"),
            P("dp", "tensor"),
            P("dp", "tensor", None),
            P("tensor", "dp"),
            P("dp", None, "tensor"),
            P("tensor", "dp"),
            P(None, "dp"),
            P(),
        ),
        check_vma=False,
    )
```

```python
import jax
import jax.numpy as jnp
from jax import lax
from jax.sharding import PartitionSpec as P

HD = 64
PROMPT = 1024
CONTS = 3
STEP = 3


norm_eps = 1e-05
branch_scale = 0.22
score_scale = 0.015625
rope_base = 10000000.0
moment_decay = 0.5
learn_rate = 0.25
ratio_eps = 1e-06
masked_fill = -1e30


def layout(lengths, group_rows):
    row_index = jnp.arange(group_rows, dtype=jnp.int32)
    ends = jnp.cumsum(lengths)
    starts = ends - lengths
    within = row_index - PROMPT
    inside = (within[:, None] >= starts[None, :]) & (within[:, None] < ends[None, :])
    labels = jnp.arange(1, CONTS + 1, dtype=jnp.int32)
    segment = jnp.sum(jnp.where(inside, labels[None, :], 0), axis=1)
    offsets = jnp.sum(jnp.where(inside, starts[None, :], 0), axis=1)
    position = row_index - offsets
    causal = row_index[None, :] <= row_index[:, None]
    shared = (segment[None, :] == segment[:, None]) | (segment[None, :] == 0)
    return (causal & shared, position)


def rope_tables(position):
    half_size = HD // 2
    inverse = rope_base ** (-2.0 * jnp.arange(half_size, dtype=jnp.float32) / HD)
    angle = position.astype(jnp.float32)[:, None] * inverse[None, :]
    return (jnp.cos(angle)[:, None, :], jnp.sin(angle)[:, None, :])


def rotate(field, cos_table, sin_table):
    half_size = field.shape[-1] // 2
    first_half = field[..., :half_size]
    second_half = field[..., half_size:]
    return jnp.concatenate(
        [
            first_half * cos_table - second_half * sin_table,
            second_half * cos_table + first_half * sin_table,
        ],
        axis=-1,
    )


def rotate_back(grad_field, cos_table, sin_table):
    half_size = grad_field.shape[-1] // 2
    first_half = grad_field[..., :half_size]
    second_half = grad_field[..., half_size:]
    return jnp.concatenate(
        [
            first_half * cos_table + second_half * sin_table,
            second_half * cos_table - first_half * sin_table,
        ],
        axis=-1,
    )


def attend(queries, key_rows, values, visible, block_rows):
    outputs = []
    log_totals = []
    for block in range(2):
        begin = block * block_rows
        stop = begin + block_rows
        scores = (
            jnp.einsum(
                "ikrd,jkd->krij",
                queries[begin:stop],
                key_rows[:stop],
                preferred_element_type=jnp.float32,
            )
            * score_scale
        )
        scores = jnp.where(visible[begin:stop, :stop][None, None], scores, masked_fill)
        row_peak = jnp.max(scores, axis=-1, keepdims=True)
        shifted_exp = jnp.exp(scores - row_peak)
        row_total = jnp.sum(shifted_exp, axis=-1, keepdims=True)
        attn_prob = (shifted_exp / row_total).astype(jnp.bfloat16)
        outputs.append(
            jnp.einsum(
                "krij,jkd->ikrd", attn_prob, values[:stop], preferred_element_type=jnp.float32
            )
        )
        log_totals.append(row_peak + jnp.log(row_total))
    return (jnp.concatenate(outputs, axis=0), jnp.concatenate(log_totals, axis=2))


def attend_back(queries, key_rows, values, visible, log_totals, mixed_grad, block_rows):
    query_grads = []
    key_grad = jnp.zeros(key_rows.shape, jnp.float32)
    value_grad = jnp.zeros(values.shape, jnp.float32)
    for block in range(2):
        begin = block * block_rows
        stop = begin + block_rows
        query_block = queries[begin:stop]
        grad_block = mixed_grad[begin:stop]
        scores = (
            jnp.einsum(
                "ikrd,jkd->krij", query_block, key_rows[:stop], preferred_element_type=jnp.float32
            )
            * score_scale
        )
        attn_prob = jnp.where(
            visible[begin:stop, :stop][None, None],
            jnp.exp(scores - log_totals[:, :, begin:stop]),
            0.0,
        )
        prob_grad = jnp.einsum(
            "ikrd,jkd->krij", grad_block, values[:stop], preferred_element_type=jnp.float32
        )
        row_dot = jnp.sum(attn_prob * prob_grad, axis=-1, keepdims=True)
        score_grad = (attn_prob * (prob_grad - row_dot)).astype(jnp.bfloat16)
        query_grads.append(
            jnp.einsum(
                "krij,jkd->ikrd", score_grad, key_rows[:stop], preferred_element_type=jnp.float32
            )
            * score_scale
        )
        key_grad = key_grad.at[:stop].add(
            jnp.einsum(
                "krij,ikrd->jkd", score_grad, query_block, preferred_element_type=jnp.float32
            )
            * score_scale
        )
        value_grad = value_grad.at[:stop].add(
            jnp.einsum(
                "krij,ikrd->jkd",
                attn_prob.astype(jnp.bfloat16),
                grad_block,
                preferred_element_type=jnp.float32,
            )
        )
    return (jnp.concatenate(query_grads, axis=0), key_grad, value_grad)


def norm_back(upstream, normed_hat, scale_rows, gain_row):
    scaled = upstream * gain_row[None, :]
    through = scale_rows * (
        scaled - normed_hat * jnp.mean(scaled * normed_hat, axis=1, keepdims=True)
    )
    return (through, jnp.sum(upstream * normed_hat, axis=0))


def contract_rows(left, right):
    return lax.dot_general(
        left, right, (((0,), (0,)), ((), ())), preferred_element_type=jnp.float32
    )


def contract_cols(left, right):
    return lax.dot_general(
        left, right, (((1,), (1,)), ((), ())), preferred_element_type=jnp.float32
    )


def line_gather(x, count):
    place = lax.axis_index("tensor")
    rows = x.shape[0]
    out = jnp.zeros((count * rows,) + x.shape[1:], x.dtype)
    from_left = x
    from_right = x
    received = []
    for step in range(1, count):
        from_left = lax.ppermute(
            from_left, "tensor", [(i, i + 1) for i in range(step - 1, count - 1)]
        )
        from_right = lax.ppermute(
            from_right, "tensor", [(i, i - 1) for i in range(1, count - step + 1)]
        )
        received.append((from_left, place - step, place - step >= 0))
        received.append((from_right, place + step, place + step <= count - 1))
    for piece, slot, valid in received:
        out = lax.dynamic_update_slice_in_dim(out, piece, jnp.where(valid, slot, place) * rows, 0)
    return lax.dynamic_update_slice_in_dim(out, x, place * rows, 0)


def line_scatter(partial, count):
    place = lax.axis_index("tensor")
    rows = partial.shape[0] // count

    def chunk(index):
        return lax.dynamic_slice_in_dim(partial, jnp.clip(index, 0, count - 1) * rows, rows, 0)

    to_right = None
    to_left = None
    for step in range(1, count):
        send = chunk(place + count - step)
        if to_right is not None:
            send = send + to_right
        to_right = lax.ppermute(
            send.astype(jnp.bfloat16), "tensor", [(i, i + 1) for i in range(step)]
        ).astype(jnp.float32)
        send = chunk(place - count + step)
        if to_left is not None:
            send = send + to_left
        to_left = lax.ppermute(
            send.astype(jnp.bfloat16), "tensor", [(i, i - 1) for i in range(count - step, count)]
        ).astype(jnp.float32)
    total = chunk(place)
    if to_right is not None:
        total = total + to_right + to_left
    return total


def per_device(
    tokens,
    cotangent,
    cont_lengths,
    query_weight,
    keyval_weight,
    output_weight,
    gateup_weight,
    down_weight,
    norm_gains,
    query_moment,
    keyval_moment,
    output_moment,
    gateup_moment,
    down_moment,
    gains_moment,
    query_square,
    keyval_square,
    output_square,
    gateup_square,
    down_square,
    gains_square,
):
    masters = (query_weight, keyval_weight, output_weight, gateup_weight, down_weight, norm_gains)
    firsts = (query_moment, keyval_moment, output_moment, gateup_moment, down_moment, gains_moment)
    seconds = (query_square, keyval_square, output_square, gateup_square, down_square, gains_square)
    rounded = tuple((master.astype(jnp.bfloat16) for master in masters))
    gathered = (
        lax.all_gather(rounded[0], "dp", axis=0, tiled=True),
        lax.all_gather(rounded[1], "dp", axis=0, tiled=True),
        lax.all_gather(rounded[2], "dp", axis=1, tiled=True),
        lax.all_gather(rounded[3], "dp", axis=0, tiled=True),
        lax.all_gather(rounded[4], "dp", axis=1, tiled=True),
        lax.all_gather(rounded[5], "dp", axis=1, tiled=True),
    )
    full_query, full_keyval, full_output, full_gateup, full_down, full_gains = gathered
    gain_values = full_gains.astype(jnp.float32)
    tensor_count = lax.axis_size("tensor")
    group_rows = tokens.shape[2] * tensor_count
    block_rows = group_rows // 2
    keyval_heads = full_keyval.shape[1]
    query_heads = full_query.shape[1] // HD
    head_repeat = query_heads // keyval_heads

    def micro_step(token_rows, cot_rows, lengths):
        visible, position = layout(lengths, group_rows)
        cos_table, sin_table = rope_tables(position)
        start_rows = token_rows.astype(jnp.float32)
        scale_one = lax.rsqrt(jnp.mean(start_rows * start_rows, axis=1, keepdims=True) + norm_eps)
        hat_one = start_rows * scale_one
        normed_one = (hat_one * gain_values[0][None, :]).astype(jnp.bfloat16)
        rows_one = yield ("gather", normed_one)
        query_raw = jnp.dot(rows_one, full_query, preferred_element_type=jnp.float32).reshape(
            group_rows, query_heads, HD
        )
        keyval_raw = jnp.einsum(
            "rd,dhk->rhk", rows_one, full_keyval, preferred_element_type=jnp.float32
        )
        queries = (
            rotate(query_raw, cos_table, sin_table)
            .astype(jnp.bfloat16)
            .reshape(group_rows, keyval_heads, head_repeat, HD)
        )
        key_rows = rotate(keyval_raw[:, :, :HD], cos_table, sin_table).astype(jnp.bfloat16)
        values = keyval_raw[:, :, HD:].astype(jnp.bfloat16)
        mixed_full, log_totals = attend(queries, key_rows, values, visible, block_rows)
        mixed = mixed_full.astype(jnp.bfloat16).reshape(group_rows, query_heads * HD)
        attn_partial, _, _ = lax.optimization_barrier(
            (jnp.dot(mixed, full_output, preferred_element_type=jnp.float32), full_gateup, full_down)
        )
        attn_branch = yield ("offload_scatter", attn_partial)
        middle = start_rows + branch_scale * attn_branch
        scale_two = lax.rsqrt(jnp.mean(middle * middle, axis=1, keepdims=True) + norm_eps)
        hat_two = middle * scale_two
        normed_two = (hat_two * gain_values[1][None, :]).astype(jnp.bfloat16)
        rows_two = yield ("gather", normed_two)
        gate_up = jnp.einsum(
            "rd,dcf->rcf", rows_two, full_gateup, preferred_element_type=jnp.float32
        )
        gate_part = gate_up[:, 0]
        up_part = gate_up[:, 1]
        sigmoid_gate = jax.nn.sigmoid(gate_part)
        silu_gate = gate_part * sigmoid_gate
        hidden_state = (silu_gate * up_part).astype(jnp.bfloat16)
        upstream = cot_rows.astype(jnp.float32)
        ffn_grad = (branch_scale * upstream).astype(jnp.bfloat16)
        ffn_grad_all = yield ("gather", ffn_grad)
        ffn_branch = yield (
            "offload_scatter", jnp.dot(hidden_state, full_down, preferred_element_type=jnp.float32)
        )
        layer_rows = (middle + branch_scale * ffn_branch).astype(jnp.bfloat16)
        grad_down = contract_rows(hidden_state, ffn_grad_all)
        hidden_grad = contract_cols(ffn_grad_all, full_down)
        gate_grad = hidden_grad * up_part * sigmoid_gate * (1.0 + gate_part * (1.0 - sigmoid_gate))
        up_grad = hidden_grad * silu_gate
        gateup_grad = jnp.stack([gate_grad, up_grad], axis=1).astype(jnp.bfloat16)
        grad_gateup = jnp.einsum(
            "rd,rcf->dcf", rows_two, gateup_grad, preferred_element_type=jnp.float32
        )
        normed_two_grad = yield (
            "offload_scatter",
            jnp.einsum(
                "rcf,dcf->rd", gateup_grad, full_gateup, preferred_element_type=jnp.float32
            ),
        )
        middle_back, gain_two = norm_back(normed_two_grad, hat_two, scale_two, gain_values[1])
        middle_grad = upstream + middle_back
        attn_grad = (branch_scale * middle_grad).astype(jnp.bfloat16)
        attn_grad_all = yield ("gather", attn_grad)
        grad_output = contract_rows(mixed, attn_grad_all)
        mixed_grad = (
            contract_cols(attn_grad_all, full_output)
            .astype(jnp.bfloat16)
            .reshape(group_rows, keyval_heads, head_repeat, HD)
        )
        query_grad, key_grad, value_grad = attend_back(
            queries, key_rows, values, visible, log_totals, mixed_grad, block_rows
        )
        query_raw_grad = (
            rotate_back(query_grad.reshape(group_rows, query_heads, HD), cos_table, sin_table)
            .astype(jnp.bfloat16)
            .reshape(group_rows, query_heads * HD)
        )
        keyval_raw_grad = jnp.concatenate(
            [rotate_back(key_grad, cos_table, sin_table), value_grad], axis=2
        ).astype(jnp.bfloat16)
        grad_query = contract_rows(rows_one, query_raw_grad)
        grad_keyval = jnp.einsum(
            "rd,rhk->dhk", rows_one, keyval_raw_grad, preferred_element_type=jnp.float32
        )
        normed_one_grad = yield (
            "scatter",
            contract_cols(query_raw_grad, full_query)
            + jnp.einsum(
                "rhk,dhk->rd", keyval_raw_grad, full_keyval, preferred_element_type=jnp.float32
            ),
        )
        start_back, gain_one = norm_back(normed_one_grad, hat_one, scale_one, gain_values[0])
        input_rows = middle_grad + start_back
        gain_grad = jnp.stack([gain_one, gain_two])
        return (
            layer_rows,
            input_rows,
            (grad_query, grad_keyval, grad_output, grad_gateup, grad_down, gain_grad),
        )

    streams = [
        micro_step(tokens[index, 0], cotangent[index, 0], cont_lengths[index, 0])
        for index in range(tokens.shape[0])
    ]
    requests = [next(stream) for stream in streams]
    finished = [None] * len(streams)
    previous = None
    while any(result is None for result in finished):
        for index, stream in enumerate(streams):
            if finished[index] is not None:
                continue
            kind, value = requests[index]
            if previous is not None:
                previous, value = lax.optimization_barrier((previous, value))
            if kind == "gather":
                previous = line_gather(value, tensor_count)
            elif kind == "scatter":
                previous = line_scatter(value, tensor_count)
            else:
                previous = lax.psum_scatter(
                    value.astype(jnp.bfloat16), "tensor", scatter_dimension=0, tiled=True
                ).astype(jnp.float32)
            try:
                requests[index] = stream.send(previous)
            except StopIteration as stop:
                finished[index] = stop.value
    out_list = [result[0] for result in finished]
    grad_list = [result[1] for result in finished]
    totals = finished[0][2]
    for result in finished[1:]:
        totals = tuple((old_sum + new_term for old_sum, new_term in zip(totals, result[2])))
    layer_output = jnp.stack(out_list)[:, None]
    input_grad = jnp.stack(grad_list)[:, None]
    width = totals[0].shape[0]
    gain_total = lax.psum(totals[5], "tensor")
    summed = (
        lax.psum_scatter(
            totals[0].astype(jnp.bfloat16), "dp", scatter_dimension=0, tiled=True
        ).astype(jnp.float32),
        lax.psum_scatter(
            totals[1].reshape(width, -1).astype(jnp.bfloat16), "dp", scatter_dimension=0, tiled=True
        )
        .astype(jnp.float32)
        .reshape(-1, *totals[1].shape[1:]),
        lax.psum_scatter(
            totals[2].astype(jnp.bfloat16), "dp", scatter_dimension=1, tiled=True
        ).astype(jnp.float32),
        lax.psum_scatter(
            totals[3].reshape(width, -1).astype(jnp.bfloat16), "dp", scatter_dimension=0, tiled=True
        )
        .astype(jnp.float32)
        .reshape(-1, *totals[3].shape[1:]),
        lax.psum_scatter(
            totals[4].astype(jnp.bfloat16), "dp", scatter_dimension=1, tiled=True
        ).astype(jnp.float32),
        lax.psum_scatter(
            gain_total.astype(jnp.bfloat16), "dp", scatter_dimension=1, tiled=True
        ).astype(jnp.float32),
    )
    correction = 1.0 - moment_decay**STEP
    new_firsts = []
    new_seconds = []
    directions = []
    for grad, first, second in zip(summed, firsts, seconds):
        first_new = moment_decay * first + (1.0 - moment_decay) * grad
        second_new = moment_decay * second + (1.0 - moment_decay) * grad * grad
        direction = first_new / correction / (jnp.sqrt(second_new / correction) + ratio_eps)
        new_firsts.append(first_new)
        new_seconds.append(second_new)
        directions.append(direction)
    weight_part = jnp.concatenate(
        [
            jnp.stack([jnp.sum(masters[slot] * masters[slot]) for slot in range(5)]),
            jnp.sum(norm_gains * norm_gains, axis=1) / tensor_count,
        ]
    )
    update_part = jnp.concatenate(
        [
            jnp.stack([jnp.sum(directions[slot] * directions[slot]) for slot in range(5)]),
            jnp.sum(directions[5] * directions[5], axis=1) / tensor_count,
        ]
    )
    square_totals = lax.psum(jnp.stack([weight_part, update_part]), ("dp", "tensor"))
    trust_norms = jnp.sqrt(square_totals)
    ratio = trust_norms[0] / (trust_norms[1] + ratio_eps)
    new_weights = [masters[slot] - learn_rate * ratio[slot] * directions[slot] for slot in range(5)]
    new_gains = norm_gains - learn_rate * ratio[5:7][:, None] * directions[5]
    return (
        layer_output,
        input_grad,
        new_weights[0],
        new_weights[1],
        new_weights[2],
        new_weights[3],
        new_weights[4],
        new_gains,
        new_firsts[0],
        new_firsts[1],
        new_firsts[2],
        new_firsts[3],
        new_firsts[4],
        new_firsts[5],
        new_seconds[0],
        new_seconds[1],
        new_seconds[2],
        new_seconds[3],
        new_seconds[4],
        new_seconds[5],
        trust_norms,
    )


def solution(mesh):
    return jax.shard_map(
        per_device,
        mesh=mesh,
        in_specs=(
            P(None, "dp", "tensor", None),
            P(None, "dp", "tensor", None),
            P(None, "dp", None),
            P("dp", "tensor"),
            P("dp", "tensor", None),
            P("tensor", "dp"),
            P("dp", None, "tensor"),
            P("tensor", "dp"),
            P(None, "dp"),
            P("dp", "tensor"),
            P("dp", "tensor", None),
            P("tensor", "dp"),
            P("dp", None, "tensor"),
            P("tensor", "dp"),
            P(None, "dp"),
            P("dp", "tensor"),
            P("dp", "tensor", None),
            P("tensor", "dp"),
            P("dp", None, "tensor"),
            P("tensor", "dp"),
            P(None, "dp"),
        ),
        out_specs=(
            P(None, "dp", "tensor", None),
            P(None, "dp", "tensor", None),
            P("dp", "tensor"),
            P("dp", "tensor", None),
            P("tensor", "dp"),
            P("dp", None, "tensor"),
            P("tensor", "dp"),
            P(None, "dp"),
            P("dp", "tensor"),
            P("dp", "tensor", None),
            P("tensor", "dp"),
            P("dp", None, "tensor"),
            P("tensor", "dp"),
            P(None, "dp"),
            P("dp", "tensor"),
            P("dp", "tensor", None),
            P("tensor", "dp"),
            P("dp", None, "tensor"),
            P("tensor", "dp"),
            P(None, "dp"),
            P(),
        ),
        check_vma=False,
    )
```

```python
import jax
import jax.numpy as jnp
from jax import lax
from jax.sharding import PartitionSpec as P

HD = 64
PROMPT = 1024
CONTS = 3
STEP = 3


norm_eps = 1e-05
branch_scale = 0.22
score_scale = 0.015625
rope_base = 10000000.0
moment_decay = 0.5
learn_rate = 0.25
ratio_eps = 1e-06
masked_fill = -1e30


def layout(lengths, group_rows):
    row_index = jnp.arange(group_rows, dtype=jnp.int32)
    ends = jnp.cumsum(lengths)
    starts = ends - lengths
    within = row_index - PROMPT
    inside = (within[:, None] >= starts[None, :]) & (within[:, None] < ends[None, :])
    labels = jnp.arange(1, CONTS + 1, dtype=jnp.int32)
    segment = jnp.sum(jnp.where(inside, labels[None, :], 0), axis=1)
    offsets = jnp.sum(jnp.where(inside, starts[None, :], 0), axis=1)
    position = row_index - offsets
    causal = row_index[None, :] <= row_index[:, None]
    shared = (segment[None, :] == segment[:, None]) | (segment[None, :] == 0)
    return (causal & shared, position)


def rope_tables(position):
    half_size = HD // 2
    inverse = rope_base ** (-2.0 * jnp.arange(half_size, dtype=jnp.float32) / HD)
    angle = position.astype(jnp.float32)[:, None] * inverse[None, :]
    return (jnp.cos(angle)[:, None, :], jnp.sin(angle)[:, None, :])


def rotate(field, cos_table, sin_table):
    half_size = field.shape[-1] // 2
    first_half = field[..., :half_size]
    second_half = field[..., half_size:]
    return jnp.concatenate(
        [
            first_half * cos_table - second_half * sin_table,
            second_half * cos_table + first_half * sin_table,
        ],
        axis=-1,
    )


def rotate_back(grad_field, cos_table, sin_table):
    half_size = grad_field.shape[-1] // 2
    first_half = grad_field[..., :half_size]
    second_half = grad_field[..., half_size:]
    return jnp.concatenate(
        [
            first_half * cos_table + second_half * sin_table,
            second_half * cos_table - first_half * sin_table,
        ],
        axis=-1,
    )


def attend(queries, key_rows, values, visible, block_rows):
    outputs = []
    log_totals = []
    for block in range(2):
        begin = block * block_rows
        stop = begin + block_rows
        scores = (
            jnp.einsum(
                "ikrd,jkd->krij",
                queries[begin:stop],
                key_rows[:stop],
                preferred_element_type=jnp.float32,
            )
            * score_scale
        )
        scores = jnp.where(visible[begin:stop, :stop][None, None], scores, masked_fill)
        row_peak = jnp.max(scores, axis=-1, keepdims=True)
        shifted_exp = jnp.exp(scores - row_peak)
        row_total = jnp.sum(shifted_exp, axis=-1, keepdims=True)
        attn_prob = (shifted_exp / row_total).astype(jnp.bfloat16)
        outputs.append(
            jnp.einsum(
                "krij,jkd->ikrd", attn_prob, values[:stop], preferred_element_type=jnp.float32
            )
        )
        log_totals.append(row_peak + jnp.log(row_total))
    return (jnp.concatenate(outputs, axis=0), jnp.concatenate(log_totals, axis=2))


def attend_back(queries, key_rows, values, visible, log_totals, mixed_grad, block_rows):
    query_grads = []
    key_grad = jnp.zeros(key_rows.shape, jnp.float32)
    value_grad = jnp.zeros(values.shape, jnp.float32)
    for block in range(2):
        begin = block * block_rows
        stop = begin + block_rows
        query_block = queries[begin:stop]
        grad_block = mixed_grad[begin:stop]
        scores = (
            jnp.einsum(
                "ikrd,jkd->krij", query_block, key_rows[:stop], preferred_element_type=jnp.float32
            )
            * score_scale
        )
        attn_prob = jnp.where(
            visible[begin:stop, :stop][None, None],
            jnp.exp(scores - log_totals[:, :, begin:stop]),
            0.0,
        )
        prob_grad = jnp.einsum(
            "ikrd,jkd->krij", grad_block, values[:stop], preferred_element_type=jnp.float32
        )
        row_dot = jnp.sum(attn_prob * prob_grad, axis=-1, keepdims=True)
        score_grad = (attn_prob * (prob_grad - row_dot)).astype(jnp.bfloat16)
        query_grads.append(
            jnp.einsum(
                "krij,jkd->ikrd", score_grad, key_rows[:stop], preferred_element_type=jnp.float32
            )
            * score_scale
        )
        key_grad = key_grad.at[:stop].add(
            jnp.einsum(
                "krij,ikrd->jkd", score_grad, query_block, preferred_element_type=jnp.float32
            )
            * score_scale
        )
        value_grad = value_grad.at[:stop].add(
            jnp.einsum(
                "krij,ikrd->jkd",
                attn_prob.astype(jnp.bfloat16),
                grad_block,
                preferred_element_type=jnp.float32,
            )
        )
    return (jnp.concatenate(query_grads, axis=0), key_grad, value_grad)


def norm_back(upstream, normed_hat, scale_rows, gain_row):
    scaled = upstream * gain_row[None, :]
    through = scale_rows * (
        scaled - normed_hat * jnp.mean(scaled * normed_hat, axis=1, keepdims=True)
    )
    return (through, jnp.sum(upstream * normed_hat, axis=0))


def contract_rows(left, right):
    return lax.dot_general(
        left, right, (((0,), (0,)), ((), ())), preferred_element_type=jnp.float32
    )


def contract_cols(left, right):
    return lax.dot_general(
        left, right, (((1,), (1,)), ((), ())), preferred_element_type=jnp.float32
    )


def by_row_blocks(operation, rows_in, count):
    size = rows_in.shape[0] // count
    return jnp.concatenate(
        [operation(rows_in[index * size : (index + 1) * size]) for index in range(count)], axis=0
    )


def line_gather(x, count):
    place = lax.axis_index("tensor")
    rows = x.shape[0]
    out = jnp.zeros((count * rows,) + x.shape[1:], x.dtype)
    from_left = x
    from_right = x
    received = []
    for step in range(1, count):
        from_left = lax.ppermute(
            from_left, "tensor", [(i, i + 1) for i in range(step - 1, count - 1)]
        )
        from_right = lax.ppermute(
            from_right, "tensor", [(i, i - 1) for i in range(1, count - step + 1)]
        )
        received.append((from_left, place - step, place - step >= 0))
        received.append((from_right, place + step, place + step <= count - 1))
    for piece, slot, valid in received:
        out = lax.dynamic_update_slice_in_dim(out, piece, jnp.where(valid, slot, place) * rows, 0)
    return lax.dynamic_update_slice_in_dim(out, x, place * rows, 0)


def line_scatter(partial, count):
    place = lax.axis_index("tensor")
    rows = partial.shape[0] // count

    def chunk(index):
        return lax.dynamic_slice_in_dim(partial, jnp.clip(index, 0, count - 1) * rows, rows, 0)

    to_right = None
    to_left = None
    for step in range(1, count):
        send = chunk(place + count - step)
        if to_right is not None:
            send = send + to_right
        to_right = lax.ppermute(
            send.astype(jnp.bfloat16), "tensor", [(i, i + 1) for i in range(step)]
        ).astype(jnp.float32)
        send = chunk(place - count + step)
        if to_left is not None:
            send = send + to_left
        to_left = lax.ppermute(
            send.astype(jnp.bfloat16), "tensor", [(i, i - 1) for i in range(count - step, count)]
        ).astype(jnp.float32)
    total = chunk(place)
    if to_right is not None:
        total = total + to_right + to_left
    return total


def per_device(
    tokens,
    cotangent,
    cont_lengths,
    query_weight,
    keyval_weight,
    output_weight,
    gateup_weight,
    down_weight,
    norm_gains,
    query_moment,
    keyval_moment,
    output_moment,
    gateup_moment,
    down_moment,
    gains_moment,
    query_square,
    keyval_square,
    output_square,
    gateup_square,
    down_square,
    gains_square,
):
    masters = (query_weight, keyval_weight, output_weight, gateup_weight, down_weight, norm_gains)
    firsts = (query_moment, keyval_moment, output_moment, gateup_moment, down_moment, gains_moment)
    seconds = (query_square, keyval_square, output_square, gateup_square, down_square, gains_square)
    rounded = tuple((master.astype(jnp.bfloat16) for master in masters))
    gathered = (
        lax.all_gather(rounded[0], "dp", axis=0, tiled=True),
        lax.all_gather(rounded[1], "dp", axis=0, tiled=True),
        lax.all_gather(rounded[2], "dp", axis=1, tiled=True),
        lax.all_gather(rounded[3], "dp", axis=0, tiled=True),
        lax.all_gather(rounded[4], "dp", axis=1, tiled=True),
        lax.all_gather(rounded[5], "dp", axis=1, tiled=True),
    )
    full_query, full_keyval, full_output, full_gateup, full_down, full_gains = gathered
    gain_values = full_gains.astype(jnp.float32)
    tensor_count = lax.axis_size("tensor")
    group_rows = tokens.shape[2] * tensor_count
    block_rows = group_rows // 2
    keyval_heads = full_keyval.shape[1]
    query_heads = full_query.shape[1] // HD
    head_repeat = query_heads // keyval_heads

    def micro_step(token_rows, cot_rows, lengths):
        visible, position = layout(lengths, group_rows)
        cos_table, sin_table = rope_tables(position)
        start_rows = token_rows.astype(jnp.float32)
        scale_one = lax.rsqrt(jnp.mean(start_rows * start_rows, axis=1, keepdims=True) + norm_eps)
        hat_one = start_rows * scale_one
        normed_one = (hat_one * gain_values[0][None, :]).astype(jnp.bfloat16)
        rows_one = yield ("gather", normed_one)
        query_raw = jnp.dot(rows_one, full_query, preferred_element_type=jnp.float32).reshape(
            group_rows, query_heads, HD
        )
        keyval_raw = jnp.einsum(
            "rd,dhk->rhk", rows_one, full_keyval, preferred_element_type=jnp.float32
        )
        queries = (
            rotate(query_raw, cos_table, sin_table)
            .astype(jnp.bfloat16)
            .reshape(group_rows, keyval_heads, head_repeat, HD)
        )
        key_rows = rotate(keyval_raw[:, :, :HD], cos_table, sin_table).astype(jnp.bfloat16)
        values = keyval_raw[:, :, HD:].astype(jnp.bfloat16)
        mixed_full, log_totals = attend(queries, key_rows, values, visible, block_rows)
        mixed = mixed_full.astype(jnp.bfloat16).reshape(group_rows, query_heads * HD)
        attn_branch = yield (
            "scatter", jnp.dot(mixed, full_output, preferred_element_type=jnp.float32)
        )
        middle = start_rows + branch_scale * attn_branch
        scale_two = lax.rsqrt(jnp.mean(middle * middle, axis=1, keepdims=True) + norm_eps)
        hat_two = middle * scale_two
        normed_two = (hat_two * gain_values[1][None, :]).astype(jnp.bfloat16)
        rows_two = yield ("gather", normed_two)
        gate_up = by_row_blocks(
            lambda part: jnp.einsum(
                "rd,dcf->rcf", part, full_gateup, preferred_element_type=jnp.float32
            ),
            rows_two,
            tensor_count,
        )
        gate_part = gate_up[:, 0]
        up_part = gate_up[:, 1]
        sigmoid_gate = jax.nn.sigmoid(gate_part)
        silu_gate = gate_part * sigmoid_gate
        hidden_state = (silu_gate * up_part).astype(jnp.bfloat16)
        upstream = cot_rows.astype(jnp.float32)
        ffn_grad = (branch_scale * upstream).astype(jnp.bfloat16)
        ffn_grad_all = yield ("gather", ffn_grad)
        ffn_branch = yield (
            "scatter",
            by_row_blocks(
                lambda part: jnp.dot(part, full_down, preferred_element_type=jnp.float32),
                hidden_state,
                tensor_count,
            ),
        )
        layer_rows = (middle + branch_scale * ffn_branch).astype(jnp.bfloat16)
        grad_down = contract_rows(hidden_state, ffn_grad_all)
        hidden_grad = by_row_blocks(
            lambda part: contract_cols(part, full_down), ffn_grad_all, tensor_count
        )
        gate_grad = hidden_grad * up_part * sigmoid_gate * (1.0 + gate_part * (1.0 - sigmoid_gate))
        up_grad = hidden_grad * silu_gate
        gateup_grad = jnp.stack([gate_grad, up_grad], axis=1).astype(jnp.bfloat16)
        grad_gateup = jnp.einsum(
            "rd,rcf->dcf", rows_two, gateup_grad, preferred_element_type=jnp.float32
        )
        normed_two_grad = yield (
            "scatter",
            by_row_blocks(
                lambda part: jnp.einsum(
                    "rcf,dcf->rd", part, full_gateup, preferred_element_type=jnp.float32
                ),
                gateup_grad,
                tensor_count,
            ),
        )
        middle_back, gain_two = norm_back(normed_two_grad, hat_two, scale_two, gain_values[1])
        middle_grad = upstream + middle_back
        attn_grad = (branch_scale * middle_grad).astype(jnp.bfloat16)
        attn_grad_all = yield ("gather", attn_grad)
        grad_output = contract_rows(mixed, attn_grad_all)
        mixed_grad = (
            contract_cols(attn_grad_all, full_output)
            .astype(jnp.bfloat16)
            .reshape(group_rows, keyval_heads, head_repeat, HD)
        )
        query_grad, key_grad, value_grad = attend_back(
            queries, key_rows, values, visible, log_totals, mixed_grad, block_rows
        )
        query_raw_grad = (
            rotate_back(query_grad.reshape(group_rows, query_heads, HD), cos_table, sin_table)
            .astype(jnp.bfloat16)
            .reshape(group_rows, query_heads * HD)
        )
        keyval_raw_grad = jnp.concatenate(
            [rotate_back(key_grad, cos_table, sin_table), value_grad], axis=2
        ).astype(jnp.bfloat16)
        grad_query = contract_rows(rows_one, query_raw_grad)
        grad_keyval = jnp.einsum(
            "rd,rhk->dhk", rows_one, keyval_raw_grad, preferred_element_type=jnp.float32
        )
        normed_one_grad = yield (
            "scatter",
            contract_cols(query_raw_grad, full_query)
            + jnp.einsum(
                "rhk,dhk->rd", keyval_raw_grad, full_keyval, preferred_element_type=jnp.float32
            ),
        )
        start_back, gain_one = norm_back(normed_one_grad, hat_one, scale_one, gain_values[0])
        input_rows = middle_grad + start_back
        gain_grad = jnp.stack([gain_one, gain_two])
        return (
            layer_rows,
            input_rows,
            (grad_query, grad_keyval, grad_output, grad_gateup, grad_down, gain_grad),
        )

    streams = [
        micro_step(tokens[index, 0], cotangent[index, 0], cont_lengths[index, 0])
        for index in range(tokens.shape[0])
    ]
    requests = [next(stream) for stream in streams]
    finished = [None] * len(streams)
    previous = None
    while any(result is None for result in finished):
        for index, stream in enumerate(streams):
            if finished[index] is not None:
                continue
            kind, value = requests[index]
            if previous is not None:
                previous, value = lax.optimization_barrier((previous, value))
            if kind == "gather":
                previous = line_gather(value, tensor_count)
            else:
                previous = line_scatter(value, tensor_count)
            try:
                requests[index] = stream.send(previous)
            except StopIteration as stop:
                finished[index] = stop.value
    out_list = [result[0] for result in finished]
    grad_list = [result[1] for result in finished]
    totals = finished[0][2]
    for result in finished[1:]:
        totals = tuple((old_sum + new_term for old_sum, new_term in zip(totals, result[2])))
    layer_output = jnp.stack(out_list)[:, None]
    input_grad = jnp.stack(grad_list)[:, None]
    width = totals[0].shape[0]
    gain_total = lax.psum(totals[5], "tensor")
    summed = (
        lax.psum_scatter(
            totals[0].astype(jnp.bfloat16), "dp", scatter_dimension=0, tiled=True
        ).astype(jnp.float32),
        lax.psum_scatter(
            totals[1].reshape(width, -1).astype(jnp.bfloat16), "dp", scatter_dimension=0, tiled=True
        )
        .astype(jnp.float32)
        .reshape(-1, *totals[1].shape[1:]),
        lax.psum_scatter(
            totals[2].astype(jnp.bfloat16), "dp", scatter_dimension=1, tiled=True
        ).astype(jnp.float32),
        lax.psum_scatter(
            totals[3].reshape(width, -1).astype(jnp.bfloat16), "dp", scatter_dimension=0, tiled=True
        )
        .astype(jnp.float32)
        .reshape(-1, *totals[3].shape[1:]),
        lax.psum_scatter(
            totals[4].astype(jnp.bfloat16), "dp", scatter_dimension=1, tiled=True
        ).astype(jnp.float32),
        lax.psum_scatter(
            gain_total.astype(jnp.bfloat16), "dp", scatter_dimension=1, tiled=True
        ).astype(jnp.float32),
    )
    correction = 1.0 - moment_decay**STEP
    new_firsts = []
    new_seconds = []
    directions = []
    for grad, first, second in zip(summed, firsts, seconds):
        first_new = moment_decay * first + (1.0 - moment_decay) * grad
        second_new = moment_decay * second + (1.0 - moment_decay) * grad * grad
        direction = first_new / correction / (jnp.sqrt(second_new / correction) + ratio_eps)
        new_firsts.append(first_new)
        new_seconds.append(second_new)
        directions.append(direction)
    weight_part = jnp.concatenate(
        [
            jnp.stack([jnp.sum(masters[slot] * masters[slot]) for slot in range(5)]),
            jnp.sum(norm_gains * norm_gains, axis=1) / tensor_count,
        ]
    )
    update_part = jnp.concatenate(
        [
            jnp.stack([jnp.sum(directions[slot] * directions[slot]) for slot in range(5)]),
            jnp.sum(directions[5] * directions[5], axis=1) / tensor_count,
        ]
    )
    square_totals = lax.psum(jnp.stack([weight_part, update_part]), ("dp", "tensor"))
    trust_norms = jnp.sqrt(square_totals)
    ratio = trust_norms[0] / (trust_norms[1] + ratio_eps)
    new_weights = [masters[slot] - learn_rate * ratio[slot] * directions[slot] for slot in range(5)]
    new_gains = norm_gains - learn_rate * ratio[5:7][:, None] * directions[5]
    return (
        layer_output,
        input_grad,
        new_weights[0],
        new_weights[1],
        new_weights[2],
        new_weights[3],
        new_weights[4],
        new_gains,
        new_firsts[0],
        new_firsts[1],
        new_firsts[2],
        new_firsts[3],
        new_firsts[4],
        new_firsts[5],
        new_seconds[0],
        new_seconds[1],
        new_seconds[2],
        new_seconds[3],
        new_seconds[4],
        new_seconds[5],
        trust_norms,
    )


def solution(mesh):
    return jax.shard_map(
        per_device,
        mesh=mesh,
        in_specs=(
            P(None, "dp", "tensor", None),
            P(None, "dp", "tensor", None),
            P(None, "dp", None),
            P("dp", "tensor"),
            P("dp", "tensor", None),
            P("tensor", "dp"),
            P("dp", None, "tensor"),
            P("tensor", "dp"),
            P(None, "dp"),
            P("dp", "tensor"),
            P("dp", "tensor", None),
            P("tensor", "dp"),
            P("dp", None, "tensor"),
            P("tensor", "dp"),
            P(None, "dp"),
            P("dp", "tensor"),
            P("dp", "tensor", None),
            P("tensor", "dp"),
            P("dp", None, "tensor"),
            P("tensor", "dp"),
            P(None, "dp"),
        ),
        out_specs=(
            P(None, "dp", "tensor", None),
            P(None, "dp", "tensor", None),
            P("dp", "tensor"),
            P("dp", "tensor", None),
            P("tensor", "dp"),
            P("dp", None, "tensor"),
            P("tensor", "dp"),
            P(None, "dp"),
            P("dp", "tensor"),
            P("dp", "tensor", None),
            P("tensor", "dp"),
            P("dp", None, "tensor"),
            P("tensor", "dp"),
            P(None, "dp"),
            P("dp", "tensor"),
            P("dp", "tensor", None),
            P("tensor", "dp"),
            P("dp", None, "tensor"),
            P("tensor", "dp"),
            P(None, "dp"),
            P(),
        ),
        check_vma=False,
    )
```
